32 devices in a mesh: gy: 16 (over z, y, core), gz: 2 (over x).
Axes of the slice: x: 2, y: 2, z: 4, core: 2. Of those that a mesh axis runs over, the one named last changes fastest.
Arguments:
- mag_start: float32 [2, 256, 256, 256], P(None, 'gy', 'gz'), may hold values from -3 to 3
- mag_middle: float32 [2, 256, 256, 256], P(None, 'gy', 'gz'), may hold values from -3 to 3
- adjoint_end: float32 [2, 256, 256, 256], P(None, 'gy', 'gz'), may hold values from -3 to 3
- phase: float32 [256, 256, 256], P('gy', 'gz'), may hold values from -4 to 4
- labels: int32 [256, 256, 256], P('gy', 'gz'), may hold values from 0 to 3
Outputs:
- adjoint_start: float32 [2, 256, 256, 256], P(None, 'gy', 'gz')
- chi_grad: float32 [256, 256, 256], P('gy', 'gz')
The draws below stay inside these ranges and needn't reach their ends.
All inputs are finite; a program needn't handle non-finite values.
Results may differ from the reference program's by a relative error of at most 0.0003.
Values sent between devices are 32-bit elements; how exact they have to be, the bound alone decides.
No kernel may reach another device: no remote copies, remote signals or barrier semaphores. Data moves between devices by JAX's collectives and lax.ppermute only.
A program may use at most 192 MiB of HBM per device.

```python
import jax
import jax.numpy as jnp

NG = 256


def draw_mag_middle(key, part):
    noise = 0.5 * jnp.clip(jax.random.normal(jax.random.fold_in(key, 11), (2, NG, NG, NG), jnp.float32), -3.0, 3.0)
    return noise


def draw_adjoint_end(key, part):
    noise = 0.6 * jnp.clip(jax.random.normal(jax.random.fold_in(key, 23), (2, NG, NG, NG), jnp.float32), -3.0, 3.0)
    return noise


def with_ends(drawn, stream_key, least, largest):
    longest = drawn.shape.index(max(drawn.shape))
    spots = []
    for shift in (0, 1):
        where = [jax.random.randint(jax.random.fold_in(stream_key, axis), (), 0, length) for axis, length in enumerate(drawn.shape)]
        where[longest] = (where[longest] + shift) % drawn.shape[longest]
        spots.append(tuple(where))
    return drawn.at[spots[0]].set(least).at[spots[1]].set(largest)


def level_of(rng, shape, cuts, smallest, largest):
    factor_of = 1.0
    for axis_at, shards_of in cuts:
        draws = jax.random.uniform(jax.random.fold_in(jax.random.fold_in(rng, 6), axis_at), (shards_of,), jnp.float32, smallest / len(cuts), largest / len(cuts))
        factor_of = factor_of * jnp.repeat(jnp.exp(draws), shape[axis_at] // shards_of).reshape((-1,) + (1,) * (len(shape) - 1 - axis_at))
    return factor_of


def centred(rng, extent, spread, reach, split=(), held_as=jnp.bfloat16):
    values = jax.random.normal(rng, extent, jnp.float32) * spread
    if len(split) > 0:
        values = level_of(rng, extent, split, -0.22, 0.18) * values
    return jnp.clip(values, min=-reach, max=reach).astype(held_as)


def setup_inputs(seed: int = 0) -> dict:
    arg_keys = jax.random.split(jax.random.key(seed), 6)
    return {
        "mag_start": centred(arg_keys[0], (2, NG, NG, NG), 0.5, 3.0, ((1, 16), (2, 2)), jnp.float32),
        "mag_middle": draw_mag_middle(jax.random.fold_in(arg_keys[5], 71), 0),
        "adjoint_end": draw_adjoint_end(jax.random.fold_in(arg_keys[5], 71), 0),
        "phase": centred(arg_keys[3], (NG, NG, NG), 1.0, 4.0, ((0, 16), (1, 2)), jnp.float32),
        "labels": with_ends(jax.random.randint(arg_keys[4], (NG, NG, NG), 0, 4), jax.random.fold_in(arg_keys[4], 1), 0, 3).astype(jnp.int32),
    }


def laplace_periodic(field):
    total = jnp.roll(field, 1, axis=0) + jnp.roll(field, -1, axis=0)
    total = total + jnp.roll(field, 1, axis=1) + jnp.roll(field, -1, axis=1)
    total = total + jnp.roll(field, 1, axis=2) + jnp.roll(field, -1, axis=2)
    return total - 6.0 * field


def relax_rate(labels):
    rate = jnp.where(labels == 1, 0.3, 0.02)
    rate = jnp.where(labels == 2, 0.6, rate)
    rate = jnp.where(labels == 3, 1.2, rate)
    return rate.astype(jnp.float32)


def signed_freq(index):
    return jnp.where(index < NG // 2, index, index - NG).astype(jnp.int32)


def dipole_block(freq_y, freq_z, freq_x):
    square_z = freq_z * freq_z
    total = freq_y * freq_y + square_z + freq_x * freq_x
    ratio = square_z.astype(jnp.float32) / jnp.maximum(total, 1).astype(jnp.float32)
    return jnp.where(total == 0, jnp.float32(0.0), jnp.float32(1.0 / 3.0) - ratio)


def reference(mag_start, mag_middle, adjoint_end, phase, labels):
    decay = jnp.exp(-relax_rate(labels))
    factor_real = decay * jnp.cos(phase)
    factor_imag = decay * jnp.sin(phase)
    lam_real, lam_imag = adjoint_end[0], adjoint_end[1]
    phase_grad = jnp.zeros_like(phase)
    for checkpoint in (mag_middle, mag_start):
        w_real = factor_real * lam_real - factor_imag * lam_imag
        w_imag = factor_real * lam_imag + factor_imag * lam_real
        u_real = checkpoint[0] + 0.15 * laplace_periodic(checkpoint[0])
        u_imag = checkpoint[1] + 0.15 * laplace_periodic(checkpoint[1])
        phase_grad = phase_grad + (w_real * u_imag - w_imag * u_real)
        lam_real = w_real + 0.15 * laplace_periodic(w_real)
        lam_imag = w_imag + 0.15 * laplace_periodic(w_imag)
    index = jnp.arange(NG, dtype=jnp.int32)
    freq = signed_freq(index)
    kernel = dipole_block(freq[:, None, None], freq[None, :, None], freq[None, None, :])
    spectrum = jnp.fft.fftn(phase_grad)
    chi_grad = jnp.real(jnp.fft.ifftn(spectrum * kernel)).astype(jnp.float32)
    return jnp.stack([lam_real, lam_imag]), chi_grad
```

```python
import math

import jax
import jax.numpy as jnp
from jax import lax
from jax.sharding import PartitionSpec as P


def with_halo(value, sides, width):
    for axis, dim in sides:
        count, length = (lax.axis_size(axis), value.shape[dim])
        up = [(i, (i + 1) % count) for i in range(count)]
        down = [(j, i) for i, j in up]
        last = lax.slice_in_dim(value, length - width, length, axis=dim)
        first = lax.slice_in_dim(value, 0, width, axis=dim)
        before = lax.ppermute(last, axis, up)
        after = lax.ppermute(first, axis, down)
        value = jnp.concatenate([before, value, after], axis=dim)
    return value


def laplace_inner(padded):
    centre = padded[:, 1:-1, 1:-1]
    total = padded[:, :-2, 1:-1] + padded[:, 2:, 1:-1]
    total = total + padded[:, 1:-1, :-2] + padded[:, 1:-1, 2:]
    total = total + jnp.roll(centre, 1, axis=-1) + jnp.roll(centre, -1, axis=-1)
    return total - 6.0 * centre


def relax_rate(labels):
    rate = jnp.where(labels == 1, 0.3, 0.02)
    rate = jnp.where(labels == 2, 0.6, rate)
    rate = jnp.where(labels == 3, 1.2, rate)
    return rate.astype(jnp.float32)


def signed_freq(index, length):
    return jnp.where(index < length // 2, index, index - length)


def dipole_block(freq_y, freq_z, freq_x):
    square_z = freq_z * freq_z
    total = freq_y * freq_y + square_z + freq_x * freq_x
    ratio = square_z.astype(jnp.float32) / jnp.maximum(total, 1).astype(jnp.float32)
    return jnp.where(total == 0, jnp.float32(0.0), jnp.float32(1.0 / 3.0) - ratio)


def cas_table(length):
    index = jnp.arange(length, dtype=jnp.int32)
    product = index[:, None] * index[None, :] % length
    angle = product.astype(jnp.float32) * (2.0 * math.pi / length)
    return jnp.cos(angle) + jnp.sin(angle)


def along(spec, table, values):
    return jnp.einsum(spec, table, values, precision=lax.Precision.HIGHEST)


def backward_sections(mag_start, mag_middle, adjoint_end, phase, rate):
    decay = jnp.exp(-rate)
    factor_real = decay * jnp.cos(phase)
    factor_imag = decay * jnp.sin(phase)
    lam_real, lam_imag = (adjoint_end[0], adjoint_end[1])
    phase_grad = jnp.zeros_like(phase)
    for checkpoint in (mag_middle, mag_start):
        w_real = factor_real * lam_real - factor_imag * lam_imag
        w_imag = factor_real * lam_imag + factor_imag * lam_real
        stacked = jnp.stack([checkpoint[0], checkpoint[1], w_real, w_imag])
        padded = with_halo(stacked, (("gy", 1), ("gz", 2)), 1)
        lapped = laplace_inner(padded)
        u_real = checkpoint[0] + 0.15 * lapped[0]
        u_imag = checkpoint[1] + 0.15 * lapped[1]
        phase_grad = phase_grad + (w_real * u_imag - w_imag * u_real)
        lam_real = w_real + 0.15 * lapped[2]
        lam_imag = w_imag + 0.15 * lapped[3]
    return (lam_real, lam_imag, phase_grad)


def dipole_adjoint(phase_grad):
    count_y = lax.axis_size("gy")
    count_z = lax.axis_size("gz")
    parts = count_y * count_z
    block_y, block_z, length_x = phase_grad.shape
    length_y = block_y * count_y
    length_z = block_z * count_z
    block_x = length_x // parts
    table_x = cas_table(length_x)
    table_y = cas_table(length_y)
    table_z = cas_table(length_z)
    scale = 1.0 / (float(length_y) * float(length_z) * float(length_x))
    spec = along("kn,yzn->kyz", table_x, phase_grad)
    spec = spec.reshape(parts, block_x, block_y, block_z)
    spec = lax.all_to_all(spec, ("gy", "gz"), 0, 0, tiled=True)
    spec = spec.reshape(count_y, count_z, block_x, block_y, block_z)
    spec = spec.transpose(2, 0, 3, 1, 4).reshape(block_x, length_y, length_z)
    spec = along("kz,xyz->xyk", table_z, spec)
    spec = along("ky,xyz->xkz", table_y, spec)
    freq_y = signed_freq(jnp.arange(length_y, dtype=jnp.int32), length_y)
    freq_z = signed_freq(jnp.arange(length_z, dtype=jnp.int32), length_z)
    index = lax.axis_index("gy") * count_z + lax.axis_index("gz")
    freq_x = signed_freq(index * block_x + jnp.arange(block_x, dtype=jnp.int32), length_x)
    kernel = dipole_block(freq_y[None, :, None], freq_z[None, None, :], freq_x[:, None, None])
    spec = spec * kernel
    spec = along("ky,xyz->xkz", table_y, spec)
    spec = along("kz,xyz->xyk", table_z, spec)
    spec = spec.reshape(block_x, count_y, block_y, count_z, block_z)
    spec = spec.transpose(1, 3, 0, 2, 4).reshape(parts, block_x, block_y, block_z)
    spec = lax.all_to_all(spec, ("gy", "gz"), 0, 0, tiled=True)
    spec = spec.reshape(length_x, block_y, block_z)
    return along("kn,nyz->yzk", table_x, spec) * scale


def per_device(mag_start, mag_middle, adjoint_end, phase, labels):
    rate = relax_rate(labels)
    lam_real, lam_imag, phase_grad = backward_sections(
        mag_start, mag_middle, adjoint_end, phase, rate
    )
    chi_grad = dipole_adjoint(phase_grad)
    return (jnp.stack([lam_real, lam_imag]), chi_grad)


def solution(mesh):
    return jax.shard_map(
        per_device,
        mesh=mesh,
        in_specs=(
            P(None, "gy", "gz", None),
            P(None, "gy", "gz", None),
            P(None, "gy", "gz", None),
            P("gy", "gz", None),
            P("gy", "gz", None),
        ),
        out_specs=(P(None, "gy", "gz", None), P("gy", "gz", None)),
        check_vma=False,
    )
```

```python
import functools
import math

import jax
import jax.numpy as jnp
from jax import lax
from jax.experimental import pallas as pl
from jax.experimental.pallas import tpu as pltpu
from jax.sharding import PartitionSpec as P


def relax_rate(labels):
    rate = jnp.where(labels == 1, 0.3, 0.02)
    rate = jnp.where(labels == 2, 0.6, rate)
    rate = jnp.where(labels == 3, 1.2, rate)
    return rate.astype(jnp.float32)


def signed_freq(index, length):
    return jnp.where(index < length // 2, index, index - length)


def dipole_block(freq_y, freq_z, freq_x):
    square_z = freq_z * freq_z
    total = freq_y * freq_y + square_z + freq_x * freq_x
    ratio = square_z.astype(jnp.float32) / jnp.maximum(total, 1).astype(jnp.float32)
    return jnp.where(total == 0, jnp.float32(0.0), jnp.float32(1.0 / 3.0) - ratio)


def cas_table(length):
    index = jnp.arange(length, dtype=jnp.int32)
    product = index[:, None] * index[None, :] % length
    angle = product.astype(jnp.float32) * (2.0 * math.pi / length)
    return jnp.cos(angle) + jnp.sin(angle)


def along(spec, table, values):
    return jnp.einsum(spec, table, values, precision=lax.Precision.HIGHEST)


def plane_update(centre, below, above, z_low, z_high):
    length_z, length_x = centre.shape
    row = lax.broadcasted_iota(jnp.int32, centre.shape, 0)
    up = jnp.where(row == 0, z_low, pltpu.roll(centre, 1, 0))
    down = jnp.where(row == length_z - 1, z_high, pltpu.roll(centre, length_z - 1, 0))
    total = below + above + up + down
    total = total + pltpu.roll(centre, 1, 1) + pltpu.roll(centre, length_x - 1, 1)
    return centre + 0.15 * (total - 6.0 * centre)


def neighbour_planes(cur_ref, prev_ref, next_ref, y_low_ref, y_high_ref, rows, field, comp, r):
    step = pl.program_id(0)
    last = pl.num_programs(0) - 1
    if r == 0:
        below = jnp.where(step == 0, y_low_ref[field], prev_ref[comp, 0])
    else:
        below = cur_ref[comp, r - 1]
    if r == rows - 1:
        above = jnp.where(step == last, y_high_ref[field], next_ref[comp, 0])
    else:
        above = cur_ref[comp, r + 1]
    return below, above


def first_kernel(*refs, rows):
    (mm_ref, mm_prev, mm_next, ms_ref, ms_prev, ms_next, w_ref, w_prev, w_next,
     factor_ref, y_low_ref, y_high_ref, z_low_ref, z_high_ref, pg_ref, w2_ref) = refs
    fields = ((mm_ref, mm_prev, mm_next), (ms_ref, ms_prev, ms_next), (w_ref, w_prev, w_next))
    for r in range(rows):
        new = []
        for f, (cur, prev, nxt) in enumerate(fields):
            pair = []
            for comp in range(2):
                below, above = neighbour_planes(cur, prev, nxt, y_low_ref, y_high_ref, rows, 2 * f + comp, comp, r)
                pair.append(plane_update(cur[comp, r], below, above,
                                         z_low_ref[2 * f + comp, r], z_high_ref[2 * f + comp, r]))
            new.append(pair)
        (u1_real, u1_imag), (u2_real, u2_imag), (lam_real, lam_imag) = new
        w_real = w_ref[0, r]
        w_imag = w_ref[1, r]
        f_real = factor_ref[0, r]
        f_imag = factor_ref[1, r]
        w2_real = f_real * lam_real - f_imag * lam_imag
        w2_imag = f_real * lam_imag + f_imag * lam_real
        grad = w_real * u1_imag - w_imag * u1_real
        pg_ref[r] = grad + (w2_real * u2_imag - w2_imag * u2_real)
        w2_ref[0, r] = w2_real
        w2_ref[1, r] = w2_imag


def second_kernel(w_ref, w_prev, w_next, y_low_ref, y_high_ref, z_low_ref, z_high_ref, out_ref, *, rows):
    for r in range(rows):
        for comp in range(2):
            below, above = neighbour_planes(w_ref, w_prev, w_next, y_low_ref, y_high_ref, rows, comp, comp, r)
            out_ref[comp, r] = plane_update(w_ref[comp, r], below, above,
                                            z_low_ref[comp, r], z_high_ref[comp, r])


def block_rows(length_y):
    rows = 4
    while length_y % rows:
        rows //= 2
    return rows


def field_specs(shape, rows):
    comps, length_y, length_z, length_x = shape
    cur = pl.BlockSpec((comps, rows, length_z, length_x), lambda i: (0, i, 0, 0))
    prev = pl.BlockSpec((comps, 1, length_z, length_x),
                        lambda i: (0, jnp.maximum(i * rows - 1, 0), 0, 0))
    nxt = pl.BlockSpec((comps, 1, length_z, length_x),
                       lambda i: (0, jnp.minimum(i * rows + rows, length_y - 1), 0, 0))
    return [cur, prev, nxt]


def exchange_halos(stacked):
    results = []
    for axis, dim in (("gy", 1), ("gz", 2)):
        count, length = (lax.axis_size(axis), stacked.shape[dim])
        up = [(i, (i + 1) % count) for i in range(count)]
        down = [(j, i) for i, j in up]
        last = lax.index_in_dim(stacked, length - 1, axis=dim, keepdims=False)
        first = lax.index_in_dim(stacked, 0, axis=dim, keepdims=False)
        low = lax.ppermute(last, axis, up)
        high = lax.ppermute(first, axis, down)
        if dim == 2:
            low = low[:, :, None, :]
            high = high[:, :, None, :]
        results.extend([low, high])
    return results


def backward_sections(mag_start, mag_middle, adjoint_end, phase, rate):
    decay = jnp.exp(-rate)
    factor = jnp.stack([decay * jnp.cos(phase), decay * jnp.sin(phase)])
    lam_real, lam_imag = (adjoint_end[0], adjoint_end[1])
    w_first = jnp.stack([factor[0] * lam_real - factor[1] * lam_imag,
                         factor[0] * lam_imag + factor[1] * lam_real])
    _, length_y, length_z, length_x = mag_start.shape
    rows = block_rows(length_y)
    halos = exchange_halos(jnp.concatenate([mag_middle, mag_start, w_first]))
    plane = jax.ShapeDtypeStruct((length_y, length_z, length_x), jnp.float32)
    pair = jax.ShapeDtypeStruct((2, length_y, length_z, length_x), jnp.float32)
    cur = pl.BlockSpec((2, rows, length_z, length_x), lambda i: (0, i, 0, 0))
    whole = lambda shape: pl.BlockSpec(shape, lambda i: (0,) * len(shape))
    zspec = lambda comps: pl.BlockSpec((comps, rows, 1, length_x), lambda i: (0, i, 0, 0))
    phase_grad, w_second = pl.pallas_call(
        functools.partial(first_kernel, rows=rows),
        grid=(length_y // rows,),
        in_specs=field_specs(mag_middle.shape, rows) + field_specs(mag_start.shape, rows)
        + field_specs(w_first.shape, rows)
        + [cur, whole((6, length_z, length_x)), whole((6, length_z, length_x)), zspec(6), zspec(6)],
        out_specs=[pl.BlockSpec((rows, length_z, length_x), lambda i: (i, 0, 0)), cur],
        out_shape=[plane, pair],
    )(mag_middle, mag_middle, mag_middle, mag_start, mag_start, mag_start,
      w_first, w_first, w_first, factor, *halos)
    halos = exchange_halos(w_second)
    lam = pl.pallas_call(
        functools.partial(second_kernel, rows=rows),
        grid=(length_y // rows,),
        in_specs=field_specs(w_second.shape, rows)
        + [whole((2, length_z, length_x)), whole((2, length_z, length_x)), zspec(2), zspec(2)],
        out_specs=cur,
        out_shape=pair,
    )(w_second, w_second, w_second, *halos)
    return (lam, phase_grad)


def dipole_adjoint(phase_grad):
    count_y = lax.axis_size("gy")
    count_z = lax.axis_size("gz")
    parts = count_y * count_z
    block_y, block_z, length_x = phase_grad.shape
    length_y = block_y * count_y
    length_z = block_z * count_z
    block_x = length_x // parts
    table_x = cas_table(length_x)
    table_y = cas_table(length_y)
    table_z = cas_table(length_z)
    scale = 1.0 / (float(length_y) * float(length_z) * float(length_x))
    spec = along("kn,yzn->kyz", table_x, phase_grad)
    spec = spec.reshape(parts, block_x, block_y, block_z)
    spec = lax.all_to_all(spec, ("gy", "gz"), 0, 0, tiled=True)
    spec = spec.reshape(count_y, count_z, block_x, block_y, block_z)
    spec = spec.transpose(2, 0, 3, 1, 4).reshape(block_x, length_y, length_z)
    spec = along("kz,xyz->xyk", table_z, spec)
    spec = along("ky,xyz->xkz", table_y, spec)
    freq_y = signed_freq(jnp.arange(length_y, dtype=jnp.int32), length_y)
    freq_z = signed_freq(jnp.arange(length_z, dtype=jnp.int32), length_z)
    index = lax.axis_index("gy") * count_z + lax.axis_index("gz")
    freq_x = signed_freq(index * block_x + jnp.arange(block_x, dtype=jnp.int32), length_x)
    kernel = dipole_block(freq_y[None, :, None], freq_z[None, None, :], freq_x[:, None, None])
    spec = spec * kernel
    spec = along("ky,xyz->xkz", table_y, spec)
    spec = along("kz,xyz->xyk", table_z, spec)
    spec = spec.reshape(block_x, count_y, block_y, count_z, block_z)
    spec = spec.transpose(1, 3, 0, 2, 4).reshape(parts, block_x, block_y, block_z)
    spec = lax.all_to_all(spec, ("gy", "gz"), 0, 0, tiled=True)
    spec = spec.reshape(length_x, block_y, block_z)
    return along("kn,nyz->yzk", table_x, spec) * scale


def per_device(mag_start, mag_middle, adjoint_end, phase, labels):
    rate = relax_rate(labels)
    lam, phase_grad = backward_sections(mag_start, mag_middle, adjoint_end, phase, rate)
    chi_grad = dipole_adjoint(phase_grad)
    return (lam, chi_grad)


def solution(mesh):
    return jax.shard_map(
        per_device,
        mesh=mesh,
        in_specs=(
            P(None, "gy", "gz", None),
            P(None, "gy", "gz", None),
            P(None, "gy", "gz", None),
            P("gy", "gz", None),
            P("gy", "gz", None),
        ),
        out_specs=(P(None, "gy", "gz", None), P("gy", "gz", None)),
        check_vma=False,
    )
```

```python
import functools
import math

import jax
import jax.numpy as jnp
from jax import lax
from jax.experimental import pallas as pl
from jax.experimental.pallas import tpu as pltpu
from jax.sharding import PartitionSpec as P


def signed_freq(index, length):
    return jnp.where(index < length // 2, index, index - length)


def dipole_block(freq_y, freq_z, freq_x):
    square_z = freq_z * freq_z
    total = freq_y * freq_y + square_z + freq_x * freq_x
    ratio = square_z.astype(jnp.float32) / jnp.maximum(total, 1).astype(jnp.float32)
    return jnp.where(total == 0, jnp.float32(0.0), jnp.float32(1.0 / 3.0) - ratio)


def cas_table(length):
    index = jnp.arange(length, dtype=jnp.int32)
    product = index[:, None] * index[None, :] % length
    angle = product.astype(jnp.float32) * (2.0 * math.pi / length)
    return jnp.cos(angle) + jnp.sin(angle)


def along(spec, table, values):
    return jnp.einsum(spec, table, values, precision=lax.Precision.HIGH)


def plane_update(centre, below, above, z_low, z_high):
    length_z, length_x = centre.shape
    row = lax.broadcasted_iota(jnp.int32, centre.shape, 0)
    up = jnp.where(row == 0, z_low, pltpu.roll(centre, 1, 0))
    down = jnp.where(row == length_z - 1, z_high, pltpu.roll(centre, length_z - 1, 0))
    total = below + above + up + down
    total = total + pltpu.roll(centre, 1, 1) + pltpu.roll(centre, length_x - 1, 1)
    return centre + 0.15 * (total - 6.0 * centre)


def neighbour_planes(cur_ref, prev_ref, next_ref, y_low_ref, y_high_ref, rows, field, comp, r):
    step = pl.program_id(0)
    last = pl.num_programs(0) - 1
    if r == 0:
        below = jnp.where(step == 0, y_low_ref[field], prev_ref[comp, 0])
    else:
        below = cur_ref[comp, r - 1]
    if r == rows - 1:
        above = jnp.where(step == last, y_high_ref[field], next_ref[comp, 0])
    else:
        above = cur_ref[comp, r + 1]
    return below, above


def write_edges(step, rows, r, values, y_first_ref, y_last_ref, z_first_ref, z_last_ref):
    for c, value in enumerate(values):
        z_first_ref[c, r] = value[0:1]
        z_last_ref[c, r] = value[value.shape[0] - 1:]
    if r == 0:
        @pl.when(step == 0)
        def _():
            for c, value in enumerate(values):
                y_first_ref[c] = value
    if r == rows - 1:
        @pl.when(step == pl.num_programs(0) - 1)
        def _():
            for c, value in enumerate(values):
                y_last_ref[c] = value


def factor_kernel(lam_ref, phase_ref, labels_ref, factor_ref, w_ref, *edge_refs, rows):
    step = pl.program_id(0)
    for r in range(rows):
        labels = labels_ref[r]
        rate = jnp.where(labels == 1, 0.3, 0.02)
        rate = jnp.where(labels == 2, 0.6, rate)
        rate = jnp.where(labels == 3, 1.2, rate).astype(jnp.float32)
        decay = jnp.exp(-rate)
        phase = phase_ref[r]
        f_real = decay * jnp.cos(phase)
        f_imag = decay * jnp.sin(phase)
        lam_real = lam_ref[0, r]
        lam_imag = lam_ref[1, r]
        w_real = f_real * lam_real - f_imag * lam_imag
        w_imag = f_real * lam_imag + f_imag * lam_real
        factor_ref[0, r] = f_real
        factor_ref[1, r] = f_imag
        w_ref[0, r] = w_real
        w_ref[1, r] = w_imag
        write_edges(step, rows, r, [w_real, w_imag], *edge_refs)


def edge_outputs(comps, length_y, length_z, length_x, rows):
    plane = jax.ShapeDtypeStruct((comps, length_z, length_x), jnp.float32)
    row = jax.ShapeDtypeStruct((comps, length_y, 1, length_x), jnp.float32)
    plane_spec = pl.BlockSpec((comps, length_z, length_x), lambda i: (0, 0, 0))
    row_spec = pl.BlockSpec((comps, rows, 1, length_x), lambda i: (0, i, 0, 0))
    return [plane, plane, row, row], [plane_spec, plane_spec, row_spec, row_spec]


def first_kernel(*refs, rows):
    (mm_ref, mm_prev, mm_next, ms_ref, ms_prev, ms_next, w_ref, w_prev, w_next,
     factor_ref, y_low_ref, y_high_ref, z_low_ref, z_high_ref, pg_ref, w2_ref) = refs[:16]
    step = pl.program_id(0)
    fields = ((mm_ref, mm_prev, mm_next), (ms_ref, ms_prev, ms_next), (w_ref, w_prev, w_next))
    for r in range(rows):
        new = []
        for f, (cur, prev, nxt) in enumerate(fields):
            pair = []
            for comp in range(2):
                below, above = neighbour_planes(cur, prev, nxt, y_low_ref, y_high_ref, rows, 2 * f + comp, comp, r)
                pair.append(plane_update(cur[comp, r], below, above,
                                         z_low_ref[2 * f + comp, r], z_high_ref[2 * f + comp, r]))
            new.append(pair)
        (u1_real, u1_imag), (u2_real, u2_imag), (lam_real, lam_imag) = new
        w_real = w_ref[0, r]
        w_imag = w_ref[1, r]
        f_real = factor_ref[0, r]
        f_imag = factor_ref[1, r]
        w2_real = f_real * lam_real - f_imag * lam_imag
        w2_imag = f_real * lam_imag + f_imag * lam_real
        grad = w_real * u1_imag - w_imag * u1_real
        pg_ref[r] = grad + (w2_real * u2_imag - w2_imag * u2_real)
        w2_ref[0, r] = w2_real
        w2_ref[1, r] = w2_imag
        write_edges(step, rows, r, [w2_real, w2_imag], *refs[16:])


def second_kernel(w_ref, w_prev, w_next, y_low_ref, y_high_ref, z_low_ref, z_high_ref, out_ref, *, rows):
    for r in range(rows):
        for comp in range(2):
            below, above = neighbour_planes(w_ref, w_prev, w_next, y_low_ref, y_high_ref, rows, comp, comp, r)
            out_ref[comp, r] = plane_update(w_ref[comp, r], below, above,
                                            z_low_ref[comp, r], z_high_ref[comp, r])


def block_rows(length_y):
    rows = 4
    while length_y % rows:
        rows //= 2
    return rows


def field_specs(shape, rows):
    comps, length_y, length_z, length_x = shape
    cur = pl.BlockSpec((comps, rows, length_z, length_x), lambda i: (0, i, 0, 0))
    prev = pl.BlockSpec((comps, 1, length_z, length_x),
                        lambda i: (0, jnp.maximum(i * rows - 1, 0), 0, 0))
    nxt = pl.BlockSpec((comps, 1, length_z, length_x),
                       lambda i: (0, jnp.minimum(i * rows + rows, length_y - 1), 0, 0))
    return [cur, prev, nxt]


def send_edges(y_first, y_last, z_first, z_last):
    results = []
    for axis, first, last in (("gy", y_first, y_last), ("gz", z_first, z_last)):
        count = lax.axis_size(axis)
        up = [(i, (i + 1) % count) for i in range(count)]
        down = [(j, i) for i, j in up]
        results.extend([lax.ppermute(last, axis, up), lax.ppermute(first, axis, down)])
    return results


def input_edges(fields):
    y_first = jnp.concatenate([f[:, 0] for f in fields])
    y_last = jnp.concatenate([f[:, -1] for f in fields])
    z_first = jnp.concatenate([f[:, :, 0:1] for f in fields])
    z_last = jnp.concatenate([f[:, :, -1:] for f in fields])
    return [y_first, y_last, z_first, z_last]


def backward_sections(mag_start, mag_middle, adjoint_end, phase, labels):
    _, length_y, length_z, length_x = mag_start.shape
    rows = block_rows(length_y)
    grid = (length_y // rows,)
    plane = jax.ShapeDtypeStruct((length_y, length_z, length_x), jnp.float32)
    pair = jax.ShapeDtypeStruct((2, length_y, length_z, length_x), jnp.float32)
    cur = pl.BlockSpec((2, rows, length_z, length_x), lambda i: (0, i, 0, 0))
    cur_plane = pl.BlockSpec((rows, length_z, length_x), lambda i: (i, 0, 0))
    whole = lambda shape: pl.BlockSpec(shape, lambda i: (0,) * len(shape))
    zspec = lambda comps: pl.BlockSpec((comps, rows, 1, length_x), lambda i: (0, i, 0, 0))
    edge_shapes, edge_specs = edge_outputs(2, length_y, length_z, length_x, rows)
    factor, w_first, *w_edges = pl.pallas_call(
        functools.partial(factor_kernel, rows=rows),
        grid=grid,
        in_specs=[cur, cur_plane, cur_plane],
        out_specs=[cur, cur] + edge_specs,
        out_shape=[pair, pair] + edge_shapes,
    )(adjoint_end, phase, labels)
    mag_edges = input_edges([mag_middle, mag_start])
    halos = send_edges(*[jnp.concatenate([a, b]) for a, b in zip(mag_edges, w_edges)])
    phase_grad, w_second, *w2_edges = pl.pallas_call(
        functools.partial(first_kernel, rows=rows),
        grid=grid,
        in_specs=field_specs(mag_middle.shape, rows) + field_specs(mag_start.shape, rows)
        + field_specs(w_first.shape, rows)
        + [cur, whole((6, length_z, length_x)), whole((6, length_z, length_x)), zspec(6), zspec(6)],
        out_specs=[cur_plane, cur] + edge_specs,
        out_shape=[plane, pair] + edge_shapes,
    )(mag_middle, mag_middle, mag_middle, mag_start, mag_start, mag_start,
      w_first, w_first, w_first, factor, *halos)
    halos = send_edges(*w2_edges)
    lam = pl.pallas_call(
        functools.partial(second_kernel, rows=rows),
        grid=grid,
        in_specs=field_specs(w_second.shape, rows)
        + [whole((2, length_z, length_x)), whole((2, length_z, length_x)), zspec(2), zspec(2)],
        out_specs=cur,
        out_shape=pair,
    )(w_second, w_second, w_second, *halos)
    return (lam, phase_grad)


def dipole_adjoint(phase_grad):
    count_y = lax.axis_size("gy")
    count_z = lax.axis_size("gz")
    parts = count_y * count_z
    block_y, block_z, length_x = phase_grad.shape
    length_y = block_y * count_y
    length_z = block_z * count_z
    block_x = length_x // parts
    table_x = cas_table(length_x)
    table_y = cas_table(length_y)
    table_z = cas_table(length_z)
    scale = 1.0 / (float(length_y) * float(length_z) * float(length_x))
    spec = along("kn,yzn->kyz", table_x, phase_grad)
    spec = spec.reshape(parts, block_x, block_y, block_z)
    spec = lax.all_to_all(spec, ("gy", "gz"), 0, 0, tiled=True)
    spec = spec.reshape(count_y, count_z, block_x, block_y, block_z)
    spec = spec.transpose(2, 0, 3, 1, 4).reshape(block_x, length_y, length_z)
    spec = along("kz,xyz->xyk", table_z, spec)
    spec = along("ky,xyz->xkz", table_y, spec)
    freq_y = signed_freq(jnp.arange(length_y, dtype=jnp.int32), length_y)
    freq_z = signed_freq(jnp.arange(length_z, dtype=jnp.int32), length_z)
    index = lax.axis_index("gy") * count_z + lax.axis_index("gz")
    freq_x = signed_freq(index * block_x + jnp.arange(block_x, dtype=jnp.int32), length_x)
    kernel = dipole_block(freq_y[None, :, None], freq_z[None, None, :], freq_x[:, None, None])
    spec = spec * kernel
    spec = along("ky,xyz->xkz", table_y, spec)
    spec = along("kz,xyz->xyk", table_z, spec)
    spec = spec.reshape(block_x, count_y, block_y, count_z, block_z)
    spec = spec.transpose(1, 3, 0, 2, 4).reshape(parts, block_x, block_y, block_z)
    spec = lax.all_to_all(spec, ("gy", "gz"), 0, 0, tiled=True)
    spec = spec.reshape(length_x, block_y, block_z)
    return along("kn,nyz->yzk", table_x, spec) * scale


def per_device(mag_start, mag_middle, adjoint_end, phase, labels):
    lam, phase_grad = backward_sections(mag_start, mag_middle, adjoint_end, phase, labels)
    chi_grad = dipole_adjoint(phase_grad)
    return (lam, chi_grad)


def solution(mesh):
    return jax.shard_map(
        per_device,
        mesh=mesh,
        in_specs=(
            P(None, "gy", "gz", None),
            P(None, "gy", "gz", None),
            P(None, "gy", "gz", None),
            P("gy", "gz", None),
            P("gy", "gz", None),
        ),
        out_specs=(P(None, "gy", "gz", None), P("gy", "gz", None)),
        check_vma=False,
    )
```

```python
import functools
import math

import jax
import jax.numpy as jnp
from jax import lax
from jax.experimental import pallas as pl
from jax.experimental.pallas import tpu as pltpu
from jax.sharding import PartitionSpec as P


def signed_freq(index, length):
    return jnp.where(index < length // 2, index, index - length)


def dipole_block(freq_y, freq_z, freq_x):
    square_z = freq_z * freq_z
    total = freq_y * freq_y + square_z + freq_x * freq_x
    ratio = square_z.astype(jnp.float32) / jnp.maximum(total, 1).astype(jnp.float32)
    return jnp.where(total == 0, jnp.float32(0.0), jnp.float32(1.0 / 3.0) - ratio)


def cas_table(length):
    index = jnp.arange(length, dtype=jnp.int32)
    product = index[:, None] * index[None, :] % length
    angle = product.astype(jnp.float32) * (2.0 * math.pi / length)
    return jnp.cos(angle) + jnp.sin(angle)


def along(spec, table, values):
    return jnp.einsum(spec, table, values, precision=lax.Precision.HIGH)


def plane_update(centre, below, above, z_low, z_high):
    length_z, length_x = centre.shape
    row = lax.broadcasted_iota(jnp.int32, centre.shape, 0)
    up = jnp.where(row == 0, z_low, pltpu.roll(centre, 1, 0))
    down = jnp.where(row == length_z - 1, z_high, pltpu.roll(centre, length_z - 1, 0))
    total = below + above + up + down
    total = total + pltpu.roll(centre, 1, 1) + pltpu.roll(centre, length_x - 1, 1)
    return centre + 0.15 * (total - 6.0 * centre)


def neighbour_planes(cur_ref, prev_ref, next_ref, y_low_ref, y_high_ref, rows, field, comp, r):
    step = pl.program_id(0)
    last = pl.num_programs(0) - 1
    if r == 0:
        below = jnp.where(step == 0, y_low_ref[field], prev_ref[comp, 0])
    else:
        below = cur_ref[comp, r - 1]
    if r == rows - 1:
        above = jnp.where(step == last, y_high_ref[field], next_ref[comp, 0])
    else:
        above = cur_ref[comp, r + 1]
    return below, above


def write_edges(step, rows, r, values, y_first_ref, y_last_ref, z_first_ref, z_last_ref):
    for c, value in enumerate(values):
        z_first_ref[c, r] = value[0:1]
        z_last_ref[c, r] = value[value.shape[0] - 1:]
    if r == 0:
        @pl.when(step == 0)
        def _():
            for c, value in enumerate(values):
                y_first_ref[c] = value
    if r == rows - 1:
        @pl.when(step == pl.num_programs(0) - 1)
        def _():
            for c, value in enumerate(values):
                y_last_ref[c] = value


def factor_kernel(lam_ref, phase_ref, labels_ref, factor_ref, w_ref, *edge_refs, rows):
    step = pl.program_id(0)
    for r in range(rows):
        labels = labels_ref[r]
        rate = jnp.where(labels == 1, 0.3, 0.02)
        rate = jnp.where(labels == 2, 0.6, rate)
        rate = jnp.where(labels == 3, 1.2, rate).astype(jnp.float32)
        decay = jnp.exp(-rate)
        phase = phase_ref[r]
        f_real = decay * jnp.cos(phase)
        f_imag = decay * jnp.sin(phase)
        lam_real = lam_ref[0, r]
        lam_imag = lam_ref[1, r]
        w_real = f_real * lam_real - f_imag * lam_imag
        w_imag = f_real * lam_imag + f_imag * lam_real
        factor_ref[0, r] = f_real
        factor_ref[1, r] = f_imag
        w_ref[0, r] = w_real
        w_ref[1, r] = w_imag
        write_edges(step, rows, r, [w_real, w_imag], *edge_refs)


def edge_outputs(comps, length_y, length_z, length_x, rows):
    plane = jax.ShapeDtypeStruct((comps, length_z, length_x), jnp.float32)
    row = jax.ShapeDtypeStruct((comps, length_y, 1, length_x), jnp.float32)
    plane_spec = pl.BlockSpec((comps, length_z, length_x), lambda i: (0, 0, 0))
    row_spec = pl.BlockSpec((comps, rows, 1, length_x), lambda i: (0, i, 0, 0))
    return [plane, plane, row, row], [plane_spec, plane_spec, row_spec, row_spec]


def first_kernel(*refs, rows):
    (mm_ref, mm_prev, mm_next, ms_ref, ms_prev, ms_next, w_ref, w_prev, w_next,
     factor_ref, *halo_refs) = refs[:18]
    pg_ref, w2_ref = refs[18:20]
    step = pl.program_id(0)
    fields = ((mm_ref, mm_prev, mm_next), (ms_ref, ms_prev, ms_next), (w_ref, w_prev, w_next))
    for r in range(rows):
        new = []
        for f, (cur, prev, nxt) in enumerate(fields):
            y_low_ref, y_high_ref, z_low_ref, z_high_ref = halo_refs[4 * (f // 2):4 * (f // 2) + 4]
            pair = []
            for comp in range(2):
                index = 2 * f + comp if f < 2 else comp
                below, above = neighbour_planes(cur, prev, nxt, y_low_ref, y_high_ref, rows, index, comp, r)
                pair.append(plane_update(cur[comp, r], below, above,
                                         z_low_ref[index, r], z_high_ref[index, r]))
            new.append(pair)
        (u1_real, u1_imag), (u2_real, u2_imag), (lam_real, lam_imag) = new
        w_real = w_ref[0, r]
        w_imag = w_ref[1, r]
        f_real = factor_ref[0, r]
        f_imag = factor_ref[1, r]
        w2_real = f_real * lam_real - f_imag * lam_imag
        w2_imag = f_real * lam_imag + f_imag * lam_real
        grad = w_real * u1_imag - w_imag * u1_real
        pg_ref[r] = grad + (w2_real * u2_imag - w2_imag * u2_real)
        w2_ref[0, r] = w2_real
        w2_ref[1, r] = w2_imag
        write_edges(step, rows, r, [w2_real, w2_imag], *refs[20:])


def second_kernel(w_ref, w_prev, w_next, y_low_ref, y_high_ref, z_low_ref, z_high_ref, out_ref, *, rows):
    for r in range(rows):
        for comp in range(2):
            below, above = neighbour_planes(w_ref, w_prev, w_next, y_low_ref, y_high_ref, rows, comp, comp, r)
            out_ref[comp, r] = plane_update(w_ref[comp, r], below, above,
                                            z_low_ref[comp, r], z_high_ref[comp, r])


def block_rows(length_y):
    rows = 4
    while length_y % rows:
        rows //= 2
    return rows


def field_specs(shape, rows):
    comps, length_y, length_z, length_x = shape
    cur = pl.BlockSpec((comps, rows, length_z, length_x), lambda i: (0, i, 0, 0))
    prev = pl.BlockSpec((comps, 1, length_z, length_x),
                        lambda i: (0, jnp.maximum(i * rows - 1, 0), 0, 0))
    nxt = pl.BlockSpec((comps, 1, length_z, length_x),
                       lambda i: (0, jnp.minimum(i * rows + rows, length_y - 1), 0, 0))
    return [cur, prev, nxt]


def send_edges(y_first, y_last, z_first, z_last):
    results = []
    for axis, first, last in (("gy", y_first, y_last), ("gz", z_first, z_last)):
        count = lax.axis_size(axis)
        up = [(i, (i + 1) % count) for i in range(count)]
        down = [(j, i) for i, j in up]
        results.extend([lax.ppermute(last, axis, up), lax.ppermute(first, axis, down)])
    return results


def input_edges(fields):
    y_first = jnp.concatenate([f[:, 0] for f in fields])
    y_last = jnp.concatenate([f[:, -1] for f in fields])
    z_first = jnp.concatenate([f[:, :, 0:1] for f in fields])
    z_last = jnp.concatenate([f[:, :, -1:] for f in fields])
    return [y_first, y_last, z_first, z_last]


def backward_sections(mag_start, mag_middle, adjoint_end, phase, labels):
    _, length_y, length_z, length_x = mag_start.shape
    rows = block_rows(length_y)
    grid = (length_y // rows,)
    plane = jax.ShapeDtypeStruct((length_y, length_z, length_x), jnp.float32)
    pair = jax.ShapeDtypeStruct((2, length_y, length_z, length_x), jnp.float32)
    cur = pl.BlockSpec((2, rows, length_z, length_x), lambda i: (0, i, 0, 0))
    cur_plane = pl.BlockSpec((rows, length_z, length_x), lambda i: (i, 0, 0))
    whole = lambda shape: pl.BlockSpec(shape, lambda i: (0,) * len(shape))
    zspec = lambda comps: pl.BlockSpec((comps, rows, 1, length_x), lambda i: (0, i, 0, 0))
    edge_shapes, edge_specs = edge_outputs(2, length_y, length_z, length_x, rows)
    factor, w_first, *w_edges = pl.pallas_call(
        functools.partial(factor_kernel, rows=rows),
        grid=grid,
        in_specs=[cur, cur_plane, cur_plane],
        out_specs=[cur, cur] + edge_specs,
        out_shape=[pair, pair] + edge_shapes,
    )(adjoint_end, phase, labels)
    mag_halos = send_edges(*input_edges([mag_middle, mag_start]))
    w_halos = send_edges(*w_edges)
    phase_grad, w_second, *w2_edges = pl.pallas_call(
        functools.partial(first_kernel, rows=rows),
        grid=grid,
        in_specs=field_specs(mag_middle.shape, rows) + field_specs(mag_start.shape, rows)
        + field_specs(w_first.shape, rows)
        + [cur, whole((4, length_z, length_x)), whole((4, length_z, length_x)), zspec(4), zspec(4),
           whole((2, length_z, length_x)), whole((2, length_z, length_x)), zspec(2), zspec(2)],
        out_specs=[cur_plane, cur] + edge_specs,
        out_shape=[plane, pair] + edge_shapes,
    )(mag_middle, mag_middle, mag_middle, mag_start, mag_start, mag_start,
      w_first, w_first, w_first, factor, *mag_halos, *w_halos)
    halos = send_edges(*w2_edges)
    lam = pl.pallas_call(
        functools.partial(second_kernel, rows=rows),
        grid=grid,
        in_specs=field_specs(w_second.shape, rows)
        + [whole((2, length_z, length_x)), whole((2, length_z, length_x)), zspec(2), zspec(2)],
        out_specs=cur,
        out_shape=pair,
    )(w_second, w_second, w_second, *halos)
    return (lam, phase_grad)


def dipole_adjoint(phase_grad):
    count_y = lax.axis_size("gy")
    count_z = lax.axis_size("gz")
    parts = count_y * count_z
    block_y, block_z, length_x = phase_grad.shape
    length_y = block_y * count_y
    length_z = block_z * count_z
    block_x = length_x // parts
    table_x = cas_table(length_x)
    table_y = cas_table(length_y)
    table_z = cas_table(length_z)
    scale = 1.0 / (float(length_y) * float(length_z) * float(length_x))
    spec = along("kn,yzn->kyz", table_x, phase_grad)
    spec = spec.reshape(parts, block_x, block_y, block_z)
    spec = lax.all_to_all(spec, ("gy", "gz"), 0, 0, tiled=True)
    spec = spec.reshape(count_y, count_z, block_x, block_y, block_z)
    spec = spec.transpose(2, 0, 3, 1, 4).reshape(block_x, length_y, length_z)
    spec = along("kz,xyz->xyk", table_z, spec)
    spec = along("ky,xyz->xkz", table_y, spec)
    freq_y = signed_freq(jnp.arange(length_y, dtype=jnp.int32), length_y)
    freq_z = signed_freq(jnp.arange(length_z, dtype=jnp.int32), length_z)
    index = lax.axis_index("gy") * count_z + lax.axis_index("gz")
    freq_x = signed_freq(index * block_x + jnp.arange(block_x, dtype=jnp.int32), length_x)
    kernel = dipole_block(freq_y[None, :, None], freq_z[None, None, :], freq_x[:, None, None])
    spec = spec * kernel
    spec = along("ky,xyz->xkz", table_y, spec)
    spec = along("kz,xyz->xyk", table_z, spec)
    spec = spec.reshape(block_x, count_y, block_y, count_z, block_z)
    spec = spec.transpose(1, 3, 0, 2, 4).reshape(parts, block_x, block_y, block_z)
    spec = lax.all_to_all(spec, ("gy", "gz"), 0, 0, tiled=True)
    spec = spec.reshape(length_x, block_y, block_z)
    return along("kn,nyz->yzk", table_x, spec) * scale


def per_device(mag_start, mag_middle, adjoint_end, phase, labels):
    lam, phase_grad = backward_sections(mag_start, mag_middle, adjoint_end, phase, labels)
    chi_grad = dipole_adjoint(phase_grad)
    return (lam, chi_grad)


def solution(mesh):
    return jax.shard_map(
        per_device,
        mesh=mesh,
        in_specs=(
            P(None, "gy", "gz", None),
            P(None, "gy", "gz", None),
            P(None, "gy", "gz", None),
            P("gy", "gz", None),
            P("gy", "gz", None),
        ),
        out_specs=(P(None, "gy", "gz", None), P("gy", "gz", None)),
        check_vma=False,
    )
```

```python
import functools
import math

import jax
import jax.numpy as jnp
from jax import lax
from jax.experimental import pallas as pl
from jax.experimental.pallas import tpu as pltpu
from jax.sharding import PartitionSpec as P


def signed_freq(index, length):
    return jnp.where(index < length // 2, index, index - length)


def dipole_block(freq_y, freq_z, freq_x):
    square_z = freq_z * freq_z
    total = freq_y * freq_y + square_z + freq_x * freq_x
    ratio = square_z.astype(jnp.float32) / jnp.maximum(total, 1).astype(jnp.float32)
    return jnp.where(total == 0, jnp.float32(0.0), jnp.float32(1.0 / 3.0) - ratio)


def cas_table(length):
    index = jnp.arange(length, dtype=jnp.int32)
    product = index[:, None] * index[None, :] % length
    angle = product.astype(jnp.float32) * (2.0 * math.pi / length)
    return jnp.cos(angle) + jnp.sin(angle)


def along(spec, table, values):
    return jnp.einsum(spec, table, values, precision=lax.Precision.HIGH)


def plane_update(centre, below, above, z_low, z_high):
    length_z, length_x = centre.shape
    row = lax.broadcasted_iota(jnp.int32, centre.shape, 0)
    up = jnp.where(row == 0, z_low, pltpu.roll(centre, 1, 0))
    down = jnp.where(row == length_z - 1, z_high, pltpu.roll(centre, length_z - 1, 0))
    total = below + above + up + down
    total = total + pltpu.roll(centre, 1, 1) + pltpu.roll(centre, length_x - 1, 1)
    return centre + 0.15 * (total - 6.0 * centre)


def neighbour_planes(cur_ref, prev_ref, next_ref, y_low_ref, y_high_ref, rows, field, comp, r):
    step = pl.program_id(0)
    last = pl.num_programs(0) - 1
    if r == 0:
        below = jnp.where(step == 0, y_low_ref[field], prev_ref[comp, 0])
    else:
        below = cur_ref[comp, r - 1]
    if r == rows - 1:
        above = jnp.where(step == last, y_high_ref[field], next_ref[comp, 0])
    else:
        above = cur_ref[comp, r + 1]
    return below, above


def write_edges(step, rows, r, values, y_first_ref, y_last_ref, z_first_ref, z_last_ref):
    for c, value in enumerate(values):
        z_first_ref[c, r] = value[0:1]
        z_last_ref[c, r] = value[value.shape[0] - 1:]
    if r == 0:
        @pl.when(step == 0)
        def _():
            for c, value in enumerate(values):
                y_first_ref[c] = value
    if r == rows - 1:
        @pl.when(step == pl.num_programs(0) - 1)
        def _():
            for c, value in enumerate(values):
                y_last_ref[c] = value


def step_factor(labels, phase):
    rate = jnp.where(labels == 1, 0.3, 0.02)
    rate = jnp.where(labels == 2, 0.6, rate)
    rate = jnp.where(labels == 3, 1.2, rate).astype(jnp.float32)
    decay = jnp.exp(-rate)
    return decay * jnp.cos(phase), decay * jnp.sin(phase)


def halo_w(halo):
    f_real, f_imag = step_factor(halo[3], halo[2])
    lam_real, lam_imag = halo[0], halo[1]
    return jnp.stack([f_real * lam_real - f_imag * lam_imag, f_real * lam_imag + f_imag * lam_real])


def factor_kernel(lam_ref, phase_ref, labels_ref, factor_ref, w_ref, *, rows):
    for r in range(rows):
        f_real, f_imag = step_factor(labels_ref[r], phase_ref[r])
        lam_real = lam_ref[0, r]
        lam_imag = lam_ref[1, r]
        w_real = f_real * lam_real - f_imag * lam_imag
        w_imag = f_real * lam_imag + f_imag * lam_real
        factor_ref[0, r] = f_real
        factor_ref[1, r] = f_imag
        w_ref[0, r] = w_real
        w_ref[1, r] = w_imag


def edge_outputs(comps, length_y, length_z, length_x, rows):
    plane = jax.ShapeDtypeStruct((comps, length_z, length_x), jnp.float32)
    row = jax.ShapeDtypeStruct((comps, length_y, 1, length_x), jnp.float32)
    plane_spec = pl.BlockSpec((comps, length_z, length_x), lambda i: (0, 0, 0))
    row_spec = pl.BlockSpec((comps, rows, 1, length_x), lambda i: (0, i, 0, 0))
    return [plane, plane, row, row], [plane_spec, plane_spec, row_spec, row_spec]


def first_kernel(*refs, rows):
    (mm_ref, mm_prev, mm_next, ms_ref, ms_prev, ms_next, w_ref, w_prev, w_next,
     factor_ref, *halo_refs) = refs[:18]
    pg_ref, w2_ref = refs[18:20]
    step = pl.program_id(0)
    fields = ((mm_ref, mm_prev, mm_next), (ms_ref, ms_prev, ms_next), (w_ref, w_prev, w_next))
    for r in range(rows):
        new = []
        for f, (cur, prev, nxt) in enumerate(fields):
            y_low_ref, y_high_ref, z_low_ref, z_high_ref = halo_refs[4 * (f // 2):4 * (f // 2) + 4]
            pair = []
            for comp in range(2):
                index = 2 * f + comp if f < 2 else comp
                below, above = neighbour_planes(cur, prev, nxt, y_low_ref, y_high_ref, rows, index, comp, r)
                pair.append(plane_update(cur[comp, r], below, above,
                                         z_low_ref[index, r], z_high_ref[index, r]))
            new.append(pair)
        (u1_real, u1_imag), (u2_real, u2_imag), (lam_real, lam_imag) = new
        w_real = w_ref[0, r]
        w_imag = w_ref[1, r]
        f_real = factor_ref[0, r]
        f_imag = factor_ref[1, r]
        w2_real = f_real * lam_real - f_imag * lam_imag
        w2_imag = f_real * lam_imag + f_imag * lam_real
        grad = w_real * u1_imag - w_imag * u1_real
        pg_ref[r] = grad + (w2_real * u2_imag - w2_imag * u2_real)
        w2_ref[0, r] = w2_real
        w2_ref[1, r] = w2_imag
        write_edges(step, rows, r, [w2_real, w2_imag], *refs[20:])


def second_kernel(w_ref, w_prev, w_next, y_low_ref, y_high_ref, z_low_ref, z_high_ref, out_ref, *, rows):
    for r in range(rows):
        for comp in range(2):
            below, above = neighbour_planes(w_ref, w_prev, w_next, y_low_ref, y_high_ref, rows, comp, comp, r)
            out_ref[comp, r] = plane_update(w_ref[comp, r], below, above,
                                            z_low_ref[comp, r], z_high_ref[comp, r])


def block_rows(length_y):
    rows = 4
    while length_y % rows:
        rows //= 2
    return rows


def field_specs(shape, rows):
    comps, length_y, length_z, length_x = shape
    cur = pl.BlockSpec((comps, rows, length_z, length_x), lambda i: (0, i, 0, 0))
    prev = pl.BlockSpec((comps, 1, length_z, length_x),
                        lambda i: (0, jnp.maximum(i * rows - 1, 0), 0, 0))
    nxt = pl.BlockSpec((comps, 1, length_z, length_x),
                       lambda i: (0, jnp.minimum(i * rows + rows, length_y - 1), 0, 0))
    return [cur, prev, nxt]


def send_edges(y_first, y_last, z_first, z_last):
    results = []
    for axis, first, last in (("gy", y_first, y_last), ("gz", z_first, z_last)):
        count = lax.axis_size(axis)
        up = [(i, (i + 1) % count) for i in range(count)]
        down = [(j, i) for i, j in up]
        if count == 2:
            both = lax.ppermute(jnp.stack([last, first]), axis, up)
            results.extend([both[0], both[1]])
        else:
            results.extend([lax.ppermute(last, axis, up), lax.ppermute(first, axis, down)])
    return results


def input_edges(fields):
    y_first = jnp.concatenate([f[:, 0] for f in fields])
    y_last = jnp.concatenate([f[:, -1] for f in fields])
    z_first = jnp.concatenate([f[:, :, 0:1] for f in fields])
    z_last = jnp.concatenate([f[:, :, -1:] for f in fields])
    return [y_first, y_last, z_first, z_last]


def backward_sections(mag_start, mag_middle, adjoint_end, phase, labels):
    _, length_y, length_z, length_x = mag_start.shape
    rows = block_rows(length_y)
    grid = (length_y // rows,)
    plane = jax.ShapeDtypeStruct((length_y, length_z, length_x), jnp.float32)
    pair = jax.ShapeDtypeStruct((2, length_y, length_z, length_x), jnp.float32)
    cur = pl.BlockSpec((2, rows, length_z, length_x), lambda i: (0, i, 0, 0))
    cur_plane = pl.BlockSpec((rows, length_z, length_x), lambda i: (i, 0, 0))
    whole = lambda shape: pl.BlockSpec(shape, lambda i: (0,) * len(shape))
    zspec = lambda comps: pl.BlockSpec((comps, rows, 1, length_x), lambda i: (0, i, 0, 0))
    edge_shapes, edge_specs = edge_outputs(2, length_y, length_z, length_x, rows)
    halos = send_edges(*input_edges(
        [mag_middle, mag_start, adjoint_end, phase[None], labels[None].astype(jnp.float32)]))
    mag_halos = [h[:4] for h in halos]
    w_halos = [halo_w(h[4:]) for h in halos]
    factor, w_first = pl.pallas_call(
        functools.partial(factor_kernel, rows=rows),
        grid=grid,
        in_specs=[cur, cur_plane, cur_plane],
        out_specs=[cur, cur],
        out_shape=[pair, pair],
    )(adjoint_end, phase, labels)
    phase_grad, w_second, *w2_edges = pl.pallas_call(
        functools.partial(first_kernel, rows=rows),
        grid=grid,
        in_specs=field_specs(mag_middle.shape, rows) + field_specs(mag_start.shape, rows)
        + field_specs(w_first.shape, rows)
        + [cur, whole((4, length_z, length_x)), whole((4, length_z, length_x)), zspec(4), zspec(4),
           whole((2, length_z, length_x)), whole((2, length_z, length_x)), zspec(2), zspec(2)],
        out_specs=[cur_plane, cur] + edge_specs,
        out_shape=[plane, pair] + edge_shapes,
    )(mag_middle, mag_middle, mag_middle, mag_start, mag_start, mag_start,
      w_first, w_first, w_first, factor, *mag_halos, *w_halos)
    halos = send_edges(*w2_edges)
    lam = pl.pallas_call(
        functools.partial(second_kernel, rows=rows),
        grid=grid,
        in_specs=field_specs(w_second.shape, rows)
        + [whole((2, length_z, length_x)), whole((2, length_z, length_x)), zspec(2), zspec(2)],
        out_specs=cur,
        out_shape=pair,
    )(w_second, w_second, w_second, *halos)
    return (lam, phase_grad)


def dipole_adjoint(phase_grad):
    count_y = lax.axis_size("gy")
    count_z = lax.axis_size("gz")
    parts = count_y * count_z
    block_y, block_z, length_x = phase_grad.shape
    length_y = block_y * count_y
    length_z = block_z * count_z
    block_x = length_x // parts
    table_x = cas_table(length_x)
    table_y = cas_table(length_y)
    table_z = cas_table(length_z)
    scale = 1.0 / (float(length_y) * float(length_z) * float(length_x))
    spec = along("kn,yzn->kyz", table_x, phase_grad)
    spec = spec.reshape(parts, block_x, block_y, block_z)
    spec = lax.all_to_all(spec, ("gy", "gz"), 0, 0, tiled=True)
    spec = spec.reshape(count_y, count_z, block_x, block_y, block_z)
    spec = spec.transpose(2, 0, 3, 1, 4).reshape(block_x, length_y, length_z)
    spec = along("kz,xyz->xyk", table_z, spec)
    spec = along("ky,xyz->xkz", table_y, spec)
    freq_y = signed_freq(jnp.arange(length_y, dtype=jnp.int32), length_y)
    freq_z = signed_freq(jnp.arange(length_z, dtype=jnp.int32), length_z)
    index = lax.axis_index("gy") * count_z + lax.axis_index("gz")
    freq_x = signed_freq(index * block_x + jnp.arange(block_x, dtype=jnp.int32), length_x)
    kernel = dipole_block(freq_y[None, :, None], freq_z[None, None, :], freq_x[:, None, None])
    spec = spec * kernel
    spec = along("ky,xyz->xkz", table_y, spec)
    spec = along("kz,xyz->xyk", table_z, spec)
    spec = spec.reshape(block_x, count_y, block_y, count_z, block_z)
    spec = spec.transpose(1, 3, 0, 2, 4).reshape(parts, block_x, block_y, block_z)
    spec = lax.all_to_all(spec, ("gy", "gz"), 0, 0, tiled=True)
    spec = spec.reshape(length_x, block_y, block_z)
    return along("kn,nyz->yzk", table_x, spec) * scale


def per_device(mag_start, mag_middle, adjoint_end, phase, labels):
    lam, phase_grad = backward_sections(mag_start, mag_middle, adjoint_end, phase, labels)
    chi_grad = dipole_adjoint(phase_grad)
    return (lam, chi_grad)


def solution(mesh):
    return jax.shard_map(
        per_device,
        mesh=mesh,
        in_specs=(
            P(None, "gy", "gz", None),
            P(None, "gy", "gz", None),
            P(None, "gy", "gz", None),
            P("gy", "gz", None),
            P("gy", "gz", None),
        ),
        out_specs=(P(None, "gy", "gz", None), P("gy", "gz", None)),
        check_vma=False,
    )
```

```python
import functools
import math

import jax
import jax.numpy as jnp
from jax import lax
from jax.experimental import pallas as pl
from jax.experimental.pallas import tpu as pltpu
from jax.sharding import PartitionSpec as P


def signed_freq(index, length):
    return jnp.where(index < length // 2, index, index - length)


def dipole_block(freq_y, freq_z, freq_x):
    square_z = freq_z * freq_z
    total = freq_y * freq_y + square_z + freq_x * freq_x
    ratio = square_z.astype(jnp.float32) / jnp.maximum(total, 1).astype(jnp.float32)
    return jnp.where(total == 0, jnp.float32(0.0), jnp.float32(1.0 / 3.0) - ratio)


def cas_table(length):
    index = jnp.arange(length, dtype=jnp.int32)
    product = index[:, None] * index[None, :] % length
    angle = product.astype(jnp.float32) * (2.0 * math.pi / length)
    return jnp.cos(angle) + jnp.sin(angle)


def along(spec, table, values):
    return jnp.einsum(spec, table, values, precision=lax.Precision.HIGH)


def plane_update(centre, below, above, z_low, z_high):
    length_z, length_x = centre.shape
    row = lax.broadcasted_iota(jnp.int32, centre.shape, 0)
    up = jnp.where(row == 0, z_low, pltpu.roll(centre, 1, 0))
    down = jnp.where(row == length_z - 1, z_high, pltpu.roll(centre, length_z - 1, 0))
    total = below + above + up + down
    total = total + pltpu.roll(centre, 1, 1) + pltpu.roll(centre, length_x - 1, 1)
    return centre + 0.15 * (total - 6.0 * centre)


def neighbour_planes(cur_ref, prev_ref, next_ref, y_low_ref, y_high_ref, rows, field, comp, r):
    step = pl.program_id(0)
    last = pl.num_programs(0) - 1
    if r == 0:
        below = jnp.where(step == 0, y_low_ref[field], prev_ref[comp, 0])
    else:
        below = cur_ref[comp, r - 1]
    if r == rows - 1:
        above = jnp.where(step == last, y_high_ref[field], next_ref[comp, 0])
    else:
        above = cur_ref[comp, r + 1]
    return below, above


def write_edges(step, rows, r, values, y_first_ref, y_last_ref, z_first_ref, z_last_ref):
    for c, value in enumerate(values):
        z_first_ref[c, r] = value[0:1]
        z_last_ref[c, r] = value[value.shape[0] - 1:]
    if r == 0:
        @pl.when(step == 0)
        def _():
            for c, value in enumerate(values):
                y_first_ref[c] = value
    if r == rows - 1:
        @pl.when(step == pl.num_programs(0) - 1)
        def _():
            for c, value in enumerate(values):
                y_last_ref[c] = value


def step_factor(labels, phase):
    rate = jnp.where(labels == 1, 0.3, 0.02)
    rate = jnp.where(labels == 2, 0.6, rate)
    rate = jnp.where(labels == 3, 1.2, rate).astype(jnp.float32)
    decay = jnp.exp(-rate)
    return decay * jnp.cos(phase), decay * jnp.sin(phase)


def first_w(lam_real, lam_imag, labels, phase):
    f_real, f_imag = step_factor(labels, phase)
    return (f_real * lam_real - f_imag * lam_imag, f_real * lam_imag + f_imag * lam_real), (f_real, f_imag)


def factor_kernel(lam_ref, phase_ref, labels_ref, factor_ref, w_ref, *, rows):
    for r in range(rows):
        (w_real, w_imag), (f_real, f_imag) = first_w(lam_ref[0, r], lam_ref[1, r], labels_ref[r], phase_ref[r])
        factor_ref[0, r] = f_real
        factor_ref[1, r] = f_imag
        w_ref[0, r] = w_real
        w_ref[1, r] = w_imag


def edges_kernel(*refs, rows):
    (mm_y0, mm_y1, mm_z0, mm_z1, ms_y0, ms_y1, ms_z0, ms_z1, lam_y0, lam_y1, lam_z0, lam_z1,
     ph_y0, ph_y1, ph_z0, ph_z1, lb_y0, lb_y1, lb_z0, lb_z1,
     y_first_ref, y_last_ref, z_first_ref, z_last_ref) = refs

    @pl.when(pl.program_id(0) == 0)
    def _():
        for out_ref, m1, m2, lam, ph, lb in ((y_first_ref, mm_y0, ms_y0, lam_y0, ph_y0, lb_y0),
                                           (y_last_ref, mm_y1, ms_y1, lam_y1, ph_y1, lb_y1)):
            (w_real, w_imag), _ = first_w(lam[0, 0], lam[1, 0], lb[0], ph[0])
            planes = [m1[0, 0], m1[1, 0], m2[0, 0], m2[1, 0], w_real, w_imag]
            for c, value in enumerate(planes):
                out_ref[c] = value

    for r in range(rows):
        for out_ref, m1, m2, lam, ph, lb, at in ((z_first_ref, mm_z0, ms_z0, lam_z0, ph_z0, lb_z0, 0),
                                               (z_last_ref, mm_z1, ms_z1, lam_z1, ph_z1, lb_z1, 7)):
            (w_real, w_imag), _ = first_w(lam[0, r], lam[1, r], lb[r], ph[r])
            tiles = [m1[0, r], m1[1, r], m2[0, r], m2[1, r], w_real, w_imag]
            for c, value in enumerate(tiles):
                out_ref[c, r] = value[at:at + 1]


def edge_specs_of(ndim, length_y, length_z, length_x, rows):
    lead = (2,) if ndim == 4 else ()
    zero = (0,) * len(lead)
    tiles = length_z // 8
    return [
        pl.BlockSpec(lead + (1, length_z, length_x), lambda i: zero + (0, 0, 0)),
        pl.BlockSpec(lead + (1, length_z, length_x), lambda i: zero + (length_y - 1, 0, 0)),
        pl.BlockSpec(lead + (rows, 8, length_x), lambda i: zero + (i, 0, 0)),
        pl.BlockSpec(lead + (rows, 8, length_x), lambda i: zero + (i, tiles - 1, 0)),
    ]


def edge_outputs(comps, length_y, length_z, length_x, rows):
    plane = jax.ShapeDtypeStruct((comps, length_z, length_x), jnp.float32)
    row = jax.ShapeDtypeStruct((comps, length_y, 1, length_x), jnp.float32)
    plane_spec = pl.BlockSpec((comps, length_z, length_x), lambda i: (0, 0, 0))
    row_spec = pl.BlockSpec((comps, rows, 1, length_x), lambda i: (0, i, 0, 0))
    return [plane, plane, row, row], [plane_spec, plane_spec, row_spec, row_spec]


def first_kernel(*refs, rows):
    (mm_ref, mm_prev, mm_next, ms_ref, ms_prev, ms_next, w_ref, w_prev, w_next,
     factor_ref, y_low_ref, y_high_ref, z_low_ref, z_high_ref, pg_ref, w2_ref) = refs[:16]
    step = pl.program_id(0)
    fields = ((mm_ref, mm_prev, mm_next), (ms_ref, ms_prev, ms_next), (w_ref, w_prev, w_next))
    for r in range(rows):
        new = []
        for f, (cur, prev, nxt) in enumerate(fields):
            pair = []
            for comp in range(2):
                below, above = neighbour_planes(cur, prev, nxt, y_low_ref, y_high_ref, rows, 2 * f + comp, comp, r)
                pair.append(plane_update(cur[comp, r], below, above,
                                         z_low_ref[2 * f + comp, r], z_high_ref[2 * f + comp, r]))
            new.append(pair)
        (u1_real, u1_imag), (u2_real, u2_imag), (lam_real, lam_imag) = new
        w_real = w_ref[0, r]
        w_imag = w_ref[1, r]
        f_real = factor_ref[0, r]
        f_imag = factor_ref[1, r]
        w2_real = f_real * lam_real - f_imag * lam_imag
        w2_imag = f_real * lam_imag + f_imag * lam_real
        grad = w_real * u1_imag - w_imag * u1_real
        pg_ref[r] = grad + (w2_real * u2_imag - w2_imag * u2_real)
        w2_ref[0, r] = w2_real
        w2_ref[1, r] = w2_imag
        write_edges(step, rows, r, [w2_real, w2_imag], *refs[16:])


def second_kernel(w_ref, w_prev, w_next, y_low_ref, y_high_ref, z_low_ref, z_high_ref, out_ref, *, rows):
    for r in range(rows):
        for comp in range(2):
            below, above = neighbour_planes(w_ref, w_prev, w_next, y_low_ref, y_high_ref, rows, comp, comp, r)
            out_ref[comp, r] = plane_update(w_ref[comp, r], below, above,
                                            z_low_ref[comp, r], z_high_ref[comp, r])


def block_rows(length_y):
    rows = 4
    while length_y % rows:
        rows //= 2
    return rows


def field_specs(shape, rows):
    comps, length_y, length_z, length_x = shape
    cur = pl.BlockSpec((comps, rows, length_z, length_x), lambda i: (0, i, 0, 0))
    prev = pl.BlockSpec((comps, 1, length_z, length_x),
                        lambda i: (0, jnp.maximum(i * rows - 1, 0), 0, 0))
    nxt = pl.BlockSpec((comps, 1, length_z, length_x),
                       lambda i: (0, jnp.minimum(i * rows + rows, length_y - 1), 0, 0))
    return [cur, prev, nxt]


def send_edges(y_first, y_last, z_first, z_last):
    results = []
    for axis, first, last in (("gy", y_first, y_last), ("gz", z_first, z_last)):
        count = lax.axis_size(axis)
        up = [(i, (i + 1) % count) for i in range(count)]
        down = [(j, i) for i, j in up]
        if count == 2:
            both = lax.ppermute(jnp.stack([last, first]), axis, up)
            results.extend([both[0], both[1]])
        else:
            results.extend([lax.ppermute(last, axis, up), lax.ppermute(first, axis, down)])
    return results


def backward_sections(mag_start, mag_middle, adjoint_end, phase, labels):
    _, length_y, length_z, length_x = mag_start.shape
    rows = block_rows(length_y)
    grid = (length_y // rows,)
    plane = jax.ShapeDtypeStruct((length_y, length_z, length_x), jnp.float32)
    pair = jax.ShapeDtypeStruct((2, length_y, length_z, length_x), jnp.float32)
    cur = pl.BlockSpec((2, rows, length_z, length_x), lambda i: (0, i, 0, 0))
    cur_plane = pl.BlockSpec((rows, length_z, length_x), lambda i: (i, 0, 0))
    whole = lambda shape: pl.BlockSpec(shape, lambda i: (0,) * len(shape))
    zspec = lambda comps: pl.BlockSpec((comps, rows, 1, length_x), lambda i: (0, i, 0, 0))
    edge_shapes, edge_specs = edge_outputs(2, length_y, length_z, length_x, rows)
    six_shapes, six_specs = edge_outputs(6, length_y, length_z, length_x, rows)
    inputs = (mag_middle, mag_start, adjoint_end, phase, labels)
    edges = pl.pallas_call(
        functools.partial(edges_kernel, rows=rows),
        grid=grid,
        in_specs=[s for a in inputs for s in edge_specs_of(a.ndim, length_y, length_z, length_x, rows)],
        out_specs=six_specs,
        out_shape=six_shapes,
    )(*[a for a in inputs for _ in range(4)])
    halos = send_edges(*edges)
    factor, w_first = pl.pallas_call(
        functools.partial(factor_kernel, rows=rows),
        grid=grid,
        in_specs=[cur, cur_plane, cur_plane],
        out_specs=[cur, cur],
        out_shape=[pair, pair],
    )(adjoint_end, phase, labels)
    phase_grad, w_second, *w2_edges = pl.pallas_call(
        functools.partial(first_kernel, rows=rows),
        grid=grid,
        in_specs=field_specs(mag_middle.shape, rows) + field_specs(mag_start.shape, rows)
        + field_specs(w_first.shape, rows)
        + [cur, whole((6, length_z, length_x)), whole((6, length_z, length_x)), zspec(6), zspec(6)],
        out_specs=[cur_plane, cur] + edge_specs,
        out_shape=[plane, pair] + edge_shapes,
    )(mag_middle, mag_middle, mag_middle, mag_start, mag_start, mag_start,
      w_first, w_first, w_first, factor, *halos)
    halos = send_edges(*w2_edges)
    lam = pl.pallas_call(
        functools.partial(second_kernel, rows=rows),
        grid=grid,
        in_specs=field_specs(w_second.shape, rows)
        + [whole((2, length_z, length_x)), whole((2, length_z, length_x)), zspec(2), zspec(2)],
        out_specs=cur,
        out_shape=pair,
    )(w_second, w_second, w_second, *halos)
    return (lam, phase_grad)


def dipole_adjoint(phase_grad):
    count_y = lax.axis_size("gy")
    count_z = lax.axis_size("gz")
    parts = count_y * count_z
    block_y, block_z, length_x = phase_grad.shape
    length_y = block_y * count_y
    length_z = block_z * count_z
    block_x = length_x // parts
    table_x = cas_table(length_x)
    table_y = cas_table(length_y)
    table_z = cas_table(length_z)
    scale = 1.0 / (float(length_y) * float(length_z) * float(length_x))
    spec = along("kn,yzn->kyz", table_x, phase_grad)
    spec = spec.reshape(parts, block_x, block_y, block_z)
    spec = lax.all_to_all(spec, ("gy", "gz"), 0, 0, tiled=True)
    spec = spec.reshape(count_y, count_z, block_x, block_y, block_z)
    spec = spec.transpose(2, 0, 3, 1, 4).reshape(block_x, length_y, length_z)
    spec = along("kz,xyz->xyk", table_z, spec)
    spec = along("ky,xyz->xkz", table_y, spec)
    freq_y = signed_freq(jnp.arange(length_y, dtype=jnp.int32), length_y)
    freq_z = signed_freq(jnp.arange(length_z, dtype=jnp.int32), length_z)
    index = lax.axis_index("gy") * count_z + lax.axis_index("gz")
    freq_x = signed_freq(index * block_x + jnp.arange(block_x, dtype=jnp.int32), length_x)
    kernel = dipole_block(freq_y[None, :, None], freq_z[None, None, :], freq_x[:, None, None])
    spec = spec * kernel
    spec = along("ky,xyz->xkz", table_y, spec)
    spec = along("kz,xyz->xyk", table_z, spec)
    spec = spec.reshape(block_x, count_y, block_y, count_z, block_z)
    spec = spec.transpose(1, 3, 0, 2, 4).reshape(parts, block_x, block_y, block_z)
    spec = lax.all_to_all(spec, ("gy", "gz"), 0, 0, tiled=True)
    spec = spec.reshape(length_x, block_y, block_z)
    return along("kn,nyz->yzk", table_x, spec) * scale


def per_device(mag_start, mag_middle, adjoint_end, phase, labels):
    lam, phase_grad = backward_sections(mag_start, mag_middle, adjoint_end, phase, labels)
    chi_grad = dipole_adjoint(phase_grad)
    return (lam, chi_grad)


def solution(mesh):
    return jax.shard_map(
        per_device,
        mesh=mesh,
        in_specs=(
            P(None, "gy", "gz", None),
            P(None, "gy", "gz", None),
            P(None, "gy", "gz", None),
            P("gy", "gz", None),
            P("gy", "gz", None),
        ),
        out_specs=(P(None, "gy", "gz", None), P("gy", "gz", None)),
        check_vma=False,
    )
```

```python
import functools
import math

import jax
import jax.numpy as jnp
from jax import lax
from jax.experimental import pallas as pl
from jax.experimental.pallas import tpu as pltpu
from jax.sharding import PartitionSpec as P


def signed_freq(index, length):
    return jnp.where(index < length // 2, index, index - length)


def dipole_block(freq_y, freq_z, freq_x):
    square_z = freq_z * freq_z
    total = freq_y * freq_y + square_z + freq_x * freq_x
    ratio = square_z.astype(jnp.float32) / jnp.maximum(total, 1).astype(jnp.float32)
    return jnp.where(total == 0, jnp.float32(0.0), jnp.float32(1.0 / 3.0) - ratio)


def cas_table(length):
    index = jnp.arange(length, dtype=jnp.int32)
    product = index[:, None] * index[None, :] % length
    angle = product.astype(jnp.float32) * (2.0 * math.pi / length)
    return jnp.cos(angle) + jnp.sin(angle)


def along(spec, table, values):
    return jnp.einsum(spec, table, values, precision=lax.Precision.HIGH)


def plane_update(centre, below, above, z_low, z_high):
    length_z, length_x = centre.shape
    row = lax.broadcasted_iota(jnp.int32, centre.shape, 0)
    up = jnp.where(row == 0, z_low, pltpu.roll(centre, 1, 0))
    down = jnp.where(row == length_z - 1, z_high, pltpu.roll(centre, length_z - 1, 0))
    total = below + above + up + down
    total = total + pltpu.roll(centre, 1, 1) + pltpu.roll(centre, length_x - 1, 1)
    return centre + 0.15 * (total - 6.0 * centre)


def neighbour_planes(cur_ref, prev_ref, next_ref, y_low_ref, y_high_ref, rows, field, comp, r):
    step = pl.program_id(0)
    last = pl.num_programs(0) - 1
    if r == 0:
        below = jnp.where(step == 0, y_low_ref[field], prev_ref[comp, 0])
    else:
        below = cur_ref[comp, r - 1]
    if r == rows - 1:
        above = jnp.where(step == last, y_high_ref[field], next_ref[comp, 0])
    else:
        above = cur_ref[comp, r + 1]
    return below, above


def write_edges(step, rows, r, values, y_first_ref, y_last_ref, z_first_ref, z_last_ref):
    for c, value in enumerate(values):
        z_first_ref[c, r] = value[0:1]
        z_last_ref[c, r] = value[value.shape[0] - 1:]
    if r == 0:
        @pl.when(step == 0)
        def _():
            for c, value in enumerate(values):
                y_first_ref[c] = value
    if r == rows - 1:
        @pl.when(step == pl.num_programs(0) - 1)
        def _():
            for c, value in enumerate(values):
                y_last_ref[c] = value


def step_factor(labels, phase):
    rate = jnp.where(labels == 1, 0.3, 0.02)
    rate = jnp.where(labels == 2, 0.6, rate)
    rate = jnp.where(labels == 3, 1.2, rate).astype(jnp.float32)
    decay = jnp.exp(-rate)
    return decay * jnp.cos(phase), decay * jnp.sin(phase)


def first_w(lam_real, lam_imag, labels, phase):
    f_real, f_imag = step_factor(labels, phase)
    return (f_real * lam_real - f_imag * lam_imag, f_real * lam_imag + f_imag * lam_real), (f_real, f_imag)


def factor_kernel(lam_ref, phase_ref, labels_ref, factor_ref, w_ref, *, rows):
    for r in range(rows):
        (w_real, w_imag), (f_real, f_imag) = first_w(lam_ref[0, r], lam_ref[1, r], labels_ref[r], phase_ref[r])
        factor_ref[0, r] = f_real
        factor_ref[1, r] = f_imag
        w_ref[0, r] = w_real
        w_ref[1, r] = w_imag


def edges_kernel(*refs, rows):
    (mm_y0, mm_y1, mm_z0, mm_z1, ms_y0, ms_y1, ms_z0, ms_z1, lam_y0, lam_y1, lam_z0, lam_z1,
     ph_y0, ph_y1, ph_z0, ph_z1, lb_y0, lb_y1, lb_z0, lb_z1,
     y_first_ref, y_last_ref, z_first_ref, z_last_ref) = refs

    @pl.when(pl.program_id(0) == 0)
    def _():
        for out_ref, m1, m2, lam, ph, lb in ((y_first_ref, mm_y0, ms_y0, lam_y0, ph_y0, lb_y0),
                                           (y_last_ref, mm_y1, ms_y1, lam_y1, ph_y1, lb_y1)):
            (w_real, w_imag), _ = first_w(lam[0, 0], lam[1, 0], lb[0], ph[0])
            planes = [m1[0, 0], m1[1, 0], m2[0, 0], m2[1, 0], w_real, w_imag]
            for c, value in enumerate(planes):
                out_ref[c] = value

    for r in range(rows):
        for out_ref, m1, m2, lam, ph, lb, at in ((z_first_ref, mm_z0, ms_z0, lam_z0, ph_z0, lb_z0, 0),
                                               (z_last_ref, mm_z1, ms_z1, lam_z1, ph_z1, lb_z1, 7)):
            (w_real, w_imag), _ = first_w(lam[0, r], lam[1, r], lb[r], ph[r])
            tiles = [m1[0, r], m1[1, r], m2[0, r], m2[1, r], w_real, w_imag]
            for c, value in enumerate(tiles):
                out_ref[c, r] = value[at:at + 1]


def edge_specs_of(ndim, length_y, length_z, length_x, rows):
    lead = (2,) if ndim == 4 else ()
    zero = (0,) * len(lead)
    tiles = length_z // 8
    return [
        pl.BlockSpec(lead + (1, length_z, length_x), lambda i: zero + (0, 0, 0)),
        pl.BlockSpec(lead + (1, length_z, length_x), lambda i: zero + (length_y - 1, 0, 0)),
        pl.BlockSpec(lead + (rows, 8, length_x), lambda i: zero + (i, 0, 0)),
        pl.BlockSpec(lead + (rows, 8, length_x), lambda i: zero + (i, tiles - 1, 0)),
    ]


def edge_outputs(comps, length_y, length_z, length_x, rows):
    plane = jax.ShapeDtypeStruct((comps, length_z, length_x), jnp.float32)
    row = jax.ShapeDtypeStruct((comps, length_y, 1, length_x), jnp.float32)
    plane_spec = pl.BlockSpec((comps, length_z, length_x), lambda i: (0, 0, 0))
    row_spec = pl.BlockSpec((comps, rows, 1, length_x), lambda i: (0, i, 0, 0))
    return [plane, plane, row, row], [plane_spec, plane_spec, row_spec, row_spec]


def first_kernel(*refs, rows):
    (mm_ref, mm_prev, mm_next, ms_ref, ms_prev, ms_next, w_ref, w_prev, w_next,
     factor_ref, y_low_ref, y_high_ref, z_low_ref, z_high_ref, pg_ref, w2_ref) = refs[:16]
    step = pl.program_id(0)
    fields = ((mm_ref, mm_prev, mm_next), (ms_ref, ms_prev, ms_next), (w_ref, w_prev, w_next))
    for r in range(rows):
        new = []
        for f, (cur, prev, nxt) in enumerate(fields):
            pair = []
            for comp in range(2):
                below, above = neighbour_planes(cur, prev, nxt, y_low_ref, y_high_ref, rows, 2 * f + comp, comp, r)
                pair.append(plane_update(cur[comp, r], below, above,
                                         z_low_ref[2 * f + comp, r], z_high_ref[2 * f + comp, r]))
            new.append(pair)
        (u1_real, u1_imag), (u2_real, u2_imag), (lam_real, lam_imag) = new
        w_real = w_ref[0, r]
        w_imag = w_ref[1, r]
        f_real = factor_ref[0, r]
        f_imag = factor_ref[1, r]
        w2_real = f_real * lam_real - f_imag * lam_imag
        w2_imag = f_real * lam_imag + f_imag * lam_real
        grad = w_real * u1_imag - w_imag * u1_real
        pg_ref[r] = grad + (w2_real * u2_imag - w2_imag * u2_real)
        w2_ref[0, r] = w2_real
        w2_ref[1, r] = w2_imag
        write_edges(step, rows, r, [w2_real, w2_imag], *refs[16:])


def second_kernel(w_ref, w_prev, w_next, y_low_ref, y_high_ref, z_low_ref, z_high_ref, out_ref, *, rows):
    for r in range(rows):
        for comp in range(2):
            below, above = neighbour_planes(w_ref, w_prev, w_next, y_low_ref, y_high_ref, rows, comp, comp, r)
            out_ref[comp, r] = plane_update(w_ref[comp, r], below, above,
                                            z_low_ref[comp, r], z_high_ref[comp, r])


def block_rows(length_y):
    rows = 8
    while length_y % rows:
        rows //= 2
    return rows


def field_specs(shape, rows):
    comps, length_y, length_z, length_x = shape
    cur = pl.BlockSpec((comps, rows, length_z, length_x), lambda i: (0, i, 0, 0))
    prev = pl.BlockSpec((comps, 1, length_z, length_x),
                        lambda i: (0, jnp.maximum(i * rows - 1, 0), 0, 0))
    nxt = pl.BlockSpec((comps, 1, length_z, length_x),
                       lambda i: (0, jnp.minimum(i * rows + rows, length_y - 1), 0, 0))
    return [cur, prev, nxt]


def send_edges(y_first, y_last, z_first, z_last):
    results = []
    for axis, first, last in (("gy", y_first, y_last), ("gz", z_first, z_last)):
        count = lax.axis_size(axis)
        up = [(i, (i + 1) % count) for i in range(count)]
        down = [(j, i) for i, j in up]
        if count == 2:
            both = lax.ppermute(jnp.stack([last, first]), axis, up)
            results.extend([both[0], both[1]])
        else:
            results.extend([lax.ppermute(last, axis, up), lax.ppermute(first, axis, down)])
    return results


def backward_sections(mag_start, mag_middle, adjoint_end, phase, labels):
    _, length_y, length_z, length_x = mag_start.shape
    rows = block_rows(length_y)
    grid = (length_y // rows,)
    plane = jax.ShapeDtypeStruct((length_y, length_z, length_x), jnp.float32)
    pair = jax.ShapeDtypeStruct((2, length_y, length_z, length_x), jnp.float32)
    cur = pl.BlockSpec((2, rows, length_z, length_x), lambda i: (0, i, 0, 0))
    cur_plane = pl.BlockSpec((rows, length_z, length_x), lambda i: (i, 0, 0))
    whole = lambda shape: pl.BlockSpec(shape, lambda i: (0,) * len(shape))
    zspec = lambda comps: pl.BlockSpec((comps, rows, 1, length_x), lambda i: (0, i, 0, 0))
    edge_shapes, edge_specs = edge_outputs(2, length_y, length_z, length_x, rows)
    six_shapes, six_specs = edge_outputs(6, length_y, length_z, length_x, rows)
    inputs = (mag_middle, mag_start, adjoint_end, phase, labels)
    edges = pl.pallas_call(
        functools.partial(edges_kernel, rows=rows),
        grid=grid,
        in_specs=[s for a in inputs for s in edge_specs_of(a.ndim, length_y, length_z, length_x, rows)],
        out_specs=six_specs,
        out_shape=six_shapes,
    )(*[a for a in inputs for _ in range(4)])
    halos = send_edges(*edges)
    factor, w_first = pl.pallas_call(
        functools.partial(factor_kernel, rows=rows),
        grid=grid,
        in_specs=[cur, cur_plane, cur_plane],
        out_specs=[cur, cur],
        out_shape=[pair, pair],
    )(adjoint_end, phase, labels)
    phase_grad, w_second, *w2_edges = pl.pallas_call(
        functools.partial(first_kernel, rows=rows),
        grid=grid,
        in_specs=field_specs(mag_middle.shape, rows) + field_specs(mag_start.shape, rows)
        + field_specs(w_first.shape, rows)
        + [cur, whole((6, length_z, length_x)), whole((6, length_z, length_x)), zspec(6), zspec(6)],
        out_specs=[cur_plane, cur] + edge_specs,
        out_shape=[plane, pair] + edge_shapes,
    )(mag_middle, mag_middle, mag_middle, mag_start, mag_start, mag_start,
      w_first, w_first, w_first, factor, *halos)
    halos = send_edges(*w2_edges)
    lam = pl.pallas_call(
        functools.partial(second_kernel, rows=rows),
        grid=grid,
        in_specs=field_specs(w_second.shape, rows)
        + [whole((2, length_z, length_x)), whole((2, length_z, length_x)), zspec(2), zspec(2)],
        out_specs=cur,
        out_shape=pair,
    )(w_second, w_second, w_second, *halos)
    return (lam, phase_grad)


def dipole_adjoint(phase_grad):
    count_y = lax.axis_size("gy")
    count_z = lax.axis_size("gz")
    parts = count_y * count_z
    block_y, block_z, length_x = phase_grad.shape
    length_y = block_y * count_y
    length_z = block_z * count_z
    block_x = length_x // parts
    table_x = cas_table(length_x)
    table_y = cas_table(length_y)
    table_z = cas_table(length_z)
    scale = 1.0 / (float(length_y) * float(length_z) * float(length_x))
    spec = along("kn,yzn->kyz", table_x, phase_grad)
    spec = spec.reshape(parts, block_x, block_y, block_z)
    spec = lax.all_to_all(spec, ("gy", "gz"), 0, 0, tiled=True)
    spec = spec.reshape(count_y, count_z, block_x, block_y, block_z)
    spec = spec.transpose(2, 0, 3, 1, 4).reshape(block_x, length_y, length_z)
    spec = along("kz,xyz->xyk", table_z, spec)
    spec = along("ky,xyz->xkz", table_y, spec)
    freq_y = signed_freq(jnp.arange(length_y, dtype=jnp.int32), length_y)
    freq_z = signed_freq(jnp.arange(length_z, dtype=jnp.int32), length_z)
    index = lax.axis_index("gy") * count_z + lax.axis_index("gz")
    freq_x = signed_freq(index * block_x + jnp.arange(block_x, dtype=jnp.int32), length_x)
    kernel = dipole_block(freq_y[None, :, None], freq_z[None, None, :], freq_x[:, None, None])
    spec = spec * kernel
    spec = along("ky,xyz->xkz", table_y, spec)
    spec = along("kz,xyz->xyk", table_z, spec)
    spec = spec.reshape(block_x, count_y, block_y, count_z, block_z)
    spec = spec.transpose(1, 3, 0, 2, 4).reshape(parts, block_x, block_y, block_z)
    spec = lax.all_to_all(spec, ("gy", "gz"), 0, 0, tiled=True)
    spec = spec.reshape(length_x, block_y, block_z)
    return along("kn,nyz->yzk", table_x, spec) * scale


def per_device(mag_start, mag_middle, adjoint_end, phase, labels):
    lam, phase_grad = backward_sections(mag_start, mag_middle, adjoint_end, phase, labels)
    chi_grad = dipole_adjoint(phase_grad)
    return (lam, chi_grad)


def solution(mesh):
    return jax.shard_map(
        per_device,
        mesh=mesh,
        in_specs=(
            P(None, "gy", "gz", None),
            P(None, "gy", "gz", None),
            P(None, "gy", "gz", None),
            P("gy", "gz", None),
            P("gy", "gz", None),
        ),
        out_specs=(P(None, "gy", "gz", None), P("gy", "gz", None)),
        check_vma=False,
    )
```

```python
import functools
import math

import jax
import jax.numpy as jnp
from jax import lax
from jax.experimental import pallas as pl
from jax.experimental.pallas import tpu as pltpu
from jax.sharding import PartitionSpec as P


def signed_freq(index, length):
    return jnp.where(index < length // 2, index, index - length)


def dipole_block(freq_y, freq_z, freq_x):
    square_z = freq_z * freq_z
    total = freq_y * freq_y + square_z + freq_x * freq_x
    ratio = square_z.astype(jnp.float32) / jnp.maximum(total, 1).astype(jnp.float32)
    return jnp.where(total == 0, jnp.float32(0.0), jnp.float32(1.0 / 3.0) - ratio)


def cas_table(length):
    index = jnp.arange(length, dtype=jnp.int32)
    product = index[:, None] * index[None, :] % length
    angle = product.astype(jnp.float32) * (2.0 * math.pi / length)
    return jnp.cos(angle) + jnp.sin(angle)


def along(spec, table, values):
    return jnp.einsum(spec, table, values, precision=lax.Precision.HIGH)


def plane_update(centre, below, above, z_low, z_high):
    length_z, length_x = centre.shape
    row = lax.broadcasted_iota(jnp.int32, centre.shape, 0)
    up = jnp.where(row == 0, z_low, pltpu.roll(centre, 1, 0))
    down = jnp.where(row == length_z - 1, z_high, pltpu.roll(centre, length_z - 1, 0))
    total = below + above + up + down
    total = total + pltpu.roll(centre, 1, 1) + pltpu.roll(centre, length_x - 1, 1)
    return centre + 0.15 * (total - 6.0 * centre)


def neighbour_planes(cur_ref, prev_ref, next_ref, y_low_ref, y_high_ref, rows, field, comp, r):
    step = pl.program_id(0)
    last = pl.num_programs(0) - 1
    if r == 0:
        below = jnp.where(step == 0, y_low_ref[field], prev_ref[comp, 0])
    else:
        below = cur_ref[comp, r - 1]
    if r == rows - 1:
        above = jnp.where(step == last, y_high_ref[field], next_ref[comp, 0])
    else:
        above = cur_ref[comp, r + 1]
    return below, above


def write_edges(step, rows, r, values, y_first_ref, y_last_ref, z_first_ref, z_last_ref):
    for c, value in enumerate(values):
        z_first_ref[c, r] = value[0:1]
        z_last_ref[c, r] = value[value.shape[0] - 1:]
    if r == 0:
        @pl.when(step == 0)
        def _():
            for c, value in enumerate(values):
                y_first_ref[c] = value
    if r == rows - 1:
        @pl.when(step == pl.num_programs(0) - 1)
        def _():
            for c, value in enumerate(values):
                y_last_ref[c] = value


def step_factor(labels, phase):
    rate = jnp.where(labels == 1, 0.3, 0.02)
    rate = jnp.where(labels == 2, 0.6, rate)
    rate = jnp.where(labels == 3, 1.2, rate).astype(jnp.float32)
    decay = jnp.exp(-rate)
    return decay * jnp.cos(phase), decay * jnp.sin(phase)


def first_w(lam_real, lam_imag, labels, phase):
    f_real, f_imag = step_factor(labels, phase)
    return (f_real * lam_real - f_imag * lam_imag, f_real * lam_imag + f_imag * lam_real), (f_real, f_imag)


def factor_kernel(lam_ref, phase_ref, labels_ref, factor_ref, w_ref, *, rows):
    for r in range(rows):
        (w_real, w_imag), (f_real, f_imag) = first_w(lam_ref[0, r], lam_ref[1, r], labels_ref[r], phase_ref[r])
        factor_ref[0, r] = f_real
        factor_ref[1, r] = f_imag
        w_ref[0, r] = w_real
        w_ref[1, r] = w_imag


def edges_kernel(*refs, rows):
    (mm_y0, mm_y1, mm_z0, mm_z1, ms_y0, ms_y1, ms_z0, ms_z1, lam_y0, lam_y1, lam_z0, lam_z1,
     ph_y0, ph_y1, ph_z0, ph_z1, lb_y0, lb_y1, lb_z0, lb_z1,
     y_first_ref, y_last_ref, z_first_ref, z_last_ref) = refs

    @pl.when(pl.program_id(0) == 0)
    def _():
        for out_ref, m1, m2, lam, ph, lb in ((y_first_ref, mm_y0, ms_y0, lam_y0, ph_y0, lb_y0),
                                           (y_last_ref, mm_y1, ms_y1, lam_y1, ph_y1, lb_y1)):
            (w_real, w_imag), _ = first_w(lam[0, 0], lam[1, 0], lb[0], ph[0])
            planes = [m1[0, 0], m1[1, 0], m2[0, 0], m2[1, 0], w_real, w_imag]
            for c, value in enumerate(planes):
                out_ref[c] = value

    for r in range(rows):
        for out_ref, m1, m2, lam, ph, lb, at in ((z_first_ref, mm_z0, ms_z0, lam_z0, ph_z0, lb_z0, 0),
                                               (z_last_ref, mm_z1, ms_z1, lam_z1, ph_z1, lb_z1, 7)):
            (w_real, w_imag), _ = first_w(lam[0, r], lam[1, r], lb[r], ph[r])
            tiles = [m1[0, r], m1[1, r], m2[0, r], m2[1, r], w_real, w_imag]
            for c, value in enumerate(tiles):
                out_ref[c, r] = value[at:at + 1]


def edge_specs_of(ndim, length_y, length_z, length_x, rows):
    lead = (2,) if ndim == 4 else ()
    zero = (0,) * len(lead)
    tiles = length_z // 8
    return [
        pl.BlockSpec(lead + (1, length_z, length_x), lambda i: zero + (0, 0, 0)),
        pl.BlockSpec(lead + (1, length_z, length_x), lambda i: zero + (length_y - 1, 0, 0)),
        pl.BlockSpec(lead + (rows, 8, length_x), lambda i: zero + (i, 0, 0)),
        pl.BlockSpec(lead + (rows, 8, length_x), lambda i: zero + (i, tiles - 1, 0)),
    ]


def edge_outputs(comps, length_y, length_z, length_x, rows):
    plane = jax.ShapeDtypeStruct((comps, length_z, length_x), jnp.float32)
    row = jax.ShapeDtypeStruct((comps, length_y, 1, length_x), jnp.float32)
    plane_spec = pl.BlockSpec((comps, length_z, length_x), lambda i: (0, 0, 0))
    row_spec = pl.BlockSpec((comps, rows, 1, length_x), lambda i: (0, i, 0, 0))
    return [plane, plane, row, row], [plane_spec, plane_spec, row_spec, row_spec]


def first_kernel(*refs, rows):
    (mm_ref, mm_prev, mm_next, ms_ref, ms_prev, ms_next, w_ref, w_prev, w_next,
     factor_ref, y_low_ref, y_high_ref, z_low_ref, z_high_ref, pg_ref, w2_ref) = refs[:16]
    step = pl.program_id(0)
    fields = ((mm_ref, mm_prev, mm_next), (ms_ref, ms_prev, ms_next), (w_ref, w_prev, w_next))
    for r in range(rows):
        new = []
        for f, (cur, prev, nxt) in enumerate(fields):
            pair = []
            for comp in range(2):
                below, above = neighbour_planes(cur, prev, nxt, y_low_ref, y_high_ref, rows, 2 * f + comp, comp, r)
                pair.append(plane_update(cur[comp, r], below, above,
                                         z_low_ref[2 * f + comp, r], z_high_ref[2 * f + comp, r]))
            new.append(pair)
        (u1_real, u1_imag), (u2_real, u2_imag), (lam_real, lam_imag) = new
        w_real = w_ref[0, r]
        w_imag = w_ref[1, r]
        f_real = factor_ref[0, r]
        f_imag = factor_ref[1, r]
        w2_real = f_real * lam_real - f_imag * lam_imag
        w2_imag = f_real * lam_imag + f_imag * lam_real
        grad = w_real * u1_imag - w_imag * u1_real
        pg_ref[r] = grad + (w2_real * u2_imag - w2_imag * u2_real)
        w2_ref[0, r] = w2_real
        w2_ref[1, r] = w2_imag
        write_edges(step, rows, r, [w2_real, w2_imag], *refs[16:])


def second_kernel(w_ref, w_prev, w_next, y_low_ref, y_high_ref, z_low_ref, z_high_ref, out_ref, *, rows):
    for r in range(rows):
        for comp in range(2):
            below, above = neighbour_planes(w_ref, w_prev, w_next, y_low_ref, y_high_ref, rows, comp, comp, r)
            out_ref[comp, r] = plane_update(w_ref[comp, r], below, above,
                                            z_low_ref[comp, r], z_high_ref[comp, r])


def block_rows(length_y):
    rows = 8
    while length_y % rows:
        rows //= 2
    return rows


def field_specs(shape, rows):
    comps, length_y, length_z, length_x = shape
    cur = pl.BlockSpec((comps, rows, length_z, length_x), lambda i: (0, i, 0, 0))
    prev = pl.BlockSpec((comps, 1, length_z, length_x),
                        lambda i: (0, jnp.maximum(i * rows - 1, 0), 0, 0))
    nxt = pl.BlockSpec((comps, 1, length_z, length_x),
                       lambda i: (0, jnp.minimum(i * rows + rows, length_y - 1), 0, 0))
    return [cur, prev, nxt]


def send_edges(y_first, y_last, z_first, z_last):
    results = []
    for axis, first, last in (("gy", y_first, y_last), ("gz", z_first, z_last)):
        count = lax.axis_size(axis)
        up = [(i, (i + 1) % count) for i in range(count)]
        down = [(j, i) for i, j in up]
        if count == 2:
            both = lax.ppermute(jnp.stack([last, first]), axis, up)
            results.extend([both[0], both[1]])
        else:
            results.extend([lax.ppermute(last, axis, up), lax.ppermute(first, axis, down)])
    return results


def backward_sections(mag_start, mag_middle, adjoint_end, phase, labels):
    _, length_y, length_z, length_x = mag_start.shape
    rows = block_rows(length_y)
    grid = (length_y // rows,)
    plane = jax.ShapeDtypeStruct((length_y, length_z, length_x), jnp.float32)
    pair = jax.ShapeDtypeStruct((2, length_y, length_z, length_x), jnp.float32)
    cur = pl.BlockSpec((2, rows, length_z, length_x), lambda i: (0, i, 0, 0))
    cur_plane = pl.BlockSpec((rows, length_z, length_x), lambda i: (i, 0, 0))
    whole = lambda shape: pl.BlockSpec(shape, lambda i: (0,) * len(shape))
    zspec = lambda comps: pl.BlockSpec((comps, rows, 1, length_x), lambda i: (0, i, 0, 0))
    edge_shapes, edge_specs = edge_outputs(2, length_y, length_z, length_x, rows)
    six_shapes, six_specs = edge_outputs(6, length_y, length_z, length_x, rows)
    inputs = (mag_middle, mag_start, adjoint_end, phase, labels)
    edges = pl.pallas_call(
        functools.partial(edges_kernel, rows=rows),
        grid=grid,
        in_specs=[s for a in inputs for s in edge_specs_of(a.ndim, length_y, length_z, length_x, rows)],
        out_specs=six_specs,
        out_shape=six_shapes,
    )(*[a for a in inputs for _ in range(4)])
    halos = send_edges(*edges)
    factor, w_first = pl.pallas_call(
        functools.partial(factor_kernel, rows=rows),
        grid=grid,
        in_specs=[cur, cur_plane, cur_plane],
        out_specs=[cur, cur],
        out_shape=[pair, pair],
    )(adjoint_end, phase, labels)
    phase_grad, w_second, *w2_edges = pl.pallas_call(
        functools.partial(first_kernel, rows=rows),
        grid=grid,
        in_specs=field_specs(mag_middle.shape, rows) + field_specs(mag_start.shape, rows)
        + field_specs(w_first.shape, rows)
        + [cur, whole((6, length_z, length_x)), whole((6, length_z, length_x)), zspec(6), zspec(6)],
        out_specs=[cur_plane, cur] + edge_specs,
        out_shape=[plane, pair] + edge_shapes,
    )(mag_middle, mag_middle, mag_middle, mag_start, mag_start, mag_start,
      w_first, w_first, w_first, factor, *halos)
    halos = send_edges(*w2_edges)
    lam = pl.pallas_call(
        functools.partial(second_kernel, rows=rows),
        grid=grid,
        in_specs=field_specs(w_second.shape, rows)
        + [whole((2, length_z, length_x)), whole((2, length_z, length_x)), zspec(2), zspec(2)],
        out_specs=cur,
        out_shape=pair,
    )(w_second, w_second, w_second, *halos)
    return (lam, phase_grad)


def dipole_adjoint(phase_grad):
    count_y = lax.axis_size("gy")
    count_z = lax.axis_size("gz")
    parts = count_y * count_z
    block_y, block_z, length_x = phase_grad.shape
    length_y = block_y * count_y
    length_z = block_z * count_z
    block_x = length_x // parts
    pieces = 2 if block_x % 2 == 0 else 1
    piece_x = block_x // pieces
    table_x = cas_table(length_x).reshape(parts, pieces, piece_x, length_x)
    table_y = cas_table(length_y)
    table_z = cas_table(length_z)
    scale = 1.0 / (float(length_y) * float(length_z) * float(length_x))
    freq_y = signed_freq(jnp.arange(length_y, dtype=jnp.int32), length_y)
    freq_z = signed_freq(jnp.arange(length_z, dtype=jnp.int32), length_z)
    index = lax.axis_index("gy") * count_z + lax.axis_index("gz")
    sent = []
    for p in range(pieces):
        spec = along("sxn,yzn->sxyz", table_x[:, p], phase_grad)
        sent.append(lax.all_to_all(spec, ("gy", "gz"), 0, 0, tiled=True))
    result = None
    for p in range(pieces):
        spec = sent[p].reshape(count_y, count_z, piece_x, block_y, block_z)
        spec = spec.transpose(2, 0, 3, 1, 4).reshape(piece_x, length_y, length_z)
        spec = along("kz,xyz->xyk", table_z, spec)
        spec = along("ky,xyz->xkz", table_y, spec)
        first_x = index * block_x + p * piece_x
        freq_x = signed_freq(first_x + jnp.arange(piece_x, dtype=jnp.int32), length_x)
        kernel = dipole_block(freq_y[None, :, None], freq_z[None, None, :], freq_x[:, None, None])
        spec = spec * kernel
        spec = along("ky,xyz->xkz", table_y, spec)
        spec = along("kz,xyz->xyk", table_z, spec)
        spec = spec.reshape(piece_x, count_y, block_y, count_z, block_z)
        spec = spec.transpose(1, 3, 0, 2, 4).reshape(parts, piece_x, block_y, block_z)
        spec = lax.all_to_all(spec, ("gy", "gz"), 0, 0, tiled=True)
        part = along("sxn,sxyz->yzn", table_x[:, p], spec)
        result = part if result is None else result + part
    return result * scale


def per_device(mag_start, mag_middle, adjoint_end, phase, labels):
    lam, phase_grad = backward_sections(mag_start, mag_middle, adjoint_end, phase, labels)
    chi_grad = dipole_adjoint(phase_grad)
    return (lam, chi_grad)


def solution(mesh):
    return jax.shard_map(
        per_device,
        mesh=mesh,
        in_specs=(
            P(None, "gy", "gz", None),
            P(None, "gy", "gz", None),
            P(None, "gy", "gz", None),
            P("gy", "gz", None),
            P("gy", "gz", None),
        ),
        out_specs=(P(None, "gy", "gz", None), P("gy", "gz", None)),
        check_vma=False,
    )
```

```python
import functools
import math

import jax
import jax.numpy as jnp
from jax import lax
from jax.experimental import pallas as pl
from jax.experimental.pallas import tpu as pltpu
from jax.sharding import PartitionSpec as P


def signed_freq(index, length):
    return jnp.where(index < length // 2, index, index - length)


def dipole_block(freq_y, freq_z, freq_x):
    square_z = freq_z * freq_z
    total = freq_y * freq_y + square_z + freq_x * freq_x
    ratio = square_z.astype(jnp.float32) / jnp.maximum(total, 1).astype(jnp.float32)
    return jnp.where(total == 0, jnp.float32(0.0), jnp.float32(1.0 / 3.0) - ratio)


def cas_table(length):
    index = jnp.arange(length, dtype=jnp.int32)
    product = index[:, None] * index[None, :] % length
    angle = product.astype(jnp.float32) * (2.0 * math.pi / length)
    return jnp.cos(angle) + jnp.sin(angle)


def along(spec, table, values):
    return jnp.einsum(spec, table, values, precision=lax.Precision.HIGH)


def plane_update(centre, below, above, z_low, z_high):
    length_z, length_x = centre.shape
    row = lax.broadcasted_iota(jnp.int32, centre.shape, 0)
    up = jnp.where(row == 0, z_low, pltpu.roll(centre, 1, 0))
    down = jnp.where(row == length_z - 1, z_high, pltpu.roll(centre, length_z - 1, 0))
    total = below + above + up + down
    total = total + pltpu.roll(centre, 1, 1) + pltpu.roll(centre, length_x - 1, 1)
    return centre + 0.15 * (total - 6.0 * centre)


def neighbour_planes(cur_ref, prev_ref, next_ref, y_low_ref, y_high_ref, rows, field, comp, r, step, last):
    below = cur_ref[comp, jnp.maximum(r - 1, 0)]
    below = jnp.where(r == 0, jnp.where(step == 0, y_low_ref[field], prev_ref[comp, 0]), below)
    above = cur_ref[comp, jnp.minimum(r + 1, rows - 1)]
    above = jnp.where(r == rows - 1, jnp.where(step == last, y_high_ref[field], next_ref[comp, 0]), above)
    return below, above


def write_edges(step, last, rows, r, values, y_first_ref, y_last_ref, z_first_ref, z_last_ref):
    for c, value in enumerate(values):
        z_first_ref[c, r] = value[0:1]
        z_last_ref[c, r] = value[value.shape[0] - 1:]

    @pl.when(jnp.logical_and(r == 0, step == 0))
    def _():
        for c, value in enumerate(values):
            y_first_ref[c] = value

    @pl.when(jnp.logical_and(r == rows - 1, step == last))
    def _():
        for c, value in enumerate(values):
            y_last_ref[c] = value


def for_rows(rows, body):
    def loop_body(r, carry):
        body(r)
        return carry
    lax.fori_loop(0, rows, loop_body, 0)


def step_factor(labels, phase):
    rate = jnp.where(labels == 1, 0.3, 0.02)
    rate = jnp.where(labels == 2, 0.6, rate)
    rate = jnp.where(labels == 3, 1.2, rate).astype(jnp.float32)
    decay = jnp.exp(-rate)
    return decay * jnp.cos(phase), decay * jnp.sin(phase)


def first_w(lam_real, lam_imag, labels, phase):
    f_real, f_imag = step_factor(labels, phase)
    return (f_real * lam_real - f_imag * lam_imag, f_real * lam_imag + f_imag * lam_real), (f_real, f_imag)


def factor_kernel(lam_ref, phase_ref, labels_ref, factor_ref, w_ref, *, rows):
    def body(r, carry):
        (w_real, w_imag), (f_real, f_imag) = first_w(lam_ref[0, r], lam_ref[1, r], labels_ref[r], phase_ref[r])
        factor_ref[0, r] = f_real
        factor_ref[1, r] = f_imag
        w_ref[0, r] = w_real
        w_ref[1, r] = w_imag
        return carry
    lax.fori_loop(0, rows, body, 0)


def edges_kernel(*refs, rows):
    (mm_y0, mm_y1, mm_z0, mm_z1, ms_y0, ms_y1, ms_z0, ms_z1, lam_y0, lam_y1, lam_z0, lam_z1,
     ph_y0, ph_y1, ph_z0, ph_z1, lb_y0, lb_y1, lb_z0, lb_z1,
     y_first_ref, y_last_ref, z_first_ref, z_last_ref) = refs

    @pl.when(pl.program_id(0) == 0)
    def _():
        for out_ref, m1, m2, lam, ph, lb in ((y_first_ref, mm_y0, ms_y0, lam_y0, ph_y0, lb_y0),
                                           (y_last_ref, mm_y1, ms_y1, lam_y1, ph_y1, lb_y1)):
            (w_real, w_imag), _ = first_w(lam[0, 0], lam[1, 0], lb[0], ph[0])
            planes = [m1[0, 0], m1[1, 0], m2[0, 0], m2[1, 0], w_real, w_imag]
            for c, value in enumerate(planes):
                out_ref[c] = value

    def body(r, carry):
        for out_ref, m1, m2, lam, ph, lb, at in ((z_first_ref, mm_z0, ms_z0, lam_z0, ph_z0, lb_z0, 0),
                                               (z_last_ref, mm_z1, ms_z1, lam_z1, ph_z1, lb_z1, 7)):
            (w_real, w_imag), _ = first_w(lam[0, r], lam[1, r], lb[r], ph[r])
            tiles = [m1[0, r], m1[1, r], m2[0, r], m2[1, r], w_real, w_imag]
            for c, value in enumerate(tiles):
                out_ref[c, r] = value[at:at + 1]
        return carry
    lax.fori_loop(0, rows, body, 0)


def edge_specs_of(ndim, length_y, length_z, length_x, rows):
    lead = (2,) if ndim == 4 else ()
    zero = (0,) * len(lead)
    tiles = length_z // 8
    return [
        pl.BlockSpec(lead + (1, length_z, length_x), lambda i: zero + (0, 0, 0)),
        pl.BlockSpec(lead + (1, length_z, length_x), lambda i: zero + (length_y - 1, 0, 0)),
        pl.BlockSpec(lead + (rows, 8, length_x), lambda i: zero + (i, 0, 0)),
        pl.BlockSpec(lead + (rows, 8, length_x), lambda i: zero + (i, tiles - 1, 0)),
    ]


def edge_outputs(comps, length_y, length_z, length_x, rows):
    plane = jax.ShapeDtypeStruct((comps, length_z, length_x), jnp.float32)
    row = jax.ShapeDtypeStruct((comps, length_y, 1, length_x), jnp.float32)
    plane_spec = pl.BlockSpec((comps, length_z, length_x), lambda i: (0, 0, 0))
    row_spec = pl.BlockSpec((comps, rows, 1, length_x), lambda i: (0, i, 0, 0))
    return [plane, plane, row, row], [plane_spec, plane_spec, row_spec, row_spec]


def first_kernel(*refs, rows):
    (mm_ref, mm_prev, mm_next, ms_ref, ms_prev, ms_next, w_ref, w_prev, w_next,
     factor_ref, y_low_ref, y_high_ref, z_low_ref, z_high_ref, pg_ref, w2_ref) = refs[:16]
    step = pl.program_id(0)
    last = pl.num_programs(0) - 1
    fields = ((mm_ref, mm_prev, mm_next), (ms_ref, ms_prev, ms_next), (w_ref, w_prev, w_next))

    def body(r):
        new = []
        for f, (cur, prev, nxt) in enumerate(fields):
            pair = []
            for comp in range(2):
                below, above = neighbour_planes(cur, prev, nxt, y_low_ref, y_high_ref, rows, 2 * f + comp, comp, r,
                                                step, last)
                pair.append(plane_update(cur[comp, r], below, above,
                                         z_low_ref[2 * f + comp, r], z_high_ref[2 * f + comp, r]))
            new.append(pair)
        (u1_real, u1_imag), (u2_real, u2_imag), (lam_real, lam_imag) = new
        w_real = w_ref[0, r]
        w_imag = w_ref[1, r]
        f_real = factor_ref[0, r]
        f_imag = factor_ref[1, r]
        w2_real = f_real * lam_real - f_imag * lam_imag
        w2_imag = f_real * lam_imag + f_imag * lam_real
        grad = w_real * u1_imag - w_imag * u1_real
        pg_ref[r] = grad + (w2_real * u2_imag - w2_imag * u2_real)
        w2_ref[0, r] = w2_real
        w2_ref[1, r] = w2_imag
        write_edges(step, last, rows, r, [w2_real, w2_imag], *refs[16:])

    for_rows(rows, body)


def second_kernel(w_ref, w_prev, w_next, y_low_ref, y_high_ref, z_low_ref, z_high_ref, out_ref, *, rows):
    step = pl.program_id(0)
    last = pl.num_programs(0) - 1

    def body(r):
        for comp in range(2):
            below, above = neighbour_planes(w_ref, w_prev, w_next, y_low_ref, y_high_ref, rows, comp, comp, r,
                                            step, last)
            out_ref[comp, r] = plane_update(w_ref[comp, r], below, above,
                                            z_low_ref[comp, r], z_high_ref[comp, r])

    for_rows(rows, body)


def block_rows(length_y):
    rows = 8
    while length_y % rows:
        rows //= 2
    return rows


def field_specs(shape, rows):
    comps, length_y, length_z, length_x = shape
    cur = pl.BlockSpec((comps, rows, length_z, length_x), lambda i: (0, i, 0, 0))
    prev = pl.BlockSpec((comps, 1, length_z, length_x),
                        lambda i: (0, jnp.maximum(i * rows - 1, 0), 0, 0))
    nxt = pl.BlockSpec((comps, 1, length_z, length_x),
                       lambda i: (0, jnp.minimum(i * rows + rows, length_y - 1), 0, 0))
    return [cur, prev, nxt]


def send_edges(y_first, y_last, z_first, z_last):
    results = []
    for axis, first, last in (("gy", y_first, y_last), ("gz", z_first, z_last)):
        count = lax.axis_size(axis)
        up = [(i, (i + 1) % count) for i in range(count)]
        down = [(j, i) for i, j in up]
        if count == 2:
            both = lax.ppermute(jnp.stack([last, first]), axis, up)
            results.extend([both[0], both[1]])
        else:
            results.extend([lax.ppermute(last, axis, up), lax.ppermute(first, axis, down)])
    return results


def backward_sections(mag_start, mag_middle, adjoint_end, phase, labels):
    _, length_y, length_z, length_x = mag_start.shape
    rows = block_rows(length_y)
    grid = (length_y // rows,)
    plane = jax.ShapeDtypeStruct((length_y, length_z, length_x), jnp.float32)
    pair = jax.ShapeDtypeStruct((2, length_y, length_z, length_x), jnp.float32)
    cur = pl.BlockSpec((2, rows, length_z, length_x), lambda i: (0, i, 0, 0))
    cur_plane = pl.BlockSpec((rows, length_z, length_x), lambda i: (i, 0, 0))
    whole = lambda shape: pl.BlockSpec(shape, lambda i: (0,) * len(shape))
    zspec = lambda comps: pl.BlockSpec((comps, rows, 1, length_x), lambda i: (0, i, 0, 0))
    edge_shapes, edge_specs = edge_outputs(2, length_y, length_z, length_x, rows)
    six_shapes, six_specs = edge_outputs(6, length_y, length_z, length_x, rows)
    inputs = (mag_middle, mag_start, adjoint_end, phase, labels)
    edges = pl.pallas_call(
        functools.partial(edges_kernel, rows=rows),
        grid=grid,
        in_specs=[s for a in inputs for s in edge_specs_of(a.ndim, length_y, length_z, length_x, rows)],
        out_specs=six_specs,
        out_shape=six_shapes,
    )(*[a for a in inputs for _ in range(4)])
    halos = send_edges(*edges)
    factor, w_first = pl.pallas_call(
        functools.partial(factor_kernel, rows=rows),
        grid=grid,
        in_specs=[cur, cur_plane, cur_plane],
        out_specs=[cur, cur],
        out_shape=[pair, pair],
    )(adjoint_end, phase, labels)
    phase_grad, w_second, *w2_edges = pl.pallas_call(
        functools.partial(first_kernel, rows=rows),
        grid=grid,
        in_specs=field_specs(mag_middle.shape, rows) + field_specs(mag_start.shape, rows)
        + field_specs(w_first.shape, rows)
        + [cur, whole((6, length_z, length_x)), whole((6, length_z, length_x)), zspec(6), zspec(6)],
        out_specs=[cur_plane, cur] + edge_specs,
        out_shape=[plane, pair] + edge_shapes,
    )(mag_middle, mag_middle, mag_middle, mag_start, mag_start, mag_start,
      w_first, w_first, w_first, factor, *halos)
    halos = send_edges(*w2_edges)
    lam = pl.pallas_call(
        functools.partial(second_kernel, rows=rows),
        grid=grid,
        in_specs=field_specs(w_second.shape, rows)
        + [whole((2, length_z, length_x)), whole((2, length_z, length_x)), zspec(2), zspec(2)],
        out_specs=cur,
        out_shape=pair,
    )(w_second, w_second, w_second, *halos)
    return (lam, phase_grad)


def dipole_adjoint(phase_grad):
    count_y = lax.axis_size("gy")
    count_z = lax.axis_size("gz")
    parts = count_y * count_z
    block_y, block_z, length_x = phase_grad.shape
    length_y = block_y * count_y
    length_z = block_z * count_z
    block_x = length_x // parts
    pieces = 2 if block_x % 2 == 0 else 1
    piece_x = block_x // pieces
    table_x = cas_table(length_x).reshape(parts, pieces, piece_x, length_x)
    table_y = cas_table(length_y)
    table_z = cas_table(length_z)
    scale = 1.0 / (float(length_y) * float(length_z) * float(length_x))
    freq_y = signed_freq(jnp.arange(length_y, dtype=jnp.int32), length_y)
    freq_z = signed_freq(jnp.arange(length_z, dtype=jnp.int32), length_z)
    index = lax.axis_index("gy") * count_z + lax.axis_index("gz")
    sent = []
    for p in range(pieces):
        spec = along("sxn,yzn->sxyz", table_x[:, p], phase_grad)
        sent.append(lax.all_to_all(spec, ("gy", "gz"), 0, 0, tiled=True))
    result = None
    for p in range(pieces):
        spec = sent[p].reshape(count_y, count_z, piece_x, block_y, block_z)
        spec = spec.transpose(2, 0, 3, 1, 4).reshape(piece_x, length_y, length_z)
        spec = along("kz,xyz->xyk", table_z, spec)
        spec = along("ky,xyz->xkz", table_y, spec)
        first_x = index * block_x + p * piece_x
        freq_x = signed_freq(first_x + jnp.arange(piece_x, dtype=jnp.int32), length_x)
        kernel = dipole_block(freq_y[None, :, None], freq_z[None, None, :], freq_x[:, None, None])
        spec = spec * kernel
        spec = along("ky,xyz->xkz", table_y, spec)
        spec = along("kz,xyz->xyk", table_z, spec)
        spec = spec.reshape(piece_x, count_y, block_y, count_z, block_z)
        spec = spec.transpose(1, 3, 0, 2, 4).reshape(parts, piece_x, block_y, block_z)
        spec = lax.all_to_all(spec, ("gy", "gz"), 0, 0, tiled=True)
        part = along("sxn,sxyz->yzn", table_x[:, p], spec)
        result = part if result is None else result + part
    return result * scale


def per_device(mag_start, mag_middle, adjoint_end, phase, labels):
    lam, phase_grad = backward_sections(mag_start, mag_middle, adjoint_end, phase, labels)
    chi_grad = dipole_adjoint(phase_grad)
    return (lam, chi_grad)


def solution(mesh):
    return jax.shard_map(
        per_device,
        mesh=mesh,
        in_specs=(
            P(None, "gy", "gz", None),
            P(None, "gy", "gz", None),
            P(None, "gy", "gz", None),
            P("gy", "gz", None),
            P("gy", "gz", None),
        ),
        out_specs=(P(None, "gy", "gz", None), P("gy", "gz", None)),
        check_vma=False,
    )
```

```python
import functools
import math

import jax
import numpy as np
import jax.numpy as jnp
from jax import lax
from jax.experimental import pallas as pl
from jax.experimental.pallas import tpu as pltpu
from jax.sharding import PartitionSpec as P


def signed_freq(index, length):
    return jnp.where(index < length // 2, index, index - length)


def dipole_block(freq_y, freq_z, freq_x):
    square_z = freq_z * freq_z
    total = freq_y * freq_y + square_z + freq_x * freq_x
    ratio = square_z.astype(jnp.float32) / jnp.maximum(total, 1).astype(jnp.float32)
    return jnp.where(total == 0, jnp.float32(0.0), jnp.float32(1.0 / 3.0) - ratio)


def cas_table(length):
    index = jnp.arange(length, dtype=jnp.int32)
    product = index[:, None] * index[None, :] % length
    angle = product.astype(jnp.float32) * (2.0 * math.pi / length)
    return jnp.cos(angle) + jnp.sin(angle)


def along(spec, table, values):
    return jnp.einsum(spec, table, values, precision=lax.Precision.HIGH)


def plane_update(centre, below, above, z_low, z_high):
    length_z, length_x = centre.shape
    row = lax.broadcasted_iota(jnp.int32, centre.shape, 0)
    up = jnp.where(row == 0, z_low, pltpu.roll(centre, 1, 0))
    down = jnp.where(row == length_z - 1, z_high, pltpu.roll(centre, length_z - 1, 0))
    total = below + above + up + down
    total = total + pltpu.roll(centre, 1, 1) + pltpu.roll(centre, length_x - 1, 1)
    return centre + 0.15 * (total - 6.0 * centre)


def neighbour_planes(cur_ref, prev_ref, next_ref, y_low_ref, y_high_ref, rows, field, comp, r, step, last):
    below = cur_ref[comp, jnp.maximum(r - 1, 0)]
    below = jnp.where(r == 0, jnp.where(step == 0, y_low_ref[field], prev_ref[comp, 0]), below)
    above = cur_ref[comp, jnp.minimum(r + 1, rows - 1)]
    above = jnp.where(r == rows - 1, jnp.where(step == last, y_high_ref[field], next_ref[comp, 0]), above)
    return below, above


def write_edges(step, last, rows, r, values, y_first_ref, y_last_ref, z_first_ref, z_last_ref):
    for c, value in enumerate(values):
        z_first_ref[c, r] = value[0:1]
        z_last_ref[c, r] = value[value.shape[0] - 1:]

    @pl.when(jnp.logical_and(r == 0, step == 0))
    def _():
        for c, value in enumerate(values):
            y_first_ref[c] = value

    @pl.when(jnp.logical_and(r == rows - 1, step == last))
    def _():
        for c, value in enumerate(values):
            y_last_ref[c] = value


def for_rows(rows, body):
    def loop_body(r, carry):
        body(r)
        return carry
    lax.fori_loop(0, rows, loop_body, 0)


def sin_cos(x):
    k = jnp.floor(x * (2.0 / math.pi) + 0.5)
    r = (x - k * 1.5707963705062866) - k * (-4.371139000186243e-08)
    r2 = r * r
    s = r + r * r2 * (-1.0 / 6.0 + r2 * (1.0 / 120.0 + r2 * (-1.0 / 5040.0 + r2 * (1.0 / 362880.0))))
    c = 1.0 + r2 * (-0.5 + r2 * (1.0 / 24.0 + r2 * (-1.0 / 720.0 + r2 * (1.0 / 40320.0
                                                                        + r2 * (-1.0 / 3628800.0)))))
    quadrant = k.astype(jnp.int32) & 3
    swap = (quadrant & 1) == 1
    sin_x = jnp.where(swap, c, s)
    cos_x = jnp.where(swap, s, c)
    sin_x = jnp.where(quadrant >= 2, -sin_x, sin_x)
    cos_x = jnp.where((quadrant == 1) | (quadrant == 2), -cos_x, cos_x)
    return sin_x, cos_x


def step_factor(labels, phase):
    decays = [float(np.exp(-np.float32(rate))) for rate in (0.02, 0.3, 0.6, 1.2)]
    decay = jnp.where(labels == 1, decays[1], decays[0])
    decay = jnp.where(labels == 2, decays[2], decay)
    decay = jnp.where(labels == 3, decays[3], decay).astype(jnp.float32)
    sin_p, cos_p = sin_cos(phase)
    return decay * cos_p, decay * sin_p


def first_w(lam_real, lam_imag, labels, phase):
    f_real, f_imag = step_factor(labels, phase)
    return (f_real * lam_real - f_imag * lam_imag, f_real * lam_imag + f_imag * lam_real), (f_real, f_imag)


def factor_kernel(lam_ref, phase_ref, labels_ref, factor_ref, w_ref, *, rows):
    def body(r, carry):
        (w_real, w_imag), (f_real, f_imag) = first_w(lam_ref[0, r], lam_ref[1, r], labels_ref[r], phase_ref[r])
        factor_ref[0, r] = f_real
        factor_ref[1, r] = f_imag
        w_ref[0, r] = w_real
        w_ref[1, r] = w_imag
        return carry
    lax.fori_loop(0, rows, body, 0)


def edges_kernel(*refs, rows):
    (mm_y0, mm_y1, mm_z0, mm_z1, ms_y0, ms_y1, ms_z0, ms_z1, lam_y0, lam_y1, lam_z0, lam_z1,
     ph_y0, ph_y1, ph_z0, ph_z1, lb_y0, lb_y1, lb_z0, lb_z1,
     y_first_ref, y_last_ref, z_first_ref, z_last_ref) = refs

    @pl.when(pl.program_id(0) == 0)
    def _():
        for out_ref, m1, m2, lam, ph, lb in ((y_first_ref, mm_y0, ms_y0, lam_y0, ph_y0, lb_y0),
                                           (y_last_ref, mm_y1, ms_y1, lam_y1, ph_y1, lb_y1)):
            (w_real, w_imag), _ = first_w(lam[0, 0], lam[1, 0], lb[0], ph[0])
            planes = [m1[0, 0], m1[1, 0], m2[0, 0], m2[1, 0], w_real, w_imag]
            for c, value in enumerate(planes):
                out_ref[c] = value

    def body(r, carry):
        for out_ref, m1, m2, lam, ph, lb, at in ((z_first_ref, mm_z0, ms_z0, lam_z0, ph_z0, lb_z0, 0),
                                               (z_last_ref, mm_z1, ms_z1, lam_z1, ph_z1, lb_z1, 7)):
            (w_real, w_imag), _ = first_w(lam[0, r], lam[1, r], lb[r], ph[r])
            tiles = [m1[0, r], m1[1, r], m2[0, r], m2[1, r], w_real, w_imag]
            for c, value in enumerate(tiles):
                out_ref[c, r] = value[at:at + 1]
        return carry
    lax.fori_loop(0, rows, body, 0)


def edge_specs_of(ndim, length_y, length_z, length_x, rows):
    lead = (2,) if ndim == 4 else ()
    zero = (0,) * len(lead)
    tiles = length_z // 8
    return [
        pl.BlockSpec(lead + (1, length_z, length_x), lambda i: zero + (0, 0, 0)),
        pl.BlockSpec(lead + (1, length_z, length_x), lambda i: zero + (length_y - 1, 0, 0)),
        pl.BlockSpec(lead + (rows, 8, length_x), lambda i: zero + (i, 0, 0)),
        pl.BlockSpec(lead + (rows, 8, length_x), lambda i: zero + (i, tiles - 1, 0)),
    ]


def edge_outputs(comps, length_y, length_z, length_x, rows):
    plane = jax.ShapeDtypeStruct((comps, length_z, length_x), jnp.float32)
    row = jax.ShapeDtypeStruct((comps, length_y, 1, length_x), jnp.float32)
    plane_spec = pl.BlockSpec((comps, length_z, length_x), lambda i: (0, 0, 0))
    row_spec = pl.BlockSpec((comps, rows, 1, length_x), lambda i: (0, i, 0, 0))
    return [plane, plane, row, row], [plane_spec, plane_spec, row_spec, row_spec]


def first_kernel(*refs, rows):
    (mm_ref, mm_prev, mm_next, ms_ref, ms_prev, ms_next, w_ref, w_prev, w_next,
     factor_ref, y_low_ref, y_high_ref, z_low_ref, z_high_ref, pg_ref, w2_ref) = refs[:16]
    step = pl.program_id(0)
    last = pl.num_programs(0) - 1
    fields = ((mm_ref, mm_prev, mm_next), (ms_ref, ms_prev, ms_next), (w_ref, w_prev, w_next))

    def body(r):
        new = []
        for f, (cur, prev, nxt) in enumerate(fields):
            pair = []
            for comp in range(2):
                below, above = neighbour_planes(cur, prev, nxt, y_low_ref, y_high_ref, rows, 2 * f + comp, comp, r,
                                                step, last)
                pair.append(plane_update(cur[comp, r], below, above,
                                         z_low_ref[2 * f + comp, r], z_high_ref[2 * f + comp, r]))
            new.append(pair)
        (u1_real, u1_imag), (u2_real, u2_imag), (lam_real, lam_imag) = new
        w_real = w_ref[0, r]
        w_imag = w_ref[1, r]
        f_real = factor_ref[0, r]
        f_imag = factor_ref[1, r]
        w2_real = f_real * lam_real - f_imag * lam_imag
        w2_imag = f_real * lam_imag + f_imag * lam_real
        grad = w_real * u1_imag - w_imag * u1_real
        pg_ref[r] = grad + (w2_real * u2_imag - w2_imag * u2_real)
        w2_ref[0, r] = w2_real
        w2_ref[1, r] = w2_imag
        write_edges(step, last, rows, r, [w2_real, w2_imag], *refs[16:])

    for_rows(rows, body)


def second_kernel(w_ref, w_prev, w_next, y_low_ref, y_high_ref, z_low_ref, z_high_ref, out_ref, *, rows):
    step = pl.program_id(0)
    last = pl.num_programs(0) - 1

    def body(r):
        for comp in range(2):
            below, above = neighbour_planes(w_ref, w_prev, w_next, y_low_ref, y_high_ref, rows, comp, comp, r,
                                            step, last)
            out_ref[comp, r] = plane_update(w_ref[comp, r], below, above,
                                            z_low_ref[comp, r], z_high_ref[comp, r])

    for_rows(rows, body)


def block_rows(length_y):
    rows = 8
    while length_y % rows:
        rows //= 2
    return rows


def field_specs(shape, rows):
    comps, length_y, length_z, length_x = shape
    cur = pl.BlockSpec((comps, rows, length_z, length_x), lambda i: (0, i, 0, 0))
    prev = pl.BlockSpec((comps, 1, length_z, length_x),
                        lambda i: (0, jnp.maximum(i * rows - 1, 0), 0, 0))
    nxt = pl.BlockSpec((comps, 1, length_z, length_x),
                       lambda i: (0, jnp.minimum(i * rows + rows, length_y - 1), 0, 0))
    return [cur, prev, nxt]


def send_edges(y_first, y_last, z_first, z_last):
    results = []
    for axis, first, last in (("gy", y_first, y_last), ("gz", z_first, z_last)):
        count = lax.axis_size(axis)
        up = [(i, (i + 1) % count) for i in range(count)]
        down = [(j, i) for i, j in up]
        if count == 2:
            both = lax.ppermute(jnp.stack([last, first]), axis, up)
            results.extend([both[0], both[1]])
        else:
            results.extend([lax.ppermute(last, axis, up), lax.ppermute(first, axis, down)])
    return results


def backward_sections(mag_start, mag_middle, adjoint_end, phase, labels):
    _, length_y, length_z, length_x = mag_start.shape
    rows = block_rows(length_y)
    grid = (length_y // rows,)
    plane = jax.ShapeDtypeStruct((length_y, length_z, length_x), jnp.float32)
    pair = jax.ShapeDtypeStruct((2, length_y, length_z, length_x), jnp.float32)
    cur = pl.BlockSpec((2, rows, length_z, length_x), lambda i: (0, i, 0, 0))
    cur_plane = pl.BlockSpec((rows, length_z, length_x), lambda i: (i, 0, 0))
    whole = lambda shape: pl.BlockSpec(shape, lambda i: (0,) * len(shape))
    zspec = lambda comps: pl.BlockSpec((comps, rows, 1, length_x), lambda i: (0, i, 0, 0))
    edge_shapes, edge_specs = edge_outputs(2, length_y, length_z, length_x, rows)
    six_shapes, six_specs = edge_outputs(6, length_y, length_z, length_x, rows)
    inputs = (mag_middle, mag_start, adjoint_end, phase, labels)
    edges = pl.pallas_call(
        functools.partial(edges_kernel, rows=rows),
        grid=grid,
        in_specs=[s for a in inputs for s in edge_specs_of(a.ndim, length_y, length_z, length_x, rows)],
        out_specs=six_specs,
        out_shape=six_shapes,
    )(*[a for a in inputs for _ in range(4)])
    halos = send_edges(*edges)
    factor, w_first = pl.pallas_call(
        functools.partial(factor_kernel, rows=rows),
        grid=grid,
        in_specs=[cur, cur_plane, cur_plane],
        out_specs=[cur, cur],
        out_shape=[pair, pair],
    )(adjoint_end, phase, labels)
    phase_grad, w_second, *w2_edges = pl.pallas_call(
        functools.partial(first_kernel, rows=rows),
        grid=grid,
        in_specs=field_specs(mag_middle.shape, rows) + field_specs(mag_start.shape, rows)
        + field_specs(w_first.shape, rows)
        + [cur, whole((6, length_z, length_x)), whole((6, length_z, length_x)), zspec(6), zspec(6)],
        out_specs=[cur_plane, cur] + edge_specs,
        out_shape=[plane, pair] + edge_shapes,
    )(mag_middle, mag_middle, mag_middle, mag_start, mag_start, mag_start,
      w_first, w_first, w_first, factor, *halos)
    halos = send_edges(*w2_edges)
    lam = pl.pallas_call(
        functools.partial(second_kernel, rows=rows),
        grid=grid,
        in_specs=field_specs(w_second.shape, rows)
        + [whole((2, length_z, length_x)), whole((2, length_z, length_x)), zspec(2), zspec(2)],
        out_specs=cur,
        out_shape=pair,
    )(w_second, w_second, w_second, *halos)
    return (lam, phase_grad)


def dipole_adjoint(phase_grad):
    count_y = lax.axis_size("gy")
    count_z = lax.axis_size("gz")
    parts = count_y * count_z
    block_y, block_z, length_x = phase_grad.shape
    length_y = block_y * count_y
    length_z = block_z * count_z
    block_x = length_x // parts
    pieces = 2 if block_x % 2 == 0 else 1
    piece_x = block_x // pieces
    table_x = cas_table(length_x).reshape(parts, pieces, piece_x, length_x)
    table_y = cas_table(length_y)
    table_z = cas_table(length_z)
    scale = 1.0 / (float(length_y) * float(length_z) * float(length_x))
    freq_y = signed_freq(jnp.arange(length_y, dtype=jnp.int32), length_y)
    freq_z = signed_freq(jnp.arange(length_z, dtype=jnp.int32), length_z)
    index = lax.axis_index("gy") * count_z + lax.axis_index("gz")
    sent = []
    for p in range(pieces):
        spec = along("sxn,yzn->sxyz", table_x[:, p], phase_grad)
        sent.append(lax.all_to_all(spec, ("gy", "gz"), 0, 0, tiled=True))
    result = None
    for p in range(pieces):
        spec = sent[p].reshape(count_y, count_z, piece_x, block_y, block_z)
        spec = spec.transpose(2, 0, 3, 1, 4).reshape(piece_x, length_y, length_z)
        spec = along("kz,xyz->xyk", table_z, spec)
        spec = along("ky,xyz->xkz", table_y, spec)
        first_x = index * block_x + p * piece_x
        freq_x = signed_freq(first_x + jnp.arange(piece_x, dtype=jnp.int32), length_x)
        kernel = dipole_block(freq_y[None, :, None], freq_z[None, None, :], freq_x[:, None, None])
        spec = spec * kernel
        spec = along("ky,xyz->xkz", table_y, spec)
        spec = along("kz,xyz->xyk", table_z, spec)
        spec = spec.reshape(piece_x, count_y, block_y, count_z, block_z)
        spec = spec.transpose(1, 3, 0, 2, 4).reshape(parts, piece_x, block_y, block_z)
        spec = lax.all_to_all(spec, ("gy", "gz"), 0, 0, tiled=True)
        part = along("sxn,sxyz->yzn", table_x[:, p], spec)
        result = part if result is None else result + part
    return result * scale


def per_device(mag_start, mag_middle, adjoint_end, phase, labels):
    lam, phase_grad = backward_sections(mag_start, mag_middle, adjoint_end, phase, labels)
    chi_grad = dipole_adjoint(phase_grad)
    return (lam, chi_grad)


def solution(mesh):
    return jax.shard_map(
        per_device,
        mesh=mesh,
        in_specs=(
            P(None, "gy", "gz", None),
            P(None, "gy", "gz", None),
            P(None, "gy", "gz", None),
            P("gy", "gz", None),
            P("gy", "gz", None),
        ),
        out_specs=(P(None, "gy", "gz", None), P("gy", "gz", None)),
        check_vma=False,
    )
```

```python
import functools
import math

import jax
import numpy as np
import jax.numpy as jnp
from jax import lax
from jax.experimental import pallas as pl
from jax.experimental.pallas import tpu as pltpu
from jax.sharding import PartitionSpec as P


def signed_freq(index, length):
    return jnp.where(index < length // 2, index, index - length)


def dipole_block(freq_y, freq_z, freq_x):
    square_z = freq_z * freq_z
    total = freq_y * freq_y + square_z + freq_x * freq_x
    ratio = square_z.astype(jnp.float32) / jnp.maximum(total, 1).astype(jnp.float32)
    return jnp.where(total == 0, jnp.float32(0.0), jnp.float32(1.0 / 3.0) - ratio)


def cas_table(length):
    index = jnp.arange(length, dtype=jnp.int32)
    product = index[:, None] * index[None, :] % length
    angle = product.astype(jnp.float32) * (2.0 * math.pi / length)
    return jnp.cos(angle) + jnp.sin(angle)


def along(spec, table, values):
    return jnp.einsum(spec, table, values, precision=lax.Precision.HIGH)


def plane_update(centre, below, above, z_low, z_high):
    length_z, length_x = centre.shape
    row = lax.broadcasted_iota(jnp.int32, centre.shape, 0)
    up = jnp.where(row == 0, z_low, pltpu.roll(centre, 1, 0))
    down = jnp.where(row == length_z - 1, z_high, pltpu.roll(centre, length_z - 1, 0))
    total = below + above + up + down
    total = total + pltpu.roll(centre, 1, 1) + pltpu.roll(centre, length_x - 1, 1)
    return centre + 0.15 * (total - 6.0 * centre)


def neighbour_planes(cur_ref, prev_ref, next_ref, y_low_ref, y_high_ref, rows, field, comp, r, step, last):
    below = cur_ref[comp, jnp.maximum(r - 1, 0)]
    below = jnp.where(r == 0, jnp.where(step == 0, y_low_ref[field], prev_ref[comp, 0]), below)
    above = cur_ref[comp, jnp.minimum(r + 1, rows - 1)]
    above = jnp.where(r == rows - 1, jnp.where(step == last, y_high_ref[field], next_ref[comp, 0]), above)
    return below, above


def write_edges(step, last, rows, r, values, y_first_ref, y_last_ref, z_first_ref, z_last_ref):
    for c, value in enumerate(values):
        z_first_ref[c, r] = value[0:1]
        z_last_ref[c, r] = value[value.shape[0] - 1:]

    @pl.when(jnp.logical_and(r == 0, step == 0))
    def _():
        for c, value in enumerate(values):
            y_first_ref[c] = value

    @pl.when(jnp.logical_and(r == rows - 1, step == last))
    def _():
        for c, value in enumerate(values):
            y_last_ref[c] = value


def for_rows(rows, body):
    def loop_body(r, carry):
        body(r)
        return carry
    lax.fori_loop(0, rows, loop_body, 0)


def sin_cos(x):
    k = jnp.floor(x * (2.0 / math.pi) + 0.5)
    r = (x - k * 1.5707963705062866) - k * (-4.371139000186243e-08)
    r2 = r * r
    s = r + r * r2 * (-1.0 / 6.0 + r2 * (1.0 / 120.0 + r2 * (-1.0 / 5040.0 + r2 * (1.0 / 362880.0))))
    c = 1.0 + r2 * (-0.5 + r2 * (1.0 / 24.0 + r2 * (-1.0 / 720.0 + r2 * (1.0 / 40320.0
                                                                        + r2 * (-1.0 / 3628800.0)))))
    quadrant = k.astype(jnp.int32) & 3
    swap = (quadrant & 1) == 1
    sin_x = jnp.where(swap, c, s)
    cos_x = jnp.where(swap, s, c)
    sin_x = jnp.where(quadrant >= 2, -sin_x, sin_x)
    cos_x = jnp.where((quadrant == 1) | (quadrant == 2), -cos_x, cos_x)
    return sin_x, cos_x


def step_factor(labels, phase):
    decays = [float(np.exp(-np.float32(rate))) for rate in (0.02, 0.3, 0.6, 1.2)]
    decay = jnp.where(labels == 1, decays[1], decays[0])
    decay = jnp.where(labels == 2, decays[2], decay)
    decay = jnp.where(labels == 3, decays[3], decay).astype(jnp.float32)
    sin_p, cos_p = sin_cos(phase)
    return decay * cos_p, decay * sin_p


def first_w(lam_real, lam_imag, labels, phase):
    f_real, f_imag = step_factor(labels, phase)
    return (f_real * lam_real - f_imag * lam_imag, f_real * lam_imag + f_imag * lam_real), (f_real, f_imag)


def factor_kernel(lam_ref, phase_ref, labels_ref, factor_ref, w_ref, *, rows):
    def body(r, carry):
        (w_real, w_imag), (f_real, f_imag) = first_w(lam_ref[0, r], lam_ref[1, r], labels_ref[r], phase_ref[r])
        factor_ref[0, r] = f_real
        factor_ref[1, r] = f_imag
        w_ref[0, r] = w_real
        w_ref[1, r] = w_imag
        return carry
    lax.fori_loop(0, rows, body, 0)


def edges_kernel(*refs, rows):
    (mm_y0, mm_y1, mm_z0, mm_z1, ms_y0, ms_y1, ms_z0, ms_z1, lam_y0, lam_y1, lam_z0, lam_z1,
     ph_y0, ph_y1, ph_z0, ph_z1, lb_y0, lb_y1, lb_z0, lb_z1,
     y_first_ref, y_last_ref, z_first_ref, z_last_ref) = refs

    @pl.when(pl.program_id(0) == 0)
    def _():
        for out_ref, m1, m2, lam, ph, lb in ((y_first_ref, mm_y0, ms_y0, lam_y0, ph_y0, lb_y0),
                                           (y_last_ref, mm_y1, ms_y1, lam_y1, ph_y1, lb_y1)):
            (w_real, w_imag), _ = first_w(lam[0, 0], lam[1, 0], lb[0], ph[0])
            planes = [m1[0, 0], m1[1, 0], m2[0, 0], m2[1, 0], w_real, w_imag]
            for c, value in enumerate(planes):
                out_ref[c] = value

    def body(r, carry):
        for out_ref, m1, m2, lam, ph, lb, at in ((z_first_ref, mm_z0, ms_z0, lam_z0, ph_z0, lb_z0, 0),
                                               (z_last_ref, mm_z1, ms_z1, lam_z1, ph_z1, lb_z1, 7)):
            (w_real, w_imag), _ = first_w(lam[0, r], lam[1, r], lb[r], ph[r])
            tiles = [m1[0, r], m1[1, r], m2[0, r], m2[1, r], w_real, w_imag]
            for c, value in enumerate(tiles):
                out_ref[c, r] = value[at:at + 1]
        return carry
    lax.fori_loop(0, rows, body, 0)


def edge_specs_of(ndim, length_y, length_z, length_x, rows):
    lead = (2,) if ndim == 4 else ()
    zero = (0,) * len(lead)
    tiles = length_z // 8
    return [
        pl.BlockSpec(lead + (1, length_z, length_x), lambda i: zero + (0, 0, 0)),
        pl.BlockSpec(lead + (1, length_z, length_x), lambda i: zero + (length_y - 1, 0, 0)),
        pl.BlockSpec(lead + (rows, 8, length_x), lambda i: zero + (i, 0, 0)),
        pl.BlockSpec(lead + (rows, 8, length_x), lambda i: zero + (i, tiles - 1, 0)),
    ]


def edge_outputs(comps, length_y, length_z, length_x, rows):
    plane = jax.ShapeDtypeStruct((comps, length_z, length_x), jnp.float32)
    row = jax.ShapeDtypeStruct((comps, length_y, 1, length_x), jnp.float32)
    plane_spec = pl.BlockSpec((comps, length_z, length_x), lambda i: (0, 0, 0))
    row_spec = pl.BlockSpec((comps, rows, 1, length_x), lambda i: (0, i, 0, 0))
    return [plane, plane, row, row], [plane_spec, plane_spec, row_spec, row_spec]


def first_kernel(*refs, rows):
    (mm_ref, mm_prev, mm_next, ms_ref, ms_prev, ms_next, w_ref, w_prev, w_next,
     factor_ref, y_low_ref, y_high_ref, z_low_ref, z_high_ref, pg_ref, w2_ref) = refs[:16]
    step = pl.program_id(0)
    last = pl.num_programs(0) - 1
    fields = ((mm_ref, mm_prev, mm_next), (ms_ref, ms_prev, ms_next), (w_ref, w_prev, w_next))

    def body(r):
        new = []
        for f, (cur, prev, nxt) in enumerate(fields):
            pair = []
            for comp in range(2):
                below, above = neighbour_planes(cur, prev, nxt, y_low_ref, y_high_ref, rows, 2 * f + comp, comp, r,
                                                step, last)
                pair.append(plane_update(cur[comp, r], below, above,
                                         z_low_ref[2 * f + comp, r], z_high_ref[2 * f + comp, r]))
            new.append(pair)
        (u1_real, u1_imag), (u2_real, u2_imag), (lam_real, lam_imag) = new
        w_real = w_ref[0, r]
        w_imag = w_ref[1, r]
        f_real = factor_ref[0, r]
        f_imag = factor_ref[1, r]
        w2_real = f_real * lam_real - f_imag * lam_imag
        w2_imag = f_real * lam_imag + f_imag * lam_real
        grad = w_real * u1_imag - w_imag * u1_real
        pg_ref[r] = grad + (w2_real * u2_imag - w2_imag * u2_real)
        w2_ref[0, r] = w2_real
        w2_ref[1, r] = w2_imag
        write_edges(step, last, rows, r, [w2_real, w2_imag], *refs[16:])

    for_rows(rows, body)


def second_kernel(w_ref, w_prev, w_next, y_low_ref, y_high_ref, z_low_ref, z_high_ref, out_ref, *, rows):
    step = pl.program_id(0)
    last = pl.num_programs(0) - 1

    def body(r):
        for comp in range(2):
            below, above = neighbour_planes(w_ref, w_prev, w_next, y_low_ref, y_high_ref, rows, comp, comp, r,
                                            step, last)
            out_ref[comp, r] = plane_update(w_ref[comp, r], below, above,
                                            z_low_ref[comp, r], z_high_ref[comp, r])

    for_rows(rows, body)


def block_rows(length_y):
    rows = 8
    while length_y % rows:
        rows //= 2
    return rows


def field_specs(shape, rows):
    comps, length_y, length_z, length_x = shape
    cur = pl.BlockSpec((comps, rows, length_z, length_x), lambda i: (0, i, 0, 0))
    prev = pl.BlockSpec((comps, 1, length_z, length_x),
                        lambda i: (0, jnp.maximum(i * rows - 1, 0), 0, 0))
    nxt = pl.BlockSpec((comps, 1, length_z, length_x),
                       lambda i: (0, jnp.minimum(i * rows + rows, length_y - 1), 0, 0))
    return [cur, prev, nxt]


def send_edges(y_first, y_last, z_first, z_last):
    results = []
    for axis, first, last in (("gy", y_first, y_last), ("gz", z_first, z_last)):
        count = lax.axis_size(axis)
        up = [(i, (i + 1) % count) for i in range(count)]
        down = [(j, i) for i, j in up]
        if count == 2:
            both = lax.ppermute(jnp.stack([last, first]), axis, up)
            results.extend([both[0], both[1]])
        else:
            results.extend([lax.ppermute(last, axis, up), lax.ppermute(first, axis, down)])
    return results


def backward_sections(mag_start, mag_middle, adjoint_end, phase, labels):
    _, length_y, length_z, length_x = mag_start.shape
    rows = block_rows(length_y)
    grid = (length_y // rows,)
    plane = jax.ShapeDtypeStruct((length_y, length_z, length_x), jnp.float32)
    pair = jax.ShapeDtypeStruct((2, length_y, length_z, length_x), jnp.float32)
    cur = pl.BlockSpec((2, rows, length_z, length_x), lambda i: (0, i, 0, 0))
    cur_plane = pl.BlockSpec((rows, length_z, length_x), lambda i: (i, 0, 0))
    whole = lambda shape: pl.BlockSpec(shape, lambda i: (0,) * len(shape))
    zspec = lambda comps: pl.BlockSpec((comps, rows, 1, length_x), lambda i: (0, i, 0, 0))
    edge_shapes, edge_specs = edge_outputs(2, length_y, length_z, length_x, rows)
    six_shapes, six_specs = edge_outputs(6, length_y, length_z, length_x, rows)
    inputs = (mag_middle, mag_start, adjoint_end, phase, labels)
    edges = pl.pallas_call(
        functools.partial(edges_kernel, rows=rows),
        grid=grid,
        in_specs=[s for a in inputs for s in edge_specs_of(a.ndim, length_y, length_z, length_x, rows)],
        out_specs=six_specs,
        out_shape=six_shapes,
    )(*[a for a in inputs for _ in range(4)])
    halos = send_edges(*edges)
    factor, w_first = pl.pallas_call(
        functools.partial(factor_kernel, rows=rows),
        grid=grid,
        in_specs=[cur, cur_plane, cur_plane],
        out_specs=[cur, cur],
        out_shape=[pair, pair],
    )(adjoint_end, phase, labels)
    phase_grad, w_second, *w2_edges = pl.pallas_call(
        functools.partial(first_kernel, rows=rows),
        grid=grid,
        in_specs=field_specs(mag_middle.shape, rows) + field_specs(mag_start.shape, rows)
        + field_specs(w_first.shape, rows)
        + [cur, whole((6, length_z, length_x)), whole((6, length_z, length_x)), zspec(6), zspec(6)],
        out_specs=[cur_plane, cur] + edge_specs,
        out_shape=[plane, pair] + edge_shapes,
    )(mag_middle, mag_middle, mag_middle, mag_start, mag_start, mag_start,
      w_first, w_first, w_first, factor, *halos)
    halos = send_edges(*w2_edges)
    lam = pl.pallas_call(
        functools.partial(second_kernel, rows=rows),
        grid=grid,
        in_specs=field_specs(w_second.shape, rows)
        + [whole((2, length_z, length_x)), whole((2, length_z, length_x)), zspec(2), zspec(2)],
        out_specs=cur,
        out_shape=pair,
    )(w_second, w_second, w_second, *halos)
    return (lam, phase_grad)


def dipole_adjoint(phase_grad, lam):
    count_y = lax.axis_size("gy")
    count_z = lax.axis_size("gz")
    parts = count_y * count_z
    block_y, block_z, length_x = phase_grad.shape
    length_y = block_y * count_y
    length_z = block_z * count_z
    block_x = length_x // parts
    pieces = 2 if block_x % 2 == 0 else 1
    piece_x = block_x // pieces
    table_x = cas_table(length_x).reshape(parts, pieces, piece_x, length_x)
    table_y = cas_table(length_y)
    table_z = cas_table(length_z)
    scale = 1.0 / (float(length_y) * float(length_z) * float(length_x))
    freq_y = signed_freq(jnp.arange(length_y, dtype=jnp.int32), length_y)
    freq_z = signed_freq(jnp.arange(length_z, dtype=jnp.int32), length_z)
    index = lax.axis_index("gy") * count_z + lax.axis_index("gz")
    sent = []
    for p in range(pieces):
        spec = along("sxn,yzn->sxyz", table_x[:, p], phase_grad)
        if p == pieces - 1 and pieces > 1:
            lam, spec = lax.optimization_barrier((lam, spec))
        sent.append(lax.all_to_all(spec, ("gy", "gz"), 0, 0, tiled=True))
    result = None
    for p in range(pieces):
        spec = sent[p].reshape(count_y, count_z, piece_x, block_y, block_z)
        spec = spec.transpose(2, 0, 3, 1, 4).reshape(piece_x, length_y, length_z)
        spec = along("kz,xyz->xyk", table_z, spec)
        spec = along("ky,xyz->xkz", table_y, spec)
        first_x = index * block_x + p * piece_x
        freq_x = signed_freq(first_x + jnp.arange(piece_x, dtype=jnp.int32), length_x)
        kernel = dipole_block(freq_y[None, :, None], freq_z[None, None, :], freq_x[:, None, None])
        spec = spec * kernel
        spec = along("ky,xyz->xkz", table_y, spec)
        spec = along("kz,xyz->xyk", table_z, spec)
        spec = spec.reshape(piece_x, count_y, block_y, count_z, block_z)
        spec = spec.transpose(1, 3, 0, 2, 4).reshape(parts, piece_x, block_y, block_z)
        spec = lax.all_to_all(spec, ("gy", "gz"), 0, 0, tiled=True)
        part = along("sxn,sxyz->yzn", table_x[:, p], spec)
        result = part if result is None else result + part
    return result * scale, lam


def per_device(mag_start, mag_middle, adjoint_end, phase, labels):
    lam, phase_grad = backward_sections(mag_start, mag_middle, adjoint_end, phase, labels)
    chi_grad, lam = dipole_adjoint(phase_grad, lam)
    return (lam, chi_grad)


def solution(mesh):
    return jax.shard_map(
        per_device,
        mesh=mesh,
        in_specs=(
            P(None, "gy", "gz", None),
            P(None, "gy", "gz", None),
            P(None, "gy", "gz", None),
            P("gy", "gz", None),
            P("gy", "gz", None),
        ),
        out_specs=(P(None, "gy", "gz", None), P("gy", "gz", None)),
        check_vma=False,
    )
```

```python
import functools
import math

import jax
import numpy as np
import jax.numpy as jnp
from jax import lax
from jax.experimental import pallas as pl
from jax.experimental.pallas import tpu as pltpu
from jax.sharding import PartitionSpec as P


def signed_freq(index, length):
    return jnp.where(index < length // 2, index, index - length)


def dipole_block(freq_y, freq_z, freq_x):
    square_z = freq_z * freq_z
    total = freq_y * freq_y + square_z + freq_x * freq_x
    ratio = square_z.astype(jnp.float32) / jnp.maximum(total, 1).astype(jnp.float32)
    return jnp.where(total == 0, jnp.float32(0.0), jnp.float32(1.0 / 3.0) - ratio)


def cas_table(length):
    index = jnp.arange(length, dtype=jnp.int32)
    product = index[:, None] * index[None, :] % length
    angle = product.astype(jnp.float32) * (2.0 * math.pi / length)
    return jnp.cos(angle) + jnp.sin(angle)


def along(spec, table, values):
    return jnp.einsum(spec, table, values, precision=lax.Precision.HIGH)


def plane_update(centre, below, above, z_low, z_high):
    length_z, length_x = centre.shape
    row = lax.broadcasted_iota(jnp.int32, centre.shape, 0)
    up = jnp.where(row == 0, z_low, pltpu.roll(centre, 1, 0))
    down = jnp.where(row == length_z - 1, z_high, pltpu.roll(centre, length_z - 1, 0))
    total = below + above + up + down
    total = total + pltpu.roll(centre, 1, 1) + pltpu.roll(centre, length_x - 1, 1)
    return centre + 0.15 * (total - 6.0 * centre)


def neighbour_planes(cur_ref, prev_ref, next_ref, y_low_ref, y_high_ref, rows, field, comp, r, step, last):
    below = cur_ref[comp, jnp.maximum(r - 1, 0)]
    below = jnp.where(r == 0, jnp.where(step == 0, y_low_ref[field], prev_ref[comp, 0]), below)
    above = cur_ref[comp, jnp.minimum(r + 1, rows - 1)]
    above = jnp.where(r == rows - 1, jnp.where(step == last, y_high_ref[field], next_ref[comp, 0]), above)
    return below, above


def write_edges(step, last, rows, r, values, y_first_ref, y_last_ref, z_first_ref, z_last_ref):
    for c, value in enumerate(values):
        z_first_ref[c, r] = value[0:1]
        z_last_ref[c, r] = value[value.shape[0] - 1:]

    @pl.when(jnp.logical_and(r == 0, step == 0))
    def _():
        for c, value in enumerate(values):
            y_first_ref[c] = value

    @pl.when(jnp.logical_and(r == rows - 1, step == last))
    def _():
        for c, value in enumerate(values):
            y_last_ref[c] = value


def for_rows(rows, body):
    def loop_body(r, carry):
        body(r)
        return carry
    lax.fori_loop(0, rows, loop_body, 0)


def sin_cos(x):
    k = jnp.floor(x * (2.0 / math.pi) + 0.5)
    r = (x - k * 1.5707963705062866) - k * (-4.371139000186243e-08)
    r2 = r * r
    s = r + r * r2 * (-1.0 / 6.0 + r2 * (1.0 / 120.0 + r2 * (-1.0 / 5040.0 + r2 * (1.0 / 362880.0))))
    c = 1.0 + r2 * (-0.5 + r2 * (1.0 / 24.0 + r2 * (-1.0 / 720.0 + r2 * (1.0 / 40320.0
                                                                        + r2 * (-1.0 / 3628800.0)))))
    quadrant = k.astype(jnp.int32) & 3
    swap = (quadrant & 1) == 1
    sin_x = jnp.where(swap, c, s)
    cos_x = jnp.where(swap, s, c)
    sin_x = jnp.where(quadrant >= 2, -sin_x, sin_x)
    cos_x = jnp.where((quadrant == 1) | (quadrant == 2), -cos_x, cos_x)
    return sin_x, cos_x


def step_factor(labels, phase):
    decays = [float(np.exp(-np.float32(rate))) for rate in (0.02, 0.3, 0.6, 1.2)]
    decay = jnp.where(labels == 1, decays[1], decays[0])
    decay = jnp.where(labels == 2, decays[2], decay)
    decay = jnp.where(labels == 3, decays[3], decay).astype(jnp.float32)
    sin_p, cos_p = sin_cos(phase)
    return decay * cos_p, decay * sin_p


def first_w(lam_real, lam_imag, labels, phase):
    f_real, f_imag = step_factor(labels, phase)
    return (f_real * lam_real - f_imag * lam_imag, f_real * lam_imag + f_imag * lam_real), (f_real, f_imag)


def factor_kernel(lam_ref, phase_ref, labels_ref, factor_ref, w_ref, *, rows):
    def body(r, carry):
        (w_real, w_imag), (f_real, f_imag) = first_w(lam_ref[0, r], lam_ref[1, r], labels_ref[r], phase_ref[r])
        factor_ref[0, r] = f_real
        factor_ref[1, r] = f_imag
        w_ref[0, r] = w_real
        w_ref[1, r] = w_imag
        return carry
    lax.fori_loop(0, rows, body, 0)


def edges_kernel(*refs, rows):
    (mm_y0, mm_y1, mm_z0, mm_z1, ms_y0, ms_y1, ms_z0, ms_z1, lam_y0, lam_y1, lam_z0, lam_z1,
     ph_y0, ph_y1, ph_z0, ph_z1, lb_y0, lb_y1, lb_z0, lb_z1,
     y_first_ref, y_last_ref, z_first_ref, z_last_ref) = refs

    @pl.when(pl.program_id(0) == 0)
    def _():
        for out_ref, m1, m2, lam, ph, lb in ((y_first_ref, mm_y0, ms_y0, lam_y0, ph_y0, lb_y0),
                                           (y_last_ref, mm_y1, ms_y1, lam_y1, ph_y1, lb_y1)):
            (w_real, w_imag), _ = first_w(lam[0, 0], lam[1, 0], lb[0], ph[0])
            planes = [m1[0, 0], m1[1, 0], m2[0, 0], m2[1, 0], w_real, w_imag]
            for c, value in enumerate(planes):
                out_ref[c] = value

    def body(r, carry):
        for out_ref, m1, m2, lam, ph, lb, at in ((z_first_ref, mm_z0, ms_z0, lam_z0, ph_z0, lb_z0, 0),
                                               (z_last_ref, mm_z1, ms_z1, lam_z1, ph_z1, lb_z1, 7)):
            (w_real, w_imag), _ = first_w(lam[0, r], lam[1, r], lb[r], ph[r])
            tiles = [m1[0, r], m1[1, r], m2[0, r], m2[1, r], w_real, w_imag]
            for c, value in enumerate(tiles):
                out_ref[c, r] = value[at:at + 1]
        return carry
    lax.fori_loop(0, rows, body, 0)


def edge_specs_of(ndim, length_y, length_z, length_x, rows):
    lead = (2,) if ndim == 4 else ()
    zero = (0,) * len(lead)
    tiles = length_z // 8
    return [
        pl.BlockSpec(lead + (1, length_z, length_x), lambda i: zero + (0, 0, 0)),
        pl.BlockSpec(lead + (1, length_z, length_x), lambda i: zero + (length_y - 1, 0, 0)),
        pl.BlockSpec(lead + (rows, 8, length_x), lambda i: zero + (i, 0, 0)),
        pl.BlockSpec(lead + (rows, 8, length_x), lambda i: zero + (i, tiles - 1, 0)),
    ]


def edge_outputs(comps, length_y, length_z, length_x, rows):
    plane = jax.ShapeDtypeStruct((comps, length_z, length_x), jnp.float32)
    row = jax.ShapeDtypeStruct((comps, length_y, 1, length_x), jnp.float32)
    plane_spec = pl.BlockSpec((comps, length_z, length_x), lambda i: (0, 0, 0))
    row_spec = pl.BlockSpec((comps, rows, 1, length_x), lambda i: (0, i, 0, 0))
    return [plane, plane, row, row], [plane_spec, plane_spec, row_spec, row_spec]


def first_kernel(*refs, rows):
    (mm_ref, mm_prev, mm_next, ms_ref, ms_prev, ms_next, w_ref, w_prev, w_next,
     factor_ref, y_low_ref, y_high_ref, z_low_ref, z_high_ref, pg_ref, w2_ref) = refs[:16]
    step = pl.program_id(0)
    last = pl.num_programs(0) - 1
    fields = ((mm_ref, mm_prev, mm_next), (ms_ref, ms_prev, ms_next), (w_ref, w_prev, w_next))

    def body(r):
        new = []
        for f, (cur, prev, nxt) in enumerate(fields):
            pair = []
            for comp in range(2):
                below, above = neighbour_planes(cur, prev, nxt, y_low_ref, y_high_ref, rows, 2 * f + comp, comp, r,
                                                step, last)
                pair.append(plane_update(cur[comp, r], below, above,
                                         z_low_ref[2 * f + comp, r], z_high_ref[2 * f + comp, r]))
            new.append(pair)
        (u1_real, u1_imag), (u2_real, u2_imag), (lam_real, lam_imag) = new
        w_real = w_ref[0, r]
        w_imag = w_ref[1, r]
        f_real = factor_ref[0, r]
        f_imag = factor_ref[1, r]
        w2_real = f_real * lam_real - f_imag * lam_imag
        w2_imag = f_real * lam_imag + f_imag * lam_real
        grad = w_real * u1_imag - w_imag * u1_real
        pg_ref[r] = grad + (w2_real * u2_imag - w2_imag * u2_real)
        w2_ref[0, r] = w2_real
        w2_ref[1, r] = w2_imag
        write_edges(step, last, rows, r, [w2_real, w2_imag], *refs[16:])

    for_rows(rows, body)


def second_kernel(w_ref, w_prev, w_next, y_low_ref, y_high_ref, z_low_ref, z_high_ref, out_ref, *, rows):
    step = pl.program_id(0)
    last = pl.num_programs(0) - 1

    def body(r):
        for comp in range(2):
            below, above = neighbour_planes(w_ref, w_prev, w_next, y_low_ref, y_high_ref, rows, comp, comp, r,
                                            step, last)
            out_ref[comp, r] = plane_update(w_ref[comp, r], below, above,
                                            z_low_ref[comp, r], z_high_ref[comp, r])

    for_rows(rows, body)


def block_rows(length_y):
    rows = 8
    while length_y % rows:
        rows //= 2
    return rows


def field_specs(shape, rows):
    comps, length_y, length_z, length_x = shape
    cur = pl.BlockSpec((comps, rows, length_z, length_x), lambda i: (0, i, 0, 0))
    prev = pl.BlockSpec((comps, 1, length_z, length_x),
                        lambda i: (0, jnp.maximum(i * rows - 1, 0), 0, 0))
    nxt = pl.BlockSpec((comps, 1, length_z, length_x),
                       lambda i: (0, jnp.minimum(i * rows + rows, length_y - 1), 0, 0))
    return [cur, prev, nxt]


def send_edges(y_first, y_last, z_first, z_last):
    results = []
    for axis, first, last in (("gy", y_first, y_last), ("gz", z_first, z_last)):
        count = lax.axis_size(axis)
        up = [(i, (i + 1) % count) for i in range(count)]
        down = [(j, i) for i, j in up]
        if count == 2:
            both = lax.ppermute(jnp.stack([last, first]), axis, up)
            results.extend([both[0], both[1]])
        else:
            results.extend([lax.ppermute(last, axis, up), lax.ppermute(first, axis, down)])
    return results


def backward_sections(mag_start, mag_middle, adjoint_end, phase, labels):
    _, length_y, length_z, length_x = mag_start.shape
    rows = block_rows(length_y)
    grid = (length_y // rows,)
    plane = jax.ShapeDtypeStruct((length_y, length_z, length_x), jnp.float32)
    pair = jax.ShapeDtypeStruct((2, length_y, length_z, length_x), jnp.float32)
    cur = pl.BlockSpec((2, rows, length_z, length_x), lambda i: (0, i, 0, 0))
    cur_plane = pl.BlockSpec((rows, length_z, length_x), lambda i: (i, 0, 0))
    whole = lambda shape: pl.BlockSpec(shape, lambda i: (0,) * len(shape))
    zspec = lambda comps: pl.BlockSpec((comps, rows, 1, length_x), lambda i: (0, i, 0, 0))
    edge_shapes, edge_specs = edge_outputs(2, length_y, length_z, length_x, rows)
    six_shapes, six_specs = edge_outputs(6, length_y, length_z, length_x, rows)
    inputs = (mag_middle, mag_start, adjoint_end, phase, labels)
    edges = pl.pallas_call(
        functools.partial(edges_kernel, rows=rows),
        grid=grid,
        in_specs=[s for a in inputs for s in edge_specs_of(a.ndim, length_y, length_z, length_x, rows)],
        out_specs=six_specs,
        out_shape=six_shapes,
    )(*[a for a in inputs for _ in range(4)])
    halos = send_edges(*edges)
    factor, w_first = pl.pallas_call(
        functools.partial(factor_kernel, rows=rows),
        grid=grid,
        in_specs=[cur, cur_plane, cur_plane],
        out_specs=[cur, cur],
        out_shape=[pair, pair],
    )(adjoint_end, phase, labels)
    phase_grad, w_second, *w2_edges = pl.pallas_call(
        functools.partial(first_kernel, rows=rows),
        grid=grid,
        in_specs=field_specs(mag_middle.shape, rows) + field_specs(mag_start.shape, rows)
        + field_specs(w_first.shape, rows)
        + [cur, whole((6, length_z, length_x)), whole((6, length_z, length_x)), zspec(6), zspec(6)],
        out_specs=[cur_plane, cur] + edge_specs,
        out_shape=[plane, pair] + edge_shapes,
    )(mag_middle, mag_middle, mag_middle, mag_start, mag_start, mag_start,
      w_first, w_first, w_first, factor, *halos)
    halos = send_edges(*w2_edges)
    return phase_grad, functools.partial(finish_lambda, w_second, rows, grid, cur, whole, zspec, length_z, length_x), halos


def finish_lambda(w_second, rows, grid, cur, whole, zspec, length_z, length_x, halos):
    pair = jax.ShapeDtypeStruct(w_second.shape, jnp.float32)
    lam = pl.pallas_call(
        functools.partial(second_kernel, rows=rows),
        grid=grid,
        in_specs=field_specs(w_second.shape, rows)
        + [whole((2, length_z, length_x)), whole((2, length_z, length_x)), zspec(2), zspec(2)],
        out_specs=cur,
        out_shape=pair,
    )(w_second, w_second, w_second, *halos)
    return lam


def dipole_adjoint(phase_grad, finish, halos):
    count_y = lax.axis_size("gy")
    count_z = lax.axis_size("gz")
    parts = count_y * count_z
    block_y, block_z, length_x = phase_grad.shape
    length_y = block_y * count_y
    length_z = block_z * count_z
    block_x = length_x // parts
    pieces = 2 if block_x % 2 == 0 else 1
    piece_x = block_x // pieces
    table_x = cas_table(length_x).reshape(parts, pieces, piece_x, length_x)
    table_y = cas_table(length_y)
    table_z = cas_table(length_z)
    scale = 1.0 / (float(length_y) * float(length_z) * float(length_x))
    freq_y = signed_freq(jnp.arange(length_y, dtype=jnp.int32), length_y)
    freq_z = signed_freq(jnp.arange(length_z, dtype=jnp.int32), length_z)
    index = lax.axis_index("gy") * count_z + lax.axis_index("gz")
    sent = []
    for p in range(pieces):
        spec = along("sxn,yzn->sxyz", table_x[:, p], phase_grad)
        if p == 0:
            halos, spec = lax.optimization_barrier((halos, spec))
        sent.append(lax.all_to_all(spec, ("gy", "gz"), 0, 0, tiled=True))
        if p == 0:
            lam = finish(halos)
    result = None
    for p in range(pieces):
        spec = sent[p].reshape(count_y, count_z, piece_x, block_y, block_z)
        spec = spec.transpose(2, 0, 3, 1, 4).reshape(piece_x, length_y, length_z)
        spec = along("kz,xyz->xyk", table_z, spec)
        spec = along("ky,xyz->xkz", table_y, spec)
        first_x = index * block_x + p * piece_x
        freq_x = signed_freq(first_x + jnp.arange(piece_x, dtype=jnp.int32), length_x)
        kernel = dipole_block(freq_y[None, :, None], freq_z[None, None, :], freq_x[:, None, None])
        spec = spec * kernel
        spec = along("ky,xyz->xkz", table_y, spec)
        spec = along("kz,xyz->xyk", table_z, spec)
        spec = spec.reshape(piece_x, count_y, block_y, count_z, block_z)
        spec = spec.transpose(1, 3, 0, 2, 4).reshape(parts, piece_x, block_y, block_z)
        spec = lax.all_to_all(spec, ("gy", "gz"), 0, 0, tiled=True)
        part = along("sxn,sxyz->yzn", table_x[:, p], spec)
        result = part if result is None else result + part
    return result * scale, lam


def per_device(mag_start, mag_middle, adjoint_end, phase, labels):
    phase_grad, finish, halos = backward_sections(mag_start, mag_middle, adjoint_end, phase, labels)
    chi_grad, lam = dipole_adjoint(phase_grad, finish, halos)
    return (lam, chi_grad)


def solution(mesh):
    return jax.shard_map(
        per_device,
        mesh=mesh,
        in_specs=(
            P(None, "gy", "gz", None),
            P(None, "gy", "gz", None),
            P(None, "gy", "gz", None),
            P("gy", "gz", None),
            P("gy", "gz", None),
        ),
        out_specs=(P(None, "gy", "gz", None), P("gy", "gz", None)),
        check_vma=False,
    )
```

```python
import functools
import math

import jax
import numpy as np
import jax.numpy as jnp
from jax import lax
from jax.experimental import pallas as pl
from jax.experimental.pallas import tpu as pltpu
from jax.sharding import PartitionSpec as P


def signed_freq(index, length):
    return jnp.where(index < length // 2, index, index - length)


def dipole_block(freq_y, freq_z, freq_x):
    square_z = freq_z * freq_z
    total = freq_y * freq_y + square_z + freq_x * freq_x
    ratio = square_z.astype(jnp.float32) / jnp.maximum(total, 1).astype(jnp.float32)
    return jnp.where(total == 0, jnp.float32(0.0), jnp.float32(1.0 / 3.0) - ratio)


def cas_table(length):
    index = jnp.arange(length, dtype=jnp.int32)
    product = index[:, None] * index[None, :] % length
    angle = product.astype(jnp.float32) * (2.0 * math.pi / length)
    return jnp.cos(angle) + jnp.sin(angle)


def along(spec, table, values):
    return jnp.einsum(spec, table, values, precision=lax.Precision.HIGH)


def plane_update(centre, below, above, z_low, z_high):
    length_z, length_x = centre.shape
    row = lax.broadcasted_iota(jnp.int32, centre.shape, 0)
    up = jnp.where(row == 0, z_low, pltpu.roll(centre, 1, 0))
    down = jnp.where(row == length_z - 1, z_high, pltpu.roll(centre, length_z - 1, 0))
    total = below + above + up + down
    total = total + pltpu.roll(centre, 1, 1) + pltpu.roll(centre, length_x - 1, 1)
    return centre + 0.15 * (total - 6.0 * centre)


def neighbour_planes(cur_ref, prev_ref, next_ref, y_low_ref, y_high_ref, rows, field, comp, r, step, last):
    if isinstance(r, int) and r == 0:
        below = jnp.where(step == 0, y_low_ref[field], prev_ref[comp, 0])
    else:
        below = cur_ref[comp, r - 1]
    if isinstance(r, int) and r == rows - 1:
        above = jnp.where(step == last, y_high_ref[field], next_ref[comp, 0])
    else:
        above = cur_ref[comp, r + 1]
    return below, above


def write_edges(step, last, rows, r, values, y_first_ref, y_last_ref, z_first_ref, z_last_ref):
    for c, value in enumerate(values):
        z_first_ref[c, r] = value[0:1]
        z_last_ref[c, r] = value[value.shape[0] - 1:]
    if isinstance(r, int) and r == 0:
        @pl.when(step == 0)
        def _():
            for c, value in enumerate(values):
                y_first_ref[c] = value
    if isinstance(r, int) and r == rows - 1:
        @pl.when(step == last)
        def _():
            for c, value in enumerate(values):
                y_last_ref[c] = value


def for_rows(rows, body):
    body(0)
    if rows > 2:
        def loop_body(r, carry):
            body(r)
            return carry
        lax.fori_loop(1, rows - 1, loop_body, 0)
    if rows > 1:
        body(rows - 1)


def sin_cos(x):
    k = jnp.floor(x * (2.0 / math.pi) + 0.5)
    r = (x - k * 1.5707963705062866) - k * (-4.371139000186243e-08)
    r2 = r * r
    s = r + r * r2 * (-1.0 / 6.0 + r2 * (1.0 / 120.0 + r2 * (-1.0 / 5040.0 + r2 * (1.0 / 362880.0))))
    c = 1.0 + r2 * (-0.5 + r2 * (1.0 / 24.0 + r2 * (-1.0 / 720.0 + r2 * (1.0 / 40320.0
                                                                        + r2 * (-1.0 / 3628800.0)))))
    quadrant = k.astype(jnp.int32) & 3
    swap = (quadrant & 1) == 1
    sin_x = jnp.where(swap, c, s)
    cos_x = jnp.where(swap, s, c)
    sin_x = jnp.where(quadrant >= 2, -sin_x, sin_x)
    cos_x = jnp.where((quadrant == 1) | (quadrant == 2), -cos_x, cos_x)
    return sin_x, cos_x


def step_factor(labels, phase):
    decays = [float(np.exp(-np.float32(rate))) for rate in (0.02, 0.3, 0.6, 1.2)]
    decay = jnp.where(labels == 1, decays[1], decays[0])
    decay = jnp.where(labels == 2, decays[2], decay)
    decay = jnp.where(labels == 3, decays[3], decay).astype(jnp.float32)
    sin_p, cos_p = sin_cos(phase)
    return decay * cos_p, decay * sin_p


def first_w(lam_real, lam_imag, labels, phase):
    f_real, f_imag = step_factor(labels, phase)
    return (f_real * lam_real - f_imag * lam_imag, f_real * lam_imag + f_imag * lam_real), (f_real, f_imag)


def factor_kernel(lam_ref, phase_ref, labels_ref, factor_ref, w_ref, *, rows):
    def body(r, carry):
        (w_real, w_imag), (f_real, f_imag) = first_w(lam_ref[0, r], lam_ref[1, r], labels_ref[r], phase_ref[r])
        factor_ref[0, r] = f_real
        factor_ref[1, r] = f_imag
        w_ref[0, r] = w_real
        w_ref[1, r] = w_imag
        return carry
    lax.fori_loop(0, rows, body, 0)


def edges_kernel(*refs, rows):
    (mm_y0, mm_y1, mm_z0, mm_z1, ms_y0, ms_y1, ms_z0, ms_z1, lam_y0, lam_y1, lam_z0, lam_z1,
     ph_y0, ph_y1, ph_z0, ph_z1, lb_y0, lb_y1, lb_z0, lb_z1,
     y_first_ref, y_last_ref, z_first_ref, z_last_ref) = refs

    @pl.when(pl.program_id(0) == 0)
    def _():
        for out_ref, m1, m2, lam, ph, lb in ((y_first_ref, mm_y0, ms_y0, lam_y0, ph_y0, lb_y0),
                                           (y_last_ref, mm_y1, ms_y1, lam_y1, ph_y1, lb_y1)):
            (w_real, w_imag), _ = first_w(lam[0, 0], lam[1, 0], lb[0], ph[0])
            planes = [m1[0, 0], m1[1, 0], m2[0, 0], m2[1, 0], w_real, w_imag]
            for c, value in enumerate(planes):
                out_ref[c] = value

    def body(r, carry):
        for out_ref, m1, m2, lam, ph, lb, at in ((z_first_ref, mm_z0, ms_z0, lam_z0, ph_z0, lb_z0, 0),
                                               (z_last_ref, mm_z1, ms_z1, lam_z1, ph_z1, lb_z1, 7)):
            (w_real, w_imag), _ = first_w(lam[0, r], lam[1, r], lb[r], ph[r])
            tiles = [m1[0, r], m1[1, r], m2[0, r], m2[1, r], w_real, w_imag]
            for c, value in enumerate(tiles):
                out_ref[c, r] = value[at:at + 1]
        return carry
    lax.fori_loop(0, rows, body, 0)


def edge_specs_of(ndim, length_y, length_z, length_x, rows):
    lead = (2,) if ndim == 4 else ()
    zero = (0,) * len(lead)
    tiles = length_z // 8
    return [
        pl.BlockSpec(lead + (1, length_z, length_x), lambda i: zero + (0, 0, 0)),
        pl.BlockSpec(lead + (1, length_z, length_x), lambda i: zero + (length_y - 1, 0, 0)),
        pl.BlockSpec(lead + (rows, 8, length_x), lambda i: zero + (i, 0, 0)),
        pl.BlockSpec(lead + (rows, 8, length_x), lambda i: zero + (i, tiles - 1, 0)),
    ]


def edge_outputs(comps, length_y, length_z, length_x, rows):
    plane = jax.ShapeDtypeStruct((comps, length_z, length_x), jnp.float32)
    row = jax.ShapeDtypeStruct((comps, length_y, 1, length_x), jnp.float32)
    plane_spec = pl.BlockSpec((comps, length_z, length_x), lambda i: (0, 0, 0))
    row_spec = pl.BlockSpec((comps, rows, 1, length_x), lambda i: (0, i, 0, 0))
    return [plane, plane, row, row], [plane_spec, plane_spec, row_spec, row_spec]


def first_kernel(*refs, rows):
    (mm_ref, mm_prev, mm_next, ms_ref, ms_prev, ms_next, w_ref, w_prev, w_next,
     factor_ref, y_low_ref, y_high_ref, z_low_ref, z_high_ref, pg_ref, w2_ref) = refs[:16]
    step = pl.program_id(0)
    last = pl.num_programs(0) - 1
    fields = ((mm_ref, mm_prev, mm_next), (ms_ref, ms_prev, ms_next), (w_ref, w_prev, w_next))

    def body(r):
        new = []
        for f, (cur, prev, nxt) in enumerate(fields):
            pair = []
            for comp in range(2):
                below, above = neighbour_planes(cur, prev, nxt, y_low_ref, y_high_ref, rows, 2 * f + comp, comp, r,
                                                step, last)
                pair.append(plane_update(cur[comp, r], below, above,
                                         z_low_ref[2 * f + comp, r], z_high_ref[2 * f + comp, r]))
            new.append(pair)
        (u1_real, u1_imag), (u2_real, u2_imag), (lam_real, lam_imag) = new
        w_real = w_ref[0, r]
        w_imag = w_ref[1, r]
        f_real = factor_ref[0, r]
        f_imag = factor_ref[1, r]
        w2_real = f_real * lam_real - f_imag * lam_imag
        w2_imag = f_real * lam_imag + f_imag * lam_real
        grad = w_real * u1_imag - w_imag * u1_real
        pg_ref[r] = grad + (w2_real * u2_imag - w2_imag * u2_real)
        w2_ref[0, r] = w2_real
        w2_ref[1, r] = w2_imag
        write_edges(step, last, rows, r, [w2_real, w2_imag], *refs[16:])

    for_rows(rows, body)


def second_kernel(w_ref, w_prev, w_next, y_low_ref, y_high_ref, z_low_ref, z_high_ref, out_ref, *, rows):
    step = pl.program_id(0)
    last = pl.num_programs(0) - 1

    def body(r):
        for comp in range(2):
            below, above = neighbour_planes(w_ref, w_prev, w_next, y_low_ref, y_high_ref, rows, comp, comp, r,
                                            step, last)
            out_ref[comp, r] = plane_update(w_ref[comp, r], below, above,
                                            z_low_ref[comp, r], z_high_ref[comp, r])

    for_rows(rows, body)


def block_rows(length_y):
    rows = 8
    while length_y % rows:
        rows //= 2
    return rows


def field_specs(shape, rows):
    comps, length_y, length_z, length_x = shape
    cur = pl.BlockSpec((comps, rows, length_z, length_x), lambda i: (0, i, 0, 0))
    prev = pl.BlockSpec((comps, 1, length_z, length_x),
                        lambda i: (0, jnp.maximum(i * rows - 1, 0), 0, 0))
    nxt = pl.BlockSpec((comps, 1, length_z, length_x),
                       lambda i: (0, jnp.minimum(i * rows + rows, length_y - 1), 0, 0))
    return [cur, prev, nxt]


def send_edges(y_first, y_last, z_first, z_last):
    results = []
    for axis, first, last in (("gy", y_first, y_last), ("gz", z_first, z_last)):
        count = lax.axis_size(axis)
        up = [(i, (i + 1) % count) for i in range(count)]
        down = [(j, i) for i, j in up]
        if count == 2:
            both = lax.ppermute(jnp.stack([last, first]), axis, up)
            results.extend([both[0], both[1]])
        else:
            results.extend([lax.ppermute(last, axis, up), lax.ppermute(first, axis, down)])
    return results


def backward_sections(mag_start, mag_middle, adjoint_end, phase, labels):
    _, length_y, length_z, length_x = mag_start.shape
    rows = block_rows(length_y)
    grid = (length_y // rows,)
    plane = jax.ShapeDtypeStruct((length_y, length_z, length_x), jnp.float32)
    pair = jax.ShapeDtypeStruct((2, length_y, length_z, length_x), jnp.float32)
    cur = pl.BlockSpec((2, rows, length_z, length_x), lambda i: (0, i, 0, 0))
    cur_plane = pl.BlockSpec((rows, length_z, length_x), lambda i: (i, 0, 0))
    whole = lambda shape: pl.BlockSpec(shape, lambda i: (0,) * len(shape))
    zspec = lambda comps: pl.BlockSpec((comps, rows, 1, length_x), lambda i: (0, i, 0, 0))
    edge_shapes, edge_specs = edge_outputs(2, length_y, length_z, length_x, rows)
    six_shapes, six_specs = edge_outputs(6, length_y, length_z, length_x, rows)
    inputs = (mag_middle, mag_start, adjoint_end, phase, labels)
    edges = pl.pallas_call(
        functools.partial(edges_kernel, rows=rows),
        grid=grid,
        in_specs=[s for a in inputs for s in edge_specs_of(a.ndim, length_y, length_z, length_x, rows)],
        out_specs=six_specs,
        out_shape=six_shapes,
    )(*[a for a in inputs for _ in range(4)])
    halos = send_edges(*edges)
    factor, w_first = pl.pallas_call(
        functools.partial(factor_kernel, rows=rows),
        grid=grid,
        in_specs=[cur, cur_plane, cur_plane],
        out_specs=[cur, cur],
        out_shape=[pair, pair],
    )(adjoint_end, phase, labels)
    phase_grad, w_second, *w2_edges = pl.pallas_call(
        functools.partial(first_kernel, rows=rows),
        grid=grid,
        in_specs=field_specs(mag_middle.shape, rows) + field_specs(mag_start.shape, rows)
        + field_specs(w_first.shape, rows)
        + [cur, whole((6, length_z, length_x)), whole((6, length_z, length_x)), zspec(6), zspec(6)],
        out_specs=[cur_plane, cur] + edge_specs,
        out_shape=[plane, pair] + edge_shapes,
    )(mag_middle, mag_middle, mag_middle, mag_start, mag_start, mag_start,
      w_first, w_first, w_first, factor, *halos)
    halos = send_edges(*w2_edges)
    return phase_grad, functools.partial(finish_lambda, w_second, rows, grid, cur, whole, zspec, length_z, length_x), halos


def finish_lambda(w_second, rows, grid, cur, whole, zspec, length_z, length_x, halos):
    pair = jax.ShapeDtypeStruct(w_second.shape, jnp.float32)
    lam = pl.pallas_call(
        functools.partial(second_kernel, rows=rows),
        grid=grid,
        in_specs=field_specs(w_second.shape, rows)
        + [whole((2, length_z, length_x)), whole((2, length_z, length_x)), zspec(2), zspec(2)],
        out_specs=cur,
        out_shape=pair,
    )(w_second, w_second, w_second, *halos)
    return lam


def dipole_adjoint(phase_grad, finish, halos):
    count_y = lax.axis_size("gy")
    count_z = lax.axis_size("gz")
    parts = count_y * count_z
    block_y, block_z, length_x = phase_grad.shape
    length_y = block_y * count_y
    length_z = block_z * count_z
    block_x = length_x // parts
    pieces = 2 if block_x % 2 == 0 else 1
    piece_x = block_x // pieces
    table_x = cas_table(length_x).reshape(parts, pieces, piece_x, length_x)
    table_y = cas_table(length_y)
    table_z = cas_table(length_z)
    scale = 1.0 / (float(length_y) * float(length_z) * float(length_x))
    freq_y = signed_freq(jnp.arange(length_y, dtype=jnp.int32), length_y)
    freq_z = signed_freq(jnp.arange(length_z, dtype=jnp.int32), length_z)
    index = lax.axis_index("gy") * count_z + lax.axis_index("gz")
    sent = []
    for p in range(pieces):
        spec = along("sxn,yzn->sxyz", table_x[:, p], phase_grad)
        if p == 0:
            halos, spec = lax.optimization_barrier((halos, spec))
        sent.append(lax.all_to_all(spec, ("gy", "gz"), 0, 0, tiled=True))
        if p == 0:
            lam = finish(halos)
    result = None
    for p in range(pieces):
        spec = sent[p].reshape(count_y, count_z, piece_x, block_y, block_z)
        spec = spec.transpose(2, 0, 3, 1, 4).reshape(piece_x, length_y, length_z)
        spec = along("kz,xyz->xyk", table_z, spec)
        spec = along("ky,xyz->xkz", table_y, spec)
        first_x = index * block_x + p * piece_x
        freq_x = signed_freq(first_x + jnp.arange(piece_x, dtype=jnp.int32), length_x)
        kernel = dipole_block(freq_y[None, :, None], freq_z[None, None, :], freq_x[:, None, None])
        spec = spec * kernel
        spec = along("ky,xyz->xkz", table_y, spec)
        spec = along("kz,xyz->xyk", table_z, spec)
        spec = spec.reshape(piece_x, count_y, block_y, count_z, block_z)
        spec = spec.transpose(1, 3, 0, 2, 4).reshape(parts, piece_x, block_y, block_z)
        spec = lax.all_to_all(spec, ("gy", "gz"), 0, 0, tiled=True)
        part = along("sxn,sxyz->yzn", table_x[:, p], spec)
        result = part if result is None else result + part
    return result * scale, lam


def per_device(mag_start, mag_middle, adjoint_end, phase, labels):
    phase_grad, finish, halos = backward_sections(mag_start, mag_middle, adjoint_end, phase, labels)
    chi_grad, lam = dipole_adjoint(phase_grad, finish, halos)
    return (lam, chi_grad)


def solution(mesh):
    return jax.shard_map(
        per_device,
        mesh=mesh,
        in_specs=(
            P(None, "gy", "gz", None),
            P(None, "gy", "gz", None),
            P(None, "gy", "gz", None),
            P("gy", "gz", None),
            P("gy", "gz", None),
        ),
        out_specs=(P(None, "gy", "gz", None), P("gy", "gz", None)),
        check_vma=False,
    )
```

```python
import functools
import math

import jax
import numpy as np
import jax.numpy as jnp
from jax import lax
from jax.experimental import pallas as pl
from jax.experimental.pallas import tpu as pltpu
from jax.sharding import PartitionSpec as P


def signed_freq(index, length):
    return jnp.where(index < length // 2, index, index - length)


def dipole_block(freq_y, freq_z, freq_x):
    square_z = freq_z * freq_z
    total = freq_y * freq_y + square_z + freq_x * freq_x
    ratio = square_z.astype(jnp.float32) / jnp.maximum(total, 1).astype(jnp.float32)
    return jnp.where(total == 0, jnp.float32(0.0), jnp.float32(1.0 / 3.0) - ratio)


def cas_table(length):
    index = jnp.arange(length, dtype=jnp.int32)
    product = index[:, None] * index[None, :] % length
    angle = product.astype(jnp.float32) * (2.0 * math.pi / length)
    return jnp.cos(angle) + jnp.sin(angle)


def along(spec, table, values):
    return jnp.einsum(spec, table, values, precision=lax.Precision.HIGH)


def plane_update(centre, below, above, z_low, z_high):
    length_z, length_x = centre.shape
    row = lax.broadcasted_iota(jnp.int32, centre.shape, 0)
    up = jnp.where(row == 0, z_low, pltpu.roll(centre, 1, 0))
    down = jnp.where(row == length_z - 1, z_high, pltpu.roll(centre, length_z - 1, 0))
    total = below + above + up + down
    total = total + pltpu.roll(centre, 1, 1) + pltpu.roll(centre, length_x - 1, 1)
    return centre + 0.15 * (total - 6.0 * centre)


def neighbour_planes(cur_ref, prev_ref, next_ref, y_low_ref, y_high_ref, rows, field, comp, r, step, last):
    if isinstance(r, int) and r == 0:
        below = jnp.where(step == 0, y_low_ref[field], prev_ref[comp, 0])
    else:
        below = cur_ref[comp, r - 1]
    if isinstance(r, int) and r == rows - 1:
        above = jnp.where(step == last, y_high_ref[field], next_ref[comp, 0])
    else:
        above = cur_ref[comp, r + 1]
    return below, above


def write_edges(step, last, rows, r, values, y_first_ref, y_last_ref, z_first_ref, z_last_ref):
    for c, value in enumerate(values):
        z_first_ref[c, r] = value[0:1]
        z_last_ref[c, r] = value[value.shape[0] - 1:]
    if isinstance(r, int) and r == 0:
        @pl.when(step == 0)
        def _():
            for c, value in enumerate(values):
                y_first_ref[c] = value
    if isinstance(r, int) and r == rows - 1:
        @pl.when(step == last)
        def _():
            for c, value in enumerate(values):
                y_last_ref[c] = value


def for_rows(rows, body):
    body(0)
    if rows > 2:
        def loop_body(r, carry):
            body(r)
            return carry
        lax.fori_loop(1, rows - 1, loop_body, 0)
    if rows > 1:
        body(rows - 1)


def sin_cos(x):
    k = jnp.floor(x * (2.0 / math.pi) + 0.5)
    r = (x - k * 1.5707963705062866) - k * (-4.371139000186243e-08)
    r2 = r * r
    s = r + r * r2 * (-1.0 / 6.0 + r2 * (1.0 / 120.0 + r2 * (-1.0 / 5040.0 + r2 * (1.0 / 362880.0))))
    c = 1.0 + r2 * (-0.5 + r2 * (1.0 / 24.0 + r2 * (-1.0 / 720.0 + r2 * (1.0 / 40320.0
                                                                        + r2 * (-1.0 / 3628800.0)))))
    quadrant = k.astype(jnp.int32) & 3
    swap = (quadrant & 1) == 1
    sin_x = jnp.where(swap, c, s)
    cos_x = jnp.where(swap, s, c)
    sin_x = jnp.where(quadrant >= 2, -sin_x, sin_x)
    cos_x = jnp.where((quadrant == 1) | (quadrant == 2), -cos_x, cos_x)
    return sin_x, cos_x


def step_factor(labels, phase):
    decays = [float(np.exp(-np.float32(rate))) for rate in (0.02, 0.3, 0.6, 1.2)]
    decay = jnp.where(labels == 1, decays[1], decays[0])
    decay = jnp.where(labels == 2, decays[2], decay)
    decay = jnp.where(labels == 3, decays[3], decay).astype(jnp.float32)
    sin_p, cos_p = sin_cos(phase)
    return decay * cos_p, decay * sin_p


def first_w(lam_real, lam_imag, labels, phase):
    f_real, f_imag = step_factor(labels, phase)
    return (f_real * lam_real - f_imag * lam_imag, f_real * lam_imag + f_imag * lam_real), (f_real, f_imag)


def factor_kernel(lam_ref, phase_ref, labels_ref, factor_ref, w_ref, *, rows):
    def body(r, carry):
        (w_real, w_imag), (f_real, f_imag) = first_w(lam_ref[0, r], lam_ref[1, r], labels_ref[r], phase_ref[r])
        factor_ref[0, r] = f_real
        factor_ref[1, r] = f_imag
        w_ref[0, r] = w_real
        w_ref[1, r] = w_imag
        return carry
    lax.fori_loop(0, rows, body, 0)


def edges_kernel(*refs, rows):
    (mm_y0, mm_y1, mm_z0, mm_z1, ms_y0, ms_y1, ms_z0, ms_z1, lam_y0, lam_y1, lam_z0, lam_z1,
     ph_y0, ph_y1, ph_z0, ph_z1, lb_y0, lb_y1, lb_z0, lb_z1,
     y_first_ref, y_last_ref, z_first_ref, z_last_ref) = refs

    @pl.when(pl.program_id(0) == 0)
    def _():
        for out_ref, m1, m2, lam, ph, lb in ((y_first_ref, mm_y0, ms_y0, lam_y0, ph_y0, lb_y0),
                                           (y_last_ref, mm_y1, ms_y1, lam_y1, ph_y1, lb_y1)):
            (w_real, w_imag), _ = first_w(lam[0, 0], lam[1, 0], lb[0], ph[0])
            planes = [m1[0, 0], m1[1, 0], m2[0, 0], m2[1, 0], w_real, w_imag]
            for c, value in enumerate(planes):
                out_ref[c] = value

    def body(r, carry):
        for out_ref, m1, m2, lam, ph, lb, at in ((z_first_ref, mm_z0, ms_z0, lam_z0, ph_z0, lb_z0, 0),
                                               (z_last_ref, mm_z1, ms_z1, lam_z1, ph_z1, lb_z1, 7)):
            (w_real, w_imag), _ = first_w(lam[0, r], lam[1, r], lb[r], ph[r])
            tiles = [m1[0, r], m1[1, r], m2[0, r], m2[1, r], w_real, w_imag]
            for c, value in enumerate(tiles):
                out_ref[c, r] = value[at:at + 1]
        return carry
    lax.fori_loop(0, rows, body, 0)


def edge_specs_of(ndim, length_y, length_z, length_x, rows):
    lead = (2,) if ndim == 4 else ()
    zero = (0,) * len(lead)
    tiles = length_z // 8
    return [
        pl.BlockSpec(lead + (1, length_z, length_x), lambda i: zero + (0, 0, 0)),
        pl.BlockSpec(lead + (1, length_z, length_x), lambda i: zero + (length_y - 1, 0, 0)),
        pl.BlockSpec(lead + (rows, 8, length_x), lambda i: zero + (i, 0, 0)),
        pl.BlockSpec(lead + (rows, 8, length_x), lambda i: zero + (i, tiles - 1, 0)),
    ]


def edge_outputs(comps, length_y, length_z, length_x, rows):
    plane = jax.ShapeDtypeStruct((comps, length_z, length_x), jnp.float32)
    row = jax.ShapeDtypeStruct((comps, length_y, 1, length_x), jnp.float32)
    plane_spec = pl.BlockSpec((comps, length_z, length_x), lambda i: (0, 0, 0))
    row_spec = pl.BlockSpec((comps, rows, 1, length_x), lambda i: (0, i, 0, 0))
    return [plane, plane, row, row], [plane_spec, plane_spec, row_spec, row_spec]


def first_kernel(*refs, rows, base, last):
    (mm_ref, mm_prev, mm_next, ms_ref, ms_prev, ms_next, w_ref, w_prev, w_next,
     factor_ref, y_low_ref, y_high_ref, z_low_ref, z_high_ref, pg_ref, w2_ref) = refs[:16]
    step = pl.program_id(0) + base
    fields = ((mm_ref, mm_prev, mm_next), (ms_ref, ms_prev, ms_next), (w_ref, w_prev, w_next))

    def body(r):
        new = []
        for f, (cur, prev, nxt) in enumerate(fields):
            pair = []
            for comp in range(2):
                below, above = neighbour_planes(cur, prev, nxt, y_low_ref, y_high_ref, rows, 2 * f + comp, comp, r,
                                                step, last)
                pair.append(plane_update(cur[comp, r], below, above,
                                         z_low_ref[2 * f + comp, r], z_high_ref[2 * f + comp, r]))
            new.append(pair)
        (u1_real, u1_imag), (u2_real, u2_imag), (lam_real, lam_imag) = new
        w_real = w_ref[0, r]
        w_imag = w_ref[1, r]
        f_real = factor_ref[0, r]
        f_imag = factor_ref[1, r]
        w2_real = f_real * lam_real - f_imag * lam_imag
        w2_imag = f_real * lam_imag + f_imag * lam_real
        grad = w_real * u1_imag - w_imag * u1_real
        pg_ref[r] = grad + (w2_real * u2_imag - w2_imag * u2_real)
        w2_ref[0, r] = w2_real
        w2_ref[1, r] = w2_imag
        write_edges(step, last, rows, r, [w2_real, w2_imag], *refs[16:])

    for_rows(rows, body)


def second_kernel(w_ref, w_prev, w_next, y_low_ref, y_high_ref, z_low_ref, z_high_ref, out_ref, *, rows):
    step = pl.program_id(0)
    last = pl.num_programs(0) - 1

    def body(r):
        for comp in range(2):
            below, above = neighbour_planes(w_ref, w_prev, w_next, y_low_ref, y_high_ref, rows, comp, comp, r,
                                            step, last)
            out_ref[comp, r] = plane_update(w_ref[comp, r], below, above,
                                            z_low_ref[comp, r], z_high_ref[comp, r])

    for_rows(rows, body)


def block_rows(length_y):
    rows = 8
    while length_y % rows:
        rows //= 2
    return rows


def field_specs(shape, rows, base=0):
    comps, length_y, length_z, length_x = shape
    cur = pl.BlockSpec((comps, rows, length_z, length_x), lambda i: (0, i + base, 0, 0))
    prev = pl.BlockSpec((comps, 1, length_z, length_x),
                        lambda i: (0, jnp.maximum((i + base) * rows - 1, 0), 0, 0))
    nxt = pl.BlockSpec((comps, 1, length_z, length_x),
                       lambda i: (0, jnp.minimum((i + base) * rows + rows, length_y - 1), 0, 0))
    return [cur, prev, nxt]


def send_edges(y_first, y_last, z_first, z_last):
    results = []
    for axis, first, last in (("gy", y_first, y_last), ("gz", z_first, z_last)):
        count = lax.axis_size(axis)
        up = [(i, (i + 1) % count) for i in range(count)]
        down = [(j, i) for i, j in up]
        if count == 2:
            both = lax.ppermute(jnp.stack([last, first]), axis, up)
            results.extend([both[0], both[1]])
        else:
            results.extend([lax.ppermute(last, axis, up), lax.ppermute(first, axis, down)])
    return results


def backward_sections(mag_start, mag_middle, adjoint_end, phase, labels):
    _, length_y, length_z, length_x = mag_start.shape
    rows = block_rows(length_y)
    grid = (length_y // rows,)
    plane = jax.ShapeDtypeStruct((length_y, length_z, length_x), jnp.float32)
    pair = jax.ShapeDtypeStruct((2, length_y, length_z, length_x), jnp.float32)
    cur = pl.BlockSpec((2, rows, length_z, length_x), lambda i: (0, i, 0, 0))
    cur_plane = pl.BlockSpec((rows, length_z, length_x), lambda i: (i, 0, 0))
    whole = lambda shape: pl.BlockSpec(shape, lambda i: (0,) * len(shape))
    zspec = lambda comps: pl.BlockSpec((comps, rows, 1, length_x), lambda i: (0, i, 0, 0))
    edge_shapes, edge_specs = edge_outputs(2, length_y, length_z, length_x, rows)
    six_shapes, six_specs = edge_outputs(6, length_y, length_z, length_x, rows)
    inputs = (mag_middle, mag_start, adjoint_end, phase, labels)
    edges = pl.pallas_call(
        functools.partial(edges_kernel, rows=rows),
        grid=grid,
        in_specs=[s for a in inputs for s in edge_specs_of(a.ndim, length_y, length_z, length_x, rows)],
        out_specs=six_specs,
        out_shape=six_shapes,
    )(*[a for a in inputs for _ in range(4)])
    halos = send_edges(*edges)
    factor, w_first = pl.pallas_call(
        functools.partial(factor_kernel, rows=rows),
        grid=grid,
        in_specs=[cur, cur_plane, cur_plane],
        out_specs=[cur, cur],
        out_shape=[pair, pair],
    )(adjoint_end, phase, labels)
    blocks = length_y // rows
    halves = 2 if blocks % 2 == 0 else 1
    half_blocks = blocks // halves
    half_y = half_blocks * rows
    half_edge_shapes, half_edge_specs = edge_outputs(2, half_y, length_z, length_x, rows)
    grads, seconds, y_firsts, y_lasts, z_firsts, z_lasts = [], [], [], [], [], []
    for h in range(halves):
        base = h * half_blocks
        grad, second, y_first, y_last, z_first, z_last = pl.pallas_call(
            functools.partial(first_kernel, rows=rows, base=base, last=blocks - 1),
            grid=(half_blocks,),
            in_specs=field_specs(mag_middle.shape, rows, base) + field_specs(mag_start.shape, rows, base)
            + field_specs(w_first.shape, rows, base)
            + [pl.BlockSpec((2, rows, length_z, length_x), lambda i, b=base: (0, i + b, 0, 0)),
               whole((6, length_z, length_x)), whole((6, length_z, length_x)),
               pl.BlockSpec((6, rows, 1, length_x), lambda i, b=base: (0, i + b, 0, 0)),
               pl.BlockSpec((6, rows, 1, length_x), lambda i, b=base: (0, i + b, 0, 0))],
            out_specs=[cur_plane, cur] + half_edge_specs,
            out_shape=[jax.ShapeDtypeStruct((half_y, length_z, length_x), jnp.float32),
                       jax.ShapeDtypeStruct((2, half_y, length_z, length_x), jnp.float32)] + half_edge_shapes,
        )(mag_middle, mag_middle, mag_middle, mag_start, mag_start, mag_start,
          w_first, w_first, w_first, factor, *halos)
        grads.append(grad)
        seconds.append(second)
        y_firsts.append(y_first)
        y_lasts.append(y_last)
        z_firsts.append(z_first)
        z_lasts.append(z_last)
    w_second = jnp.concatenate(seconds, axis=1) if halves > 1 else seconds[0]
    w2_edges = [y_firsts[0], y_lasts[-1], jnp.concatenate(z_firsts, axis=1), jnp.concatenate(z_lasts, axis=1)]
    halos = send_edges(*w2_edges)
    return grads, functools.partial(finish_lambda, w_second, rows, grid, cur, whole, zspec, length_z, length_x), halos


def finish_lambda(w_second, rows, grid, cur, whole, zspec, length_z, length_x, halos):
    pair = jax.ShapeDtypeStruct(w_second.shape, jnp.float32)
    lam = pl.pallas_call(
        functools.partial(second_kernel, rows=rows),
        grid=grid,
        in_specs=field_specs(w_second.shape, rows)
        + [whole((2, length_z, length_x)), whole((2, length_z, length_x)), zspec(2), zspec(2)],
        out_specs=cur,
        out_shape=pair,
    )(w_second, w_second, w_second, *halos)
    return lam


def dipole_adjoint(grads, finish, halos):
    count_y = lax.axis_size("gy")
    count_z = lax.axis_size("gz")
    parts = count_y * count_z
    halves = len(grads)
    half_y, block_z, length_x = grads[0].shape
    block_y = half_y * halves
    length_y = block_y * count_y
    length_z = block_z * count_z
    block_x = length_x // parts
    pieces = 2 if block_x % 2 == 0 else 1
    piece_x = block_x // pieces
    table = cas_table(length_x)
    table_x = table.reshape(parts, pieces, piece_x, length_x)
    table_y = cas_table(length_y)
    table_z = cas_table(length_z)
    scale = 1.0 / (float(length_y) * float(length_z) * float(length_x))
    freq_y = signed_freq(jnp.arange(length_y, dtype=jnp.int32), length_y)
    freq_z = signed_freq(jnp.arange(length_z, dtype=jnp.int32), length_z)
    index = lax.axis_index("gy") * count_z + lax.axis_index("gz")
    sent = []
    for h in range(halves):
        spec = along("kn,yzn->kyz", table, grads[h]).reshape(parts, block_x, half_y, block_z)
        if h == halves - 1:
            halos, spec = lax.optimization_barrier((halos, spec))
        sent.append(lax.all_to_all(spec, ("gy", "gz"), 0, 0, tiled=True))
    lam = finish(halos)
    spec = jnp.stack(sent).reshape(halves, count_y, count_z, block_x, half_y, block_z)
    whole_spec = spec.transpose(3, 1, 0, 4, 2, 5).reshape(block_x, length_y, length_z)
    result = None
    for p in range(pieces):
        spec = whole_spec[p * piece_x:(p + 1) * piece_x]
        spec = along("kz,xyz->xyk", table_z, spec)
        spec = along("ky,xyz->xkz", table_y, spec)
        first_x = index * block_x + p * piece_x
        freq_x = signed_freq(first_x + jnp.arange(piece_x, dtype=jnp.int32), length_x)
        kernel = dipole_block(freq_y[None, :, None], freq_z[None, None, :], freq_x[:, None, None])
        spec = spec * kernel
        spec = along("ky,xyz->xkz", table_y, spec)
        spec = along("kz,xyz->xyk", table_z, spec)
        spec = spec.reshape(piece_x, count_y, block_y, count_z, block_z)
        spec = spec.transpose(1, 3, 0, 2, 4).reshape(parts, piece_x, block_y, block_z)
        spec = lax.all_to_all(spec, ("gy", "gz"), 0, 0, tiled=True)
        part = along("sxn,sxyz->yzn", table_x[:, p], spec)
        result = part if result is None else result + part
    return result * scale, lam


def per_device(mag_start, mag_middle, adjoint_end, phase, labels):
    grads, finish, halos = backward_sections(mag_start, mag_middle, adjoint_end, phase, labels)
    chi_grad, lam = dipole_adjoint(grads, finish, halos)
    return (lam, chi_grad)


def solution(mesh):
    return jax.shard_map(
        per_device,
        mesh=mesh,
        in_specs=(
            P(None, "gy", "gz", None),
            P(None, "gy", "gz", None),
            P(None, "gy", "gz", None),
            P("gy", "gz", None),
            P("gy", "gz", None),
        ),
        out_specs=(P(None, "gy", "gz", None), P("gy", "gz", None)),
        check_vma=False,
    )
```

```python
import functools
import math

import jax
import numpy as np
import jax.numpy as jnp
from jax import lax
from jax.experimental import pallas as pl
from jax.experimental.pallas import tpu as pltpu
from jax.sharding import PartitionSpec as P


def signed_freq(index, length):
    return jnp.where(index < length // 2, index, index - length)


def dipole_block(freq_y, freq_z, freq_x):
    square_z = freq_z * freq_z
    total = freq_y * freq_y + square_z + freq_x * freq_x
    ratio = square_z.astype(jnp.float32) / jnp.maximum(total, 1).astype(jnp.float32)
    return jnp.where(total == 0, jnp.float32(0.0), jnp.float32(1.0 / 3.0) - ratio)


def cas_table(length):
    index = jnp.arange(length, dtype=jnp.int32)
    product = index[:, None] * index[None, :] % length
    angle = product.astype(jnp.float32) * (2.0 * math.pi / length)
    return jnp.cos(angle) + jnp.sin(angle)


def along(spec, table, values):
    return jnp.einsum(spec, table, values, precision=lax.Precision.HIGH)


def plane_update(centre, below, above, z_low, z_high):
    length_z, length_x = centre.shape
    up = pltpu.roll(centre, 1, 0)
    down = pltpu.roll(centre, length_z - 1, 0)
    if length_z > 8:
        row = lax.broadcasted_iota(jnp.int32, (8, length_x), 0)
        up = jnp.concatenate([jnp.where(row == 0, z_low, up[:8]), up[8:]], axis=0)
        down = jnp.concatenate([down[:length_z - 8], jnp.where(row == 7, z_high, down[length_z - 8:])], axis=0)
    else:
        row = lax.broadcasted_iota(jnp.int32, centre.shape, 0)
        up = jnp.where(row == 0, z_low, up)
        down = jnp.where(row == length_z - 1, z_high, down)
    total = below + above + up + down
    total = total + pltpu.roll(centre, 1, 1) + pltpu.roll(centre, length_x - 1, 1)
    return centre + 0.15 * (total - 6.0 * centre)


def neighbour_planes(cur_ref, prev_ref, next_ref, y_low_ref, y_high_ref, rows, field, comp, r, step, last):
    if isinstance(r, int) and r == 0:
        below = jnp.where(step == 0, y_low_ref[field], prev_ref[comp, 0])
    else:
        below = cur_ref[comp, r - 1]
    if isinstance(r, int) and r == rows - 1:
        above = jnp.where(step == last, y_high_ref[field], next_ref[comp, 0])
    else:
        above = cur_ref[comp, r + 1]
    return below, above


def write_edges(step, last, rows, r, values, y_first_ref, y_last_ref, z_first_ref, z_last_ref):
    for c, value in enumerate(values):
        z_first_ref[c, r] = value[0:1]
        z_last_ref[c, r] = value[value.shape[0] - 1:]
    if isinstance(r, int) and r == 0:
        @pl.when(step == 0)
        def _():
            for c, value in enumerate(values):
                y_first_ref[c] = value
    if isinstance(r, int) and r == rows - 1:
        @pl.when(step == last)
        def _():
            for c, value in enumerate(values):
                y_last_ref[c] = value


def for_rows(rows, body):
    body(0)
    if rows > 2:
        def loop_body(r, carry):
            body(r)
            return carry
        lax.fori_loop(1, rows - 1, loop_body, 0)
    if rows > 1:
        body(rows - 1)


def sin_cos(x):
    k = jnp.floor(x * (2.0 / math.pi) + 0.5)
    r = (x - k * 1.5707963705062866) - k * (-4.371139000186243e-08)
    r2 = r * r
    s = r + r * r2 * (-1.0 / 6.0 + r2 * (1.0 / 120.0 + r2 * (-1.0 / 5040.0 + r2 * (1.0 / 362880.0))))
    c = 1.0 + r2 * (-0.5 + r2 * (1.0 / 24.0 + r2 * (-1.0 / 720.0 + r2 * (1.0 / 40320.0
                                                                        + r2 * (-1.0 / 3628800.0)))))
    quadrant = k.astype(jnp.int32) & 3
    swap = (quadrant & 1) == 1
    sin_x = jnp.where(swap, c, s)
    cos_x = jnp.where(swap, s, c)
    sin_x = jnp.where(quadrant >= 2, -sin_x, sin_x)
    cos_x = jnp.where((quadrant == 1) | (quadrant == 2), -cos_x, cos_x)
    return sin_x, cos_x


def step_factor(labels, phase):
    decays = [float(np.exp(-np.float32(rate))) for rate in (0.02, 0.3, 0.6, 1.2)]
    decay = jnp.where(labels == 1, decays[1], decays[0])
    decay = jnp.where(labels == 2, decays[2], decay)
    decay = jnp.where(labels == 3, decays[3], decay).astype(jnp.float32)
    sin_p, cos_p = sin_cos(phase)
    return decay * cos_p, decay * sin_p


def first_w(lam_real, lam_imag, labels, phase):
    f_real, f_imag = step_factor(labels, phase)
    return (f_real * lam_real - f_imag * lam_imag, f_real * lam_imag + f_imag * lam_real), (f_real, f_imag)


def factor_kernel(lam_ref, phase_ref, labels_ref, factor_ref, w_ref, *, rows):
    def body(r, carry):
        (w_real, w_imag), (f_real, f_imag) = first_w(lam_ref[0, r], lam_ref[1, r], labels_ref[r], phase_ref[r])
        factor_ref[0, r] = f_real
        factor_ref[1, r] = f_imag
        w_ref[0, r] = w_real
        w_ref[1, r] = w_imag
        return carry
    lax.fori_loop(0, rows, body, 0)


def edges_kernel(*refs, rows):
    (mm_y0, mm_y1, mm_z0, mm_z1, ms_y0, ms_y1, ms_z0, ms_z1, lam_y0, lam_y1, lam_z0, lam_z1,
     ph_y0, ph_y1, ph_z0, ph_z1, lb_y0, lb_y1, lb_z0, lb_z1,
     y_first_ref, y_last_ref, z_first_ref, z_last_ref) = refs

    @pl.when(pl.program_id(0) == 0)
    def _():
        for out_ref, m1, m2, lam, ph, lb in ((y_first_ref, mm_y0, ms_y0, lam_y0, ph_y0, lb_y0),
                                           (y_last_ref, mm_y1, ms_y1, lam_y1, ph_y1, lb_y1)):
            (w_real, w_imag), _ = first_w(lam[0, 0], lam[1, 0], lb[0], ph[0])
            planes = [m1[0, 0], m1[1, 0], m2[0, 0], m2[1, 0], w_real, w_imag]
            for c, value in enumerate(planes):
                out_ref[c] = value

    def body(r, carry):
        for out_ref, m1, m2, lam, ph, lb, at in ((z_first_ref, mm_z0, ms_z0, lam_z0, ph_z0, lb_z0, 0),
                                               (z_last_ref, mm_z1, ms_z1, lam_z1, ph_z1, lb_z1, 7)):
            (w_real, w_imag), _ = first_w(lam[0, r], lam[1, r], lb[r], ph[r])
            tiles = [m1[0, r], m1[1, r], m2[0, r], m2[1, r], w_real, w_imag]
            for c, value in enumerate(tiles):
                out_ref[c, r] = value[at:at + 1]
        return carry
    lax.fori_loop(0, rows, body, 0)


def edge_specs_of(ndim, length_y, length_z, length_x, rows):
    lead = (2,) if ndim == 4 else ()
    zero = (0,) * len(lead)
    tiles = length_z // 8
    return [
        pl.BlockSpec(lead + (1, length_z, length_x), lambda i: zero + (0, 0, 0)),
        pl.BlockSpec(lead + (1, length_z, length_x), lambda i: zero + (length_y - 1, 0, 0)),
        pl.BlockSpec(lead + (rows, 8, length_x), lambda i: zero + (i, 0, 0)),
        pl.BlockSpec(lead + (rows, 8, length_x), lambda i: zero + (i, tiles - 1, 0)),
    ]


def edge_outputs(comps, length_y, length_z, length_x, rows):
    plane = jax.ShapeDtypeStruct((comps, length_z, length_x), jnp.float32)
    row = jax.ShapeDtypeStruct((comps, length_y, 1, length_x), jnp.float32)
    plane_spec = pl.BlockSpec((comps, length_z, length_x), lambda i: (0, 0, 0))
    row_spec = pl.BlockSpec((comps, rows, 1, length_x), lambda i: (0, i, 0, 0))
    return [plane, plane, row, row], [plane_spec, plane_spec, row_spec, row_spec]


def first_kernel(*refs, rows):
    (mm_ref, mm_prev, mm_next, ms_ref, ms_prev, ms_next, w_ref, w_prev, w_next,
     factor_ref, y_low_ref, y_high_ref, z_low_ref, z_high_ref, pg_ref, w2_ref) = refs[:16]
    step = pl.program_id(0)
    last = pl.num_programs(0) - 1
    fields = ((mm_ref, mm_prev, mm_next), (ms_ref, ms_prev, ms_next), (w_ref, w_prev, w_next))

    def body(r):
        new = []
        for f, (cur, prev, nxt) in enumerate(fields):
            pair = []
            for comp in range(2):
                below, above = neighbour_planes(cur, prev, nxt, y_low_ref, y_high_ref, rows, 2 * f + comp, comp, r,
                                                step, last)
                pair.append(plane_update(cur[comp, r], below, above,
                                         z_low_ref[2 * f + comp, r], z_high_ref[2 * f + comp, r]))
            new.append(pair)
        (u1_real, u1_imag), (u2_real, u2_imag), (lam_real, lam_imag) = new
        w_real = w_ref[0, r]
        w_imag = w_ref[1, r]
        f_real = factor_ref[0, r]
        f_imag = factor_ref[1, r]
        w2_real = f_real * lam_real - f_imag * lam_imag
        w2_imag = f_real * lam_imag + f_imag * lam_real
        grad = w_real * u1_imag - w_imag * u1_real
        pg_ref[r] = grad + (w2_real * u2_imag - w2_imag * u2_real)
        w2_ref[0, r] = w2_real
        w2_ref[1, r] = w2_imag
        write_edges(step, last, rows, r, [w2_real, w2_imag], *refs[16:])

    for_rows(rows, body)


def second_kernel(w_ref, w_prev, w_next, y_low_ref, y_high_ref, z_low_ref, z_high_ref, out_ref, *, rows):
    step = pl.program_id(0)
    last = pl.num_programs(0) - 1

    def body(r):
        for comp in range(2):
            below, above = neighbour_planes(w_ref, w_prev, w_next, y_low_ref, y_high_ref, rows, comp, comp, r,
                                            step, last)
            out_ref[comp, r] = plane_update(w_ref[comp, r], below, above,
                                            z_low_ref[comp, r], z_high_ref[comp, r])

    for_rows(rows, body)


def block_rows(length_y):
    rows = 8
    while length_y % rows:
        rows //= 2
    return rows


def field_specs(shape, rows):
    comps, length_y, length_z, length_x = shape
    cur = pl.BlockSpec((comps, rows, length_z, length_x), lambda i: (0, i, 0, 0))
    prev = pl.BlockSpec((comps, 1, length_z, length_x),
                        lambda i: (0, jnp.maximum(i * rows - 1, 0), 0, 0))
    nxt = pl.BlockSpec((comps, 1, length_z, length_x),
                       lambda i: (0, jnp.minimum(i * rows + rows, length_y - 1), 0, 0))
    return [cur, prev, nxt]


def send_edges(y_first, y_last, z_first, z_last):
    results = []
    for axis, first, last in (("gy", y_first, y_last), ("gz", z_first, z_last)):
        count = lax.axis_size(axis)
        up = [(i, (i + 1) % count) for i in range(count)]
        down = [(j, i) for i, j in up]
        if count == 2:
            both = lax.ppermute(jnp.stack([last, first]), axis, up)
            results.extend([both[0], both[1]])
        else:
            results.extend([lax.ppermute(last, axis, up), lax.ppermute(first, axis, down)])
    return results


def backward_sections(mag_start, mag_middle, adjoint_end, phase, labels):
    _, length_y, length_z, length_x = mag_start.shape
    rows = block_rows(length_y)
    grid = (length_y // rows,)
    plane = jax.ShapeDtypeStruct((length_y, length_z, length_x), jnp.float32)
    pair = jax.ShapeDtypeStruct((2, length_y, length_z, length_x), jnp.float32)
    cur = pl.BlockSpec((2, rows, length_z, length_x), lambda i: (0, i, 0, 0))
    cur_plane = pl.BlockSpec((rows, length_z, length_x), lambda i: (i, 0, 0))
    whole = lambda shape: pl.BlockSpec(shape, lambda i: (0,) * len(shape))
    zspec = lambda comps: pl.BlockSpec((comps, rows, 1, length_x), lambda i: (0, i, 0, 0))
    edge_shapes, edge_specs = edge_outputs(2, length_y, length_z, length_x, rows)
    six_shapes, six_specs = edge_outputs(6, length_y, length_z, length_x, rows)
    inputs = (mag_middle, mag_start, adjoint_end, phase, labels)
    edges = pl.pallas_call(
        functools.partial(edges_kernel, rows=rows),
        grid=grid,
        in_specs=[s for a in inputs for s in edge_specs_of(a.ndim, length_y, length_z, length_x, rows)],
        out_specs=six_specs,
        out_shape=six_shapes,
    )(*[a for a in inputs for _ in range(4)])
    halos = send_edges(*edges)
    factor, w_first = pl.pallas_call(
        functools.partial(factor_kernel, rows=rows),
        grid=grid,
        in_specs=[cur, cur_plane, cur_plane],
        out_specs=[cur, cur],
        out_shape=[pair, pair],
    )(adjoint_end, phase, labels)
    phase_grad, w_second, *w2_edges = pl.pallas_call(
        functools.partial(first_kernel, rows=rows),
        grid=grid,
        in_specs=field_specs(mag_middle.shape, rows) + field_specs(mag_start.shape, rows)
        + field_specs(w_first.shape, rows)
        + [cur, whole((6, length_z, length_x)), whole((6, length_z, length_x)), zspec(6), zspec(6)],
        out_specs=[cur_plane, cur] + edge_specs,
        out_shape=[plane, pair] + edge_shapes,
    )(mag_middle, mag_middle, mag_middle, mag_start, mag_start, mag_start,
      w_first, w_first, w_first, factor, *halos)
    halos = send_edges(*w2_edges)
    return phase_grad, functools.partial(finish_lambda, w_second, rows, grid, cur, whole, zspec, length_z, length_x), halos


def finish_lambda(w_second, rows, grid, cur, whole, zspec, length_z, length_x, halos):
    pair = jax.ShapeDtypeStruct(w_second.shape, jnp.float32)
    lam = pl.pallas_call(
        functools.partial(second_kernel, rows=rows),
        grid=grid,
        in_specs=field_specs(w_second.shape, rows)
        + [whole((2, length_z, length_x)), whole((2, length_z, length_x)), zspec(2), zspec(2)],
        out_specs=cur,
        out_shape=pair,
    )(w_second, w_second, w_second, *halos)
    return lam


def dipole_adjoint(phase_grad, finish, halos):
    count_y = lax.axis_size("gy")
    count_z = lax.axis_size("gz")
    parts = count_y * count_z
    block_y, block_z, length_x = phase_grad.shape
    length_y = block_y * count_y
    length_z = block_z * count_z
    block_x = length_x // parts
    pieces = 2 if block_x % 2 == 0 else 1
    piece_x = block_x // pieces
    table_x = cas_table(length_x).reshape(parts, pieces, piece_x, length_x)
    table_y = cas_table(length_y)
    table_z = cas_table(length_z)
    scale = 1.0 / (float(length_y) * float(length_z) * float(length_x))
    freq_y = signed_freq(jnp.arange(length_y, dtype=jnp.int32), length_y)
    freq_z = signed_freq(jnp.arange(length_z, dtype=jnp.int32), length_z)
    index = lax.axis_index("gy") * count_z + lax.axis_index("gz")
    sent = []
    for p in range(pieces):
        spec = along("sxn,yzn->sxyz", table_x[:, p], phase_grad)
        if p == 0:
            halos, spec = lax.optimization_barrier((halos, spec))
        sent.append(lax.all_to_all(spec, ("gy", "gz"), 0, 0, tiled=True))
        if p == 0:
            lam = finish(halos)
    result = None
    for p in range(pieces):
        spec = sent[p].reshape(count_y, count_z, piece_x, block_y, block_z)
        spec = spec.transpose(2, 0, 3, 1, 4).reshape(piece_x, length_y, length_z)
        spec = along("kz,xyz->xyk", table_z, spec)
        spec = along("ky,xyz->xkz", table_y, spec)
        first_x = index * block_x + p * piece_x
        freq_x = signed_freq(first_x + jnp.arange(piece_x, dtype=jnp.int32), length_x)
        kernel = dipole_block(freq_y[None, :, None], freq_z[None, None, :], freq_x[:, None, None])
        spec = spec * kernel
        spec = along("ky,xyz->xkz", table_y, spec)
        spec = along("kz,xyz->xyk", table_z, spec)
        spec = spec.reshape(piece_x, count_y, block_y, count_z, block_z)
        spec = spec.transpose(1, 3, 0, 2, 4).reshape(parts, piece_x, block_y, block_z)
        spec = lax.all_to_all(spec, ("gy", "gz"), 0, 0, tiled=True)
        part = along("sxn,sxyz->yzn", table_x[:, p], spec)
        result = part if result is None else result + part
    return result * scale, lam


def per_device(mag_start, mag_middle, adjoint_end, phase, labels):
    phase_grad, finish, halos = backward_sections(mag_start, mag_middle, adjoint_end, phase, labels)
    chi_grad, lam = dipole_adjoint(phase_grad, finish, halos)
    return (lam, chi_grad)


def solution(mesh):
    return jax.shard_map(
        per_device,
        mesh=mesh,
        in_specs=(
            P(None, "gy", "gz", None),
            P(None, "gy", "gz", None),
            P(None, "gy", "gz", None),
            P("gy", "gz", None),
            P("gy", "gz", None),
        ),
        out_specs=(P(None, "gy", "gz", None), P("gy", "gz", None)),
        check_vma=False,
    )
```

```python
import functools
import math

import jax
import numpy as np
import jax.numpy as jnp
from jax import lax
from jax.experimental import pallas as pl
from jax.experimental.pallas import tpu as pltpu
from jax.sharding import PartitionSpec as P


def signed_freq(index, length):
    return jnp.where(index < length // 2, index, index - length)


def dipole_block(freq_y, freq_z, freq_x):
    square_z = freq_z * freq_z
    total = freq_y * freq_y + square_z + freq_x * freq_x
    ratio = square_z.astype(jnp.float32) / jnp.maximum(total, 1).astype(jnp.float32)
    return jnp.where(total == 0, jnp.float32(0.0), jnp.float32(1.0 / 3.0) - ratio)


def cas_table(length):
    index = jnp.arange(length, dtype=jnp.int32)
    product = index[:, None] * index[None, :] % length
    angle = product.astype(jnp.float32) * (2.0 * math.pi / length)
    return jnp.cos(angle) + jnp.sin(angle)


def along(spec, table, values):
    return jnp.einsum(spec, table, values, precision=lax.Precision.HIGH)


def plane_update(centre, below, above, z_low, z_high):
    length_z, length_x = centre.shape
    up = pltpu.roll(centre, 1, 0)
    down = pltpu.roll(centre, length_z - 1, 0)
    if length_z > 8:
        row = lax.broadcasted_iota(jnp.int32, (8, length_x), 0)
        up = jnp.concatenate([jnp.where(row == 0, z_low, up[:8]), up[8:]], axis=0)
        down = jnp.concatenate([down[:length_z - 8], jnp.where(row == 7, z_high, down[length_z - 8:])], axis=0)
    else:
        row = lax.broadcasted_iota(jnp.int32, centre.shape, 0)
        up = jnp.where(row == 0, z_low, up)
        down = jnp.where(row == length_z - 1, z_high, down)
    total = below + above + up + down
    total = total + pltpu.roll(centre, 1, 1) + pltpu.roll(centre, length_x - 1, 1)
    return 0.1 * centre + 0.15 * total


def neighbour_planes(cur_ref, prev_ref, next_ref, y_low_ref, y_high_ref, rows, field, comp, r, step, last):
    if isinstance(r, int) and r == 0:
        below = jnp.where(step == 0, y_low_ref[field], prev_ref[comp, 0])
    else:
        below = cur_ref[comp, r - 1]
    if isinstance(r, int) and r == rows - 1:
        above = jnp.where(step == last, y_high_ref[field], next_ref[comp, 0])
    else:
        above = cur_ref[comp, r + 1]
    return below, above


def write_edges(step, last, rows, r, values, y_first_ref, y_last_ref, z_first_ref, z_last_ref):
    for c, value in enumerate(values):
        z_first_ref[c, r] = value[0:1]
        z_last_ref[c, r] = value[value.shape[0] - 1:]
    if isinstance(r, int) and r == 0:
        @pl.when(step == 0)
        def _():
            for c, value in enumerate(values):
                y_first_ref[c] = value
    if isinstance(r, int) and r == rows - 1:
        @pl.when(step == last)
        def _():
            for c, value in enumerate(values):
                y_last_ref[c] = value


def for_rows(rows, body):
    body(0)
    if rows > 2:
        def loop_body(r, carry):
            body(r)
            return carry
        lax.fori_loop(1, rows - 1, loop_body, 0)
    if rows > 1:
        body(rows - 1)


def sin_cos(x):
    k = jnp.floor(x * (2.0 / math.pi) + 0.5)
    r = (x - k * 1.5707963705062866) - k * (-4.371139000186243e-08)
    r2 = r * r
    s = r + r * r2 * (-1.0 / 6.0 + r2 * (1.0 / 120.0 + r2 * (-1.0 / 5040.0 + r2 * (1.0 / 362880.0))))
    c = 1.0 + r2 * (-0.5 + r2 * (1.0 / 24.0 + r2 * (-1.0 / 720.0 + r2 * (1.0 / 40320.0
                                                                        + r2 * (-1.0 / 3628800.0)))))
    quadrant = k.astype(jnp.int32) & 3
    swap = (quadrant & 1) == 1
    sin_x = jnp.where(swap, c, s)
    cos_x = jnp.where(swap, s, c)
    sin_x = jnp.where(quadrant >= 2, -sin_x, sin_x)
    cos_x = jnp.where((quadrant == 1) | (quadrant == 2), -cos_x, cos_x)
    return sin_x, cos_x


def step_factor(labels, phase):
    decays = [float(np.exp(-np.float32(rate))) for rate in (0.02, 0.3, 0.6, 1.2)]
    decay = jnp.where(labels == 1, decays[1], decays[0])
    decay = jnp.where(labels == 2, decays[2], decay)
    decay = jnp.where(labels == 3, decays[3], decay).astype(jnp.float32)
    sin_p, cos_p = sin_cos(phase)
    return decay * cos_p, decay * sin_p


def first_w(lam_real, lam_imag, labels, phase):
    f_real, f_imag = step_factor(labels, phase)
    return (f_real * lam_real - f_imag * lam_imag, f_real * lam_imag + f_imag * lam_real), (f_real, f_imag)


def factor_kernel(lam_ref, phase_ref, labels_ref, factor_ref, w_ref, *, rows):
    def body(r, carry):
        (w_real, w_imag), (f_real, f_imag) = first_w(lam_ref[0, r], lam_ref[1, r], labels_ref[r], phase_ref[r])
        factor_ref[0, r] = f_real
        factor_ref[1, r] = f_imag
        w_ref[0, r] = w_real
        w_ref[1, r] = w_imag
        return carry
    lax.fori_loop(0, rows, body, 0)


def edges_kernel(*refs, rows):
    (mm_y0, mm_y1, mm_z0, mm_z1, ms_y0, ms_y1, ms_z0, ms_z1, lam_y0, lam_y1, lam_z0, lam_z1,
     ph_y0, ph_y1, ph_z0, ph_z1, lb_y0, lb_y1, lb_z0, lb_z1,
     y_first_ref, y_last_ref, z_first_ref, z_last_ref) = refs

    @pl.when(pl.program_id(0) == 0)
    def _():
        for out_ref, m1, m2, lam, ph, lb in ((y_first_ref, mm_y0, ms_y0, lam_y0, ph_y0, lb_y0),
                                           (y_last_ref, mm_y1, ms_y1, lam_y1, ph_y1, lb_y1)):
            (w_real, w_imag), _ = first_w(lam[0, 0], lam[1, 0], lb[0], ph[0])
            planes = [m1[0, 0], m1[1, 0], m2[0, 0], m2[1, 0], w_real, w_imag]
            for c, value in enumerate(planes):
                out_ref[c] = value

    def body(r, carry):
        for out_ref, m1, m2, lam, ph, lb, at in ((z_first_ref, mm_z0, ms_z0, lam_z0, ph_z0, lb_z0, 0),
                                               (z_last_ref, mm_z1, ms_z1, lam_z1, ph_z1, lb_z1, 7)):
            (w_real, w_imag), _ = first_w(lam[0, r], lam[1, r], lb[r], ph[r])
            tiles = [m1[0, r], m1[1, r], m2[0, r], m2[1, r], w_real, w_imag]
            for c, value in enumerate(tiles):
                out_ref[c, r] = value[at:at + 1]
        return carry
    lax.fori_loop(0, rows, body, 0)


def edge_specs_of(ndim, length_y, length_z, length_x, rows):
    lead = (2,) if ndim == 4 else ()
    zero = (0,) * len(lead)
    tiles = length_z // 8
    return [
        pl.BlockSpec(lead + (1, length_z, length_x), lambda i: zero + (0, 0, 0)),
        pl.BlockSpec(lead + (1, length_z, length_x), lambda i: zero + (length_y - 1, 0, 0)),
        pl.BlockSpec(lead + (rows, 8, length_x), lambda i: zero + (i, 0, 0)),
        pl.BlockSpec(lead + (rows, 8, length_x), lambda i: zero + (i, tiles - 1, 0)),
    ]


def edge_outputs(comps, length_y, length_z, length_x, rows):
    plane = jax.ShapeDtypeStruct((comps, length_z, length_x), jnp.float32)
    row = jax.ShapeDtypeStruct((comps, length_y, 1, length_x), jnp.float32)
    plane_spec = pl.BlockSpec((comps, length_z, length_x), lambda i: (0, 0, 0))
    row_spec = pl.BlockSpec((comps, rows, 1, length_x), lambda i: (0, i, 0, 0))
    return [plane, plane, row, row], [plane_spec, plane_spec, row_spec, row_spec]


def first_kernel(*refs, rows):
    (mm_ref, mm_prev, mm_next, ms_ref, ms_prev, ms_next, w_ref, w_prev, w_next,
     factor_ref, y_low_ref, y_high_ref, z_low_ref, z_high_ref, pg_ref, w2_ref) = refs[:16]
    step = pl.program_id(0)
    last = pl.num_programs(0) - 1
    fields = ((mm_ref, mm_prev, mm_next), (ms_ref, ms_prev, ms_next), (w_ref, w_prev, w_next))

    def body(r):
        new = []
        for f, (cur, prev, nxt) in enumerate(fields):
            pair = []
            for comp in range(2):
                below, above = neighbour_planes(cur, prev, nxt, y_low_ref, y_high_ref, rows, 2 * f + comp, comp, r,
                                                step, last)
                pair.append(plane_update(cur[comp, r], below, above,
                                         z_low_ref[2 * f + comp, r], z_high_ref[2 * f + comp, r]))
            new.append(pair)
        (u1_real, u1_imag), (u2_real, u2_imag), (lam_real, lam_imag) = new
        w_real = w_ref[0, r]
        w_imag = w_ref[1, r]
        f_real = factor_ref[0, r]
        f_imag = factor_ref[1, r]
        w2_real = f_real * lam_real - f_imag * lam_imag
        w2_imag = f_real * lam_imag + f_imag * lam_real
        grad = w_real * u1_imag - w_imag * u1_real
        pg_ref[r] = grad + (w2_real * u2_imag - w2_imag * u2_real)
        w2_ref[0, r] = w2_real
        w2_ref[1, r] = w2_imag
        write_edges(step, last, rows, r, [w2_real, w2_imag], *refs[16:])

    for_rows(rows, body)


def second_kernel(w_ref, w_prev, w_next, y_low_ref, y_high_ref, z_low_ref, z_high_ref, out_ref, *, rows):
    step = pl.program_id(0)
    last = pl.num_programs(0) - 1

    def body(r):
        for comp in range(2):
            below, above = neighbour_planes(w_ref, w_prev, w_next, y_low_ref, y_high_ref, rows, comp, comp, r,
                                            step, last)
            out_ref[comp, r] = plane_update(w_ref[comp, r], below, above,
                                            z_low_ref[comp, r], z_high_ref[comp, r])

    for_rows(rows, body)


def block_rows(length_y):
    rows = 8
    while length_y % rows:
        rows //= 2
    return rows


def field_specs(shape, rows):
    comps, length_y, length_z, length_x = shape
    cur = pl.BlockSpec((comps, rows, length_z, length_x), lambda i: (0, i, 0, 0))
    prev = pl.BlockSpec((comps, 1, length_z, length_x),
                        lambda i: (0, jnp.maximum(i * rows - 1, 0), 0, 0))
    nxt = pl.BlockSpec((comps, 1, length_z, length_x),
                       lambda i: (0, jnp.minimum(i * rows + rows, length_y - 1), 0, 0))
    return [cur, prev, nxt]


def send_edges(y_first, y_last, z_first, z_last):
    results = []
    for axis, first, last in (("gy", y_first, y_last), ("gz", z_first, z_last)):
        count = lax.axis_size(axis)
        up = [(i, (i + 1) % count) for i in range(count)]
        down = [(j, i) for i, j in up]
        if count == 2:
            both = lax.ppermute(jnp.stack([last, first]), axis, up)
            results.extend([both[0], both[1]])
        else:
            results.extend([lax.ppermute(last, axis, up), lax.ppermute(first, axis, down)])
    return results


def backward_sections(mag_start, mag_middle, adjoint_end, phase, labels):
    _, length_y, length_z, length_x = mag_start.shape
    rows = block_rows(length_y)
    grid = (length_y // rows,)
    plane = jax.ShapeDtypeStruct((length_y, length_z, length_x), jnp.float32)
    pair = jax.ShapeDtypeStruct((2, length_y, length_z, length_x), jnp.float32)
    cur = pl.BlockSpec((2, rows, length_z, length_x), lambda i: (0, i, 0, 0))
    cur_plane = pl.BlockSpec((rows, length_z, length_x), lambda i: (i, 0, 0))
    whole = lambda shape: pl.BlockSpec(shape, lambda i: (0,) * len(shape))
    zspec = lambda comps: pl.BlockSpec((comps, rows, 1, length_x), lambda i: (0, i, 0, 0))
    edge_shapes, edge_specs = edge_outputs(2, length_y, length_z, length_x, rows)
    six_shapes, six_specs = edge_outputs(6, length_y, length_z, length_x, rows)
    inputs = (mag_middle, mag_start, adjoint_end, phase, labels)
    edges = pl.pallas_call(
        functools.partial(edges_kernel, rows=rows),
        grid=grid,
        in_specs=[s for a in inputs for s in edge_specs_of(a.ndim, length_y, length_z, length_x, rows)],
        out_specs=six_specs,
        out_shape=six_shapes,
    )(*[a for a in inputs for _ in range(4)])
    halos = send_edges(*edges)
    factor, w_first = pl.pallas_call(
        functools.partial(factor_kernel, rows=rows),
        grid=grid,
        in_specs=[cur, cur_plane, cur_plane],
        out_specs=[cur, cur],
        out_shape=[pair, pair],
    )(adjoint_end, phase, labels)
    phase_grad, w_second, *w2_edges = pl.pallas_call(
        functools.partial(first_kernel, rows=rows),
        grid=grid,
        in_specs=field_specs(mag_middle.shape, rows) + field_specs(mag_start.shape, rows)
        + field_specs(w_first.shape, rows)
        + [cur, whole((6, length_z, length_x)), whole((6, length_z, length_x)), zspec(6), zspec(6)],
        out_specs=[cur_plane, cur] + edge_specs,
        out_shape=[plane, pair] + edge_shapes,
    )(mag_middle, mag_middle, mag_middle, mag_start, mag_start, mag_start,
      w_first, w_first, w_first, factor, *halos)
    halos = send_edges(*w2_edges)
    return phase_grad, functools.partial(finish_lambda, w_second, rows, grid, cur, whole, zspec, length_z, length_x), halos


def finish_lambda(w_second, rows, grid, cur, whole, zspec, length_z, length_x, halos):
    pair = jax.ShapeDtypeStruct(w_second.shape, jnp.float32)
    lam = pl.pallas_call(
        functools.partial(second_kernel, rows=rows),
        grid=grid,
        in_specs=field_specs(w_second.shape, rows)
        + [whole((2, length_z, length_x)), whole((2, length_z, length_x)), zspec(2), zspec(2)],
        out_specs=cur,
        out_shape=pair,
    )(w_second, w_second, w_second, *halos)
    return lam


def dipole_adjoint(phase_grad, finish, halos):
    count_y = lax.axis_size("gy")
    count_z = lax.axis_size("gz")
    parts = count_y * count_z
    block_y, block_z, length_x = phase_grad.shape
    length_y = block_y * count_y
    length_z = block_z * count_z
    block_x = length_x // parts
    pieces = 2 if block_x % 2 == 0 else 1
    piece_x = block_x // pieces
    table_x = cas_table(length_x).reshape(parts, pieces, piece_x, length_x)
    table_y = cas_table(length_y)
    table_z = cas_table(length_z)
    scale = 1.0 / (float(length_y) * float(length_z) * float(length_x))
    freq_y = signed_freq(jnp.arange(length_y, dtype=jnp.int32), length_y)
    freq_z = signed_freq(jnp.arange(length_z, dtype=jnp.int32), length_z)
    index = lax.axis_index("gy") * count_z + lax.axis_index("gz")
    sent = []
    for p in range(pieces):
        spec = along("sxn,yzn->sxyz", table_x[:, p], phase_grad)
        if p == 0:
            halos, spec = lax.optimization_barrier((halos, spec))
        sent.append(lax.all_to_all(spec, ("gy", "gz"), 0, 0, tiled=True))
        if p == 0:
            lam = finish(halos)
    result = None
    for p in range(pieces):
        spec = sent[p].reshape(count_y, count_z, piece_x, block_y, block_z)
        spec = spec.transpose(2, 0, 3, 1, 4).reshape(piece_x, length_y, length_z)
        spec = along("kz,xyz->xyk", table_z, spec)
        spec = along("ky,xyz->xkz", table_y, spec)
        first_x = index * block_x + p * piece_x
        freq_x = signed_freq(first_x + jnp.arange(piece_x, dtype=jnp.int32), length_x)
        kernel = dipole_block(freq_y[None, :, None], freq_z[None, None, :], freq_x[:, None, None])
        spec = spec * kernel
        spec = along("ky,xyz->xkz", table_y, spec)
        spec = along("kz,xyz->xyk", table_z, spec)
        spec = spec.reshape(piece_x, count_y, block_y, count_z, block_z)
        spec = spec.transpose(1, 3, 0, 2, 4).reshape(parts, piece_x, block_y, block_z)
        spec = lax.all_to_all(spec, ("gy", "gz"), 0, 0, tiled=True)
        part = along("sxn,sxyz->yzn", table_x[:, p], spec)
        result = part if result is None else result + part
    return result * scale, lam


def per_device(mag_start, mag_middle, adjoint_end, phase, labels):
    phase_grad, finish, halos = backward_sections(mag_start, mag_middle, adjoint_end, phase, labels)
    chi_grad, lam = dipole_adjoint(phase_grad, finish, halos)
    return (lam, chi_grad)


def solution(mesh):
    return jax.shard_map(
        per_device,
        mesh=mesh,
        in_specs=(
            P(None, "gy", "gz", None),
            P(None, "gy", "gz", None),
            P(None, "gy", "gz", None),
            P("gy", "gz", None),
            P("gy", "gz", None),
        ),
        out_specs=(P(None, "gy", "gz", None), P("gy", "gz", None)),
        check_vma=False,
    )
```

```python
import functools
import math

import jax
import numpy as np
import jax.numpy as jnp
from jax import lax
from jax.experimental import pallas as pl
from jax.experimental.pallas import tpu as pltpu
from jax.sharding import PartitionSpec as P


def signed_freq(index, length):
    return jnp.where(index < length // 2, index, index - length)


def dipole_block(freq_y, freq_z, freq_x):
    square_z = freq_z * freq_z
    total = freq_y * freq_y + square_z + freq_x * freq_x
    ratio = square_z.astype(jnp.float32) / jnp.maximum(total, 1).astype(jnp.float32)
    return jnp.where(total == 0, jnp.float32(0.0), jnp.float32(1.0 / 3.0) - ratio)


def cas_table(length):
    index = jnp.arange(length, dtype=jnp.int32)
    product = index[:, None] * index[None, :] % length
    angle = product.astype(jnp.float32) * (2.0 * math.pi / length)
    return jnp.cos(angle) + jnp.sin(angle)


def along(spec, table, values):
    return jnp.einsum(spec, table, values, precision=lax.Precision.HIGH)


def plane_update(centre, below, above, z_low, z_high):
    length_z, length_x = centre.shape
    up = pltpu.roll(centre, 1, 0)
    down = pltpu.roll(centre, length_z - 1, 0)
    if length_z > 8:
        row = lax.broadcasted_iota(jnp.int32, (8, length_x), 0)
        up = jnp.concatenate([jnp.where(row == 0, z_low, up[:8]), up[8:]], axis=0)
        down = jnp.concatenate([down[:length_z - 8], jnp.where(row == 7, z_high, down[length_z - 8:])], axis=0)
    else:
        row = lax.broadcasted_iota(jnp.int32, centre.shape, 0)
        up = jnp.where(row == 0, z_low, up)
        down = jnp.where(row == length_z - 1, z_high, down)
    total = below + above + up + down
    total = total + pltpu.roll(centre, 1, 1) + pltpu.roll(centre, length_x - 1, 1)
    return centre + 0.15 * (total - 6.0 * centre)


def neighbour_planes(cur_ref, prev_ref, next_ref, y_low_ref, y_high_ref, rows, field, comp, r, step, last):
    if isinstance(r, int) and r == 0:
        below = jnp.where(step == 0, y_low_ref[field], prev_ref[comp, 0])
    else:
        below = cur_ref[comp, r - 1]
    if isinstance(r, int) and r == rows - 1:
        above = jnp.where(step == last, y_high_ref[field], next_ref[comp, 0])
    else:
        above = cur_ref[comp, r + 1]
    return below, above


def write_edges(step, last, rows, r, values, y_first_ref, y_last_ref, z_first_ref, z_last_ref):
    for c, value in enumerate(values):
        z_first_ref[c, r] = value[0:1]
        z_last_ref[c, r] = value[value.shape[0] - 1:]
    if isinstance(r, int) and r == 0:
        @pl.when(step == 0)
        def _():
            for c, value in enumerate(values):
                y_first_ref[c] = value
    if isinstance(r, int) and r == rows - 1:
        @pl.when(step == last)
        def _():
            for c, value in enumerate(values):
                y_last_ref[c] = value


def for_rows(rows, body):
    body(0)
    if rows > 2:
        def loop_body(r, carry):
            body(r)
            return carry
        lax.fori_loop(1, rows - 1, loop_body, 0)
    if rows > 1:
        body(rows - 1)


def sin_cos(x):
    k = jnp.floor(x * (2.0 / math.pi) + 0.5)
    r = (x - k * 1.5707963705062866) - k * (-4.371139000186243e-08)
    r2 = r * r
    s = r + r * r2 * (-1.0 / 6.0 + r2 * (1.0 / 120.0 + r2 * (-1.0 / 5040.0 + r2 * (1.0 / 362880.0))))
    c = 1.0 + r2 * (-0.5 + r2 * (1.0 / 24.0 + r2 * (-1.0 / 720.0 + r2 * (1.0 / 40320.0
                                                                        + r2 * (-1.0 / 3628800.0)))))
    quadrant = k.astype(jnp.int32) & 3
    swap = (quadrant & 1) == 1
    sin_x = jnp.where(swap, c, s)
    cos_x = jnp.where(swap, s, c)
    sin_x = jnp.where(quadrant >= 2, -sin_x, sin_x)
    cos_x = jnp.where((quadrant == 1) | (quadrant == 2), -cos_x, cos_x)
    return sin_x, cos_x


def step_factor(labels, phase):
    decays = [float(np.exp(-np.float32(rate))) for rate in (0.02, 0.3, 0.6, 1.2)]
    decay = jnp.where(labels == 1, decays[1], decays[0])
    decay = jnp.where(labels == 2, decays[2], decay)
    decay = jnp.where(labels == 3, decays[3], decay).astype(jnp.float32)
    sin_p, cos_p = sin_cos(phase)
    return decay * cos_p, decay * sin_p


def first_w(lam_real, lam_imag, labels, phase):
    f_real, f_imag = step_factor(labels, phase)
    return (f_real * lam_real - f_imag * lam_imag, f_real * lam_imag + f_imag * lam_real), (f_real, f_imag)


def factor_kernel(lam_ref, phase_ref, labels_ref, factor_ref, w_ref, *, rows):
    def body(r, carry):
        (w_real, w_imag), (f_real, f_imag) = first_w(lam_ref[0, r], lam_ref[1, r], labels_ref[r], phase_ref[r])
        factor_ref[0, r] = f_real
        factor_ref[1, r] = f_imag
        w_ref[0, r] = w_real
        w_ref[1, r] = w_imag
        return carry
    lax.fori_loop(0, rows, body, 0)


def edges_kernel(*refs, rows):
    (mm_y0, mm_y1, mm_z0, mm_z1, ms_y0, ms_y1, ms_z0, ms_z1, lam_y0, lam_y1, lam_z0, lam_z1,
     ph_y0, ph_y1, ph_z0, ph_z1, lb_y0, lb_y1, lb_z0, lb_z1,
     y_first_ref, y_last_ref, z_first_ref, z_last_ref) = refs

    @pl.when(pl.program_id(0) == 0)
    def _():
        for out_ref, m1, m2, lam, ph, lb in ((y_first_ref, mm_y0, ms_y0, lam_y0, ph_y0, lb_y0),
                                           (y_last_ref, mm_y1, ms_y1, lam_y1, ph_y1, lb_y1)):
            (w_real, w_imag), _ = first_w(lam[0, 0], lam[1, 0], lb[0], ph[0])
            planes = [m1[0, 0], m1[1, 0], m2[0, 0], m2[1, 0], w_real, w_imag]
            for c, value in enumerate(planes):
                out_ref[c] = value

    def body(r, carry):
        for out_ref, m1, m2, lam, ph, lb, at in ((z_first_ref, mm_z0, ms_z0, lam_z0, ph_z0, lb_z0, 0),
                                               (z_last_ref, mm_z1, ms_z1, lam_z1, ph_z1, lb_z1, 7)):
            (w_real, w_imag), _ = first_w(lam[0, r], lam[1, r], lb[r], ph[r])
            tiles = [m1[0, r], m1[1, r], m2[0, r], m2[1, r], w_real, w_imag]
            for c, value in enumerate(tiles):
                out_ref[c, r] = value[at:at + 1]
        return carry
    lax.fori_loop(0, rows, body, 0)


def edge_specs_of(ndim, length_y, length_z, length_x, rows):
    lead = (2,) if ndim == 4 else ()
    zero = (0,) * len(lead)
    tiles = length_z // 8
    return [
        pl.BlockSpec(lead + (1, length_z, length_x), lambda i: zero + (0, 0, 0)),
        pl.BlockSpec(lead + (1, length_z, length_x), lambda i: zero + (length_y - 1, 0, 0)),
        pl.BlockSpec(lead + (rows, 8, length_x), lambda i: zero + (i, 0, 0)),
        pl.BlockSpec(lead + (rows, 8, length_x), lambda i: zero + (i, tiles - 1, 0)),
    ]


def edge_outputs(comps, length_y, length_z, length_x, rows):
    plane = jax.ShapeDtypeStruct((comps, length_z, length_x), jnp.float32)
    row = jax.ShapeDtypeStruct((comps, length_y, 1, length_x), jnp.float32)
    plane_spec = pl.BlockSpec((comps, length_z, length_x), lambda i: (0, 0, 0))
    row_spec = pl.BlockSpec((comps, rows, 1, length_x), lambda i: (0, i, 0, 0))
    return [plane, plane, row, row], [plane_spec, plane_spec, row_spec, row_spec]


def first_kernel(*refs, rows):
    (mm_ref, mm_prev, mm_next, ms_ref, ms_prev, ms_next, w_ref, w_prev, w_next,
     factor_ref, y_low_ref, y_high_ref, z_low_ref, z_high_ref, pg_ref, w2_ref) = refs[:16]
    step = pl.program_id(0)
    last = pl.num_programs(0) - 1
    fields = ((mm_ref, mm_prev, mm_next), (ms_ref, ms_prev, ms_next), (w_ref, w_prev, w_next))

    def body(r):
        new = []
        for f, (cur, prev, nxt) in enumerate(fields):
            pair = []
            for comp in range(2):
                below, above = neighbour_planes(cur, prev, nxt, y_low_ref, y_high_ref, rows, 2 * f + comp, comp, r,
                                                step, last)
                pair.append(plane_update(cur[comp, r], below, above,
                                         z_low_ref[2 * f + comp, r], z_high_ref[2 * f + comp, r]))
            new.append(pair)
        (u1_real, u1_imag), (u2_real, u2_imag), (lam_real, lam_imag) = new
        w_real = w_ref[0, r]
        w_imag = w_ref[1, r]
        f_real = factor_ref[0, r]
        f_imag = factor_ref[1, r]
        w2_real = f_real * lam_real - f_imag * lam_imag
        w2_imag = f_real * lam_imag + f_imag * lam_real
        grad = w_real * u1_imag - w_imag * u1_real
        pg_ref[r] = grad + (w2_real * u2_imag - w2_imag * u2_real)
        w2_ref[0, r] = w2_real
        w2_ref[1, r] = w2_imag
        write_edges(step, last, rows, r, [w2_real, w2_imag], *refs[16:])

    for_rows(rows, body)


def second_kernel(w_ref, w_prev, w_next, y_low_ref, y_high_ref, z_low_ref, z_high_ref, out_ref, *, rows):
    step = pl.program_id(0)
    last = pl.num_programs(0) - 1

    def body(r):
        for comp in range(2):
            below, above = neighbour_planes(w_ref, w_prev, w_next, y_low_ref, y_high_ref, rows, comp, comp, r,
                                            step, last)
            out_ref[comp, r] = plane_update(w_ref[comp, r], below, above,
                                            z_low_ref[comp, r], z_high_ref[comp, r])

    for_rows(rows, body)


def block_rows(length_y):
    rows = 8
    while length_y % rows:
        rows //= 2
    return rows


def field_specs(shape, rows):
    comps, length_y, length_z, length_x = shape
    cur = pl.BlockSpec((comps, rows, length_z, length_x), lambda i: (0, i, 0, 0))
    prev = pl.BlockSpec((comps, 1, length_z, length_x),
                        lambda i: (0, jnp.maximum(i * rows - 1, 0), 0, 0))
    nxt = pl.BlockSpec((comps, 1, length_z, length_x),
                       lambda i: (0, jnp.minimum(i * rows + rows, length_y - 1), 0, 0))
    return [cur, prev, nxt]


def send_edges(y_first, y_last, z_first, z_last):
    results = []
    for axis, first, last in (("gy", y_first, y_last), ("gz", z_first, z_last)):
        count = lax.axis_size(axis)
        up = [(i, (i + 1) % count) for i in range(count)]
        down = [(j, i) for i, j in up]
        if count == 2:
            both = lax.ppermute(jnp.stack([last, first]), axis, up)
            results.extend([both[0], both[1]])
        else:
            results.extend([lax.ppermute(last, axis, up), lax.ppermute(first, axis, down)])
    return results


def backward_sections(mag_start, mag_middle, adjoint_end, phase, labels):
    _, length_y, length_z, length_x = mag_start.shape
    rows = block_rows(length_y)
    grid = (length_y // rows,)
    plane = jax.ShapeDtypeStruct((length_y, length_z, length_x), jnp.float32)
    pair = jax.ShapeDtypeStruct((2, length_y, length_z, length_x), jnp.float32)
    cur = pl.BlockSpec((2, rows, length_z, length_x), lambda i: (0, i, 0, 0))
    cur_plane = pl.BlockSpec((rows, length_z, length_x), lambda i: (i, 0, 0))
    whole = lambda shape: pl.BlockSpec(shape, lambda i: (0,) * len(shape))
    zspec = lambda comps: pl.BlockSpec((comps, rows, 1, length_x), lambda i: (0, i, 0, 0))
    edge_shapes, edge_specs = edge_outputs(2, length_y, length_z, length_x, rows)
    six_shapes, six_specs = edge_outputs(6, length_y, length_z, length_x, rows)
    inputs = (mag_middle, mag_start, adjoint_end, phase, labels)
    edges = pl.pallas_call(
        functools.partial(edges_kernel, rows=rows),
        grid=grid,
        in_specs=[s for a in inputs for s in edge_specs_of(a.ndim, length_y, length_z, length_x, rows)],
        out_specs=six_specs,
        out_shape=six_shapes,
    )(*[a for a in inputs for _ in range(4)])
    count_y = lax.axis_size("gy")
    up = [(i, (i + 1) % count_y) for i in range(count_y)]
    down = [(j, i) for i, j in up]
    mag_low = lax.ppermute(jnp.concatenate([mag_middle[:, length_y - 1], mag_start[:, length_y - 1]]), "gy", up)
    mag_high = lax.ppermute(jnp.concatenate([mag_middle[:, 0], mag_start[:, 0]]), "gy", down)
    w_low, w_high, z_low, z_high = send_edges(edges[0][4:], edges[1][4:], edges[2], edges[3])
    halos = [jnp.concatenate([mag_low, w_low]), jnp.concatenate([mag_high, w_high]), z_low, z_high]
    factor, w_first = pl.pallas_call(
        functools.partial(factor_kernel, rows=rows),
        grid=grid,
        in_specs=[cur, cur_plane, cur_plane],
        out_specs=[cur, cur],
        out_shape=[pair, pair],
    )(adjoint_end, phase, labels)
    phase_grad, w_second, *w2_edges = pl.pallas_call(
        functools.partial(first_kernel, rows=rows),
        grid=grid,
        in_specs=field_specs(mag_middle.shape, rows) + field_specs(mag_start.shape, rows)
        + field_specs(w_first.shape, rows)
        + [cur, whole((6, length_z, length_x)), whole((6, length_z, length_x)), zspec(6), zspec(6)],
        out_specs=[cur_plane, cur] + edge_specs,
        out_shape=[plane, pair] + edge_shapes,
    )(mag_middle, mag_middle, mag_middle, mag_start, mag_start, mag_start,
      w_first, w_first, w_first, factor, *halos)
    halos = send_edges(*w2_edges)
    return phase_grad, functools.partial(finish_lambda, w_second, rows, grid, cur, whole, zspec, length_z, length_x), halos


def finish_lambda(w_second, rows, grid, cur, whole, zspec, length_z, length_x, halos):
    pair = jax.ShapeDtypeStruct(w_second.shape, jnp.float32)
    lam = pl.pallas_call(
        functools.partial(second_kernel, rows=rows),
        grid=grid,
        in_specs=field_specs(w_second.shape, rows)
        + [whole((2, length_z, length_x)), whole((2, length_z, length_x)), zspec(2), zspec(2)],
        out_specs=cur,
        out_shape=pair,
    )(w_second, w_second, w_second, *halos)
    return lam


def dipole_adjoint(phase_grad, finish, halos):
    count_y = lax.axis_size("gy")
    count_z = lax.axis_size("gz")
    parts = count_y * count_z
    block_y, block_z, length_x = phase_grad.shape
    length_y = block_y * count_y
    length_z = block_z * count_z
    block_x = length_x // parts
    pieces = 2 if block_x % 2 == 0 else 1
    piece_x = block_x // pieces
    table_x = cas_table(length_x).reshape(parts, pieces, piece_x, length_x)
    table_y = cas_table(length_y)
    table_z = cas_table(length_z)
    scale = 1.0 / (float(length_y) * float(length_z) * float(length_x))
    freq_y = signed_freq(jnp.arange(length_y, dtype=jnp.int32), length_y)
    freq_z = signed_freq(jnp.arange(length_z, dtype=jnp.int32), length_z)
    index = lax.axis_index("gy") * count_z + lax.axis_index("gz")
    sent = []
    for p in range(pieces):
        spec = along("sxn,yzn->sxyz", table_x[:, p], phase_grad)
        if p == 0:
            halos, spec = lax.optimization_barrier((halos, spec))
        sent.append(lax.all_to_all(spec, ("gy", "gz"), 0, 0, tiled=True))
        if p == 0:
            lam = finish(halos)
    result = None
    for p in range(pieces):
        spec = sent[p].reshape(count_y, count_z, piece_x, block_y, block_z)
        spec = spec.transpose(2, 0, 3, 1, 4).reshape(piece_x, length_y, length_z)
        spec = along("kz,xyz->xyk", table_z, spec)
        spec = along("ky,xyz->xkz", table_y, spec)
        first_x = index * block_x + p * piece_x
        freq_x = signed_freq(first_x + jnp.arange(piece_x, dtype=jnp.int32), length_x)
        kernel = dipole_block(freq_y[None, :, None], freq_z[None, None, :], freq_x[:, None, None])
        spec = spec * kernel
        spec = along("ky,xyz->xkz", table_y, spec)
        spec = along("kz,xyz->xyk", table_z, spec)
        spec = spec.reshape(piece_x, count_y, block_y, count_z, block_z)
        spec = spec.transpose(1, 3, 0, 2, 4).reshape(parts, piece_x, block_y, block_z)
        spec = lax.all_to_all(spec, ("gy", "gz"), 0, 0, tiled=True)
        part = along("sxn,sxyz->yzn", table_x[:, p], spec)
        result = part if result is None else result + part
    return result * scale, lam


def per_device(mag_start, mag_middle, adjoint_end, phase, labels):
    phase_grad, finish, halos = backward_sections(mag_start, mag_middle, adjoint_end, phase, labels)
    chi_grad, lam = dipole_adjoint(phase_grad, finish, halos)
    return (lam, chi_grad)


def solution(mesh):
    return jax.shard_map(
        per_device,
        mesh=mesh,
        in_specs=(
            P(None, "gy", "gz", None),
            P(None, "gy", "gz", None),
            P(None, "gy", "gz", None),
            P("gy", "gz", None),
            P("gy", "gz", None),
        ),
        out_specs=(P(None, "gy", "gz", None), P("gy", "gz", None)),
        check_vma=False,
    )
```

```python
import functools
import math

import jax
import numpy as np
import jax.numpy as jnp
from jax import lax
from jax.experimental import pallas as pl
from jax.experimental.pallas import tpu as pltpu
from jax.sharding import PartitionSpec as P


def signed_freq(index, length):
    return jnp.where(index < length // 2, index, index - length)


def dipole_block(freq_y, freq_z, freq_x):
    square_z = freq_z * freq_z
    total = freq_y * freq_y + square_z + freq_x * freq_x
    ratio = square_z.astype(jnp.float32) / jnp.maximum(total, 1).astype(jnp.float32)
    return jnp.where(total == 0, jnp.float32(0.0), jnp.float32(1.0 / 3.0) - ratio)


def cas_table(length):
    index = jnp.arange(length, dtype=jnp.int32)
    product = index[:, None] * index[None, :] % length
    angle = product.astype(jnp.float32) * (2.0 * math.pi / length)
    return jnp.cos(angle) + jnp.sin(angle)


def along(spec, table, values):
    return jnp.einsum(spec, table, values, precision=lax.Precision.HIGH)


def plane_update(centre, below, above, z_low, z_high):
    length_z, length_x = centre.shape
    up = pltpu.roll(centre, 1, 0)
    down = pltpu.roll(centre, length_z - 1, 0)
    if length_z > 8:
        row = lax.broadcasted_iota(jnp.int32, (8, length_x), 0)
        up = jnp.concatenate([jnp.where(row == 0, z_low, up[:8]), up[8:]], axis=0)
        down = jnp.concatenate([down[:length_z - 8], jnp.where(row == 7, z_high, down[length_z - 8:])], axis=0)
    else:
        row = lax.broadcasted_iota(jnp.int32, centre.shape, 0)
        up = jnp.where(row == 0, z_low, up)
        down = jnp.where(row == length_z - 1, z_high, down)
    total = below + above + up + down
    total = total + pltpu.roll(centre, 1, 1) + pltpu.roll(centre, length_x - 1, 1)
    return centre + 0.15 * (total - 6.0 * centre)


def neighbour_planes(cur_ref, prev_ref, next_ref, y_low_ref, y_high_ref, rows, field, comp, r, step, last):
    if isinstance(r, int) and r == 0:
        below = jnp.where(step == 0, y_low_ref[field], prev_ref[comp, 0])
    else:
        below = cur_ref[comp, r - 1]
    if isinstance(r, int) and r == rows - 1:
        above = jnp.where(step == last, y_high_ref[field], next_ref[comp, 0])
    else:
        above = cur_ref[comp, r + 1]
    return below, above


def write_edges(step, last, rows, r, values, y_first_ref, y_last_ref, z_first_ref, z_last_ref):
    for c, value in enumerate(values):
        z_first_ref[c, r] = value[0:1]
        z_last_ref[c, r] = value[value.shape[0] - 1:]
    if isinstance(r, int) and r == 0:
        @pl.when(step == 0)
        def _():
            for c, value in enumerate(values):
                y_first_ref[c] = value
    if isinstance(r, int) and r == rows - 1:
        @pl.when(step == last)
        def _():
            for c, value in enumerate(values):
                y_last_ref[c] = value


def for_rows(rows, body):
    body(0)
    if rows > 2:
        def loop_body(r, carry):
            body(r)
            return carry
        lax.fori_loop(1, rows - 1, loop_body, 0)
    if rows > 1:
        body(rows - 1)


def sin_cos(x):
    k = jnp.floor(x * (2.0 / math.pi) + 0.5)
    r = (x - k * 1.5707963705062866) - k * (-4.371139000186243e-08)
    r2 = r * r
    s = r + r * r2 * (-1.0 / 6.0 + r2 * (1.0 / 120.0 + r2 * (-1.0 / 5040.0 + r2 * (1.0 / 362880.0))))
    c = 1.0 + r2 * (-0.5 + r2 * (1.0 / 24.0 + r2 * (-1.0 / 720.0 + r2 * (1.0 / 40320.0
                                                                        + r2 * (-1.0 / 3628800.0)))))
    quadrant = k.astype(jnp.int32) & 3
    swap = (quadrant & 1) == 1
    sin_x = jnp.where(swap, c, s)
    cos_x = jnp.where(swap, s, c)
    sin_x = jnp.where(quadrant >= 2, -sin_x, sin_x)
    cos_x = jnp.where((quadrant == 1) | (quadrant == 2), -cos_x, cos_x)
    return sin_x, cos_x


def step_factor(labels, phase):
    decays = [float(np.exp(-np.float32(rate))) for rate in (0.02, 0.3, 0.6, 1.2)]
    decay = jnp.where(labels == 1, decays[1], decays[0])
    decay = jnp.where(labels == 2, decays[2], decay)
    decay = jnp.where(labels == 3, decays[3], decay).astype(jnp.float32)
    sin_p, cos_p = sin_cos(phase)
    return decay * cos_p, decay * sin_p


def first_w(lam_real, lam_imag, labels, phase):
    f_real, f_imag = step_factor(labels, phase)
    return (f_real * lam_real - f_imag * lam_imag, f_real * lam_imag + f_imag * lam_real), (f_real, f_imag)


def factor_kernel(lam_ref, phase_ref, labels_ref, factor_ref, w_ref, *, rows):
    def body(r, carry):
        (w_real, w_imag), (f_real, f_imag) = first_w(lam_ref[0, r], lam_ref[1, r], labels_ref[r], phase_ref[r])
        factor_ref[0, r] = f_real
        factor_ref[1, r] = f_imag
        w_ref[0, r] = w_real
        w_ref[1, r] = w_imag
        return carry
    lax.fori_loop(0, rows, body, 0)


def edges_kernel(*refs, rows):
    (mm_y0, mm_y1, mm_z0, mm_z1, ms_y0, ms_y1, ms_z0, ms_z1, lam_y0, lam_y1, lam_z0, lam_z1,
     ph_y0, ph_y1, ph_z0, ph_z1, lb_y0, lb_y1, lb_z0, lb_z1,
     y_first_ref, y_last_ref, z_first_ref, z_last_ref) = refs

    @pl.when(pl.program_id(0) == 0)
    def _():
        for out_ref, m1, m2, lam, ph, lb in ((y_first_ref, mm_y0, ms_y0, lam_y0, ph_y0, lb_y0),
                                           (y_last_ref, mm_y1, ms_y1, lam_y1, ph_y1, lb_y1)):
            (w_real, w_imag), _ = first_w(lam[0, 0], lam[1, 0], lb[0], ph[0])
            planes = [m1[0, 0], m1[1, 0], m2[0, 0], m2[1, 0], w_real, w_imag]
            for c, value in enumerate(planes):
                out_ref[c] = value

    def body(r, carry):
        for out_ref, m1, m2, lam, ph, lb, at in ((z_first_ref, mm_z0, ms_z0, lam_z0, ph_z0, lb_z0, 0),
                                               (z_last_ref, mm_z1, ms_z1, lam_z1, ph_z1, lb_z1, 7)):
            (w_real, w_imag), _ = first_w(lam[0, r], lam[1, r], lb[r], ph[r])
            tiles = [m1[0, r], m1[1, r], m2[0, r], m2[1, r], w_real, w_imag]
            for c, value in enumerate(tiles):
                out_ref[c, r] = value[at:at + 1]
        return carry
    lax.fori_loop(0, rows, body, 0)


def edge_specs_of(ndim, length_y, length_z, length_x, rows):
    lead = (2,) if ndim == 4 else ()
    zero = (0,) * len(lead)
    tiles = length_z // 8
    return [
        pl.BlockSpec(lead + (1, length_z, length_x), lambda i: zero + (0, 0, 0)),
        pl.BlockSpec(lead + (1, length_z, length_x), lambda i: zero + (length_y - 1, 0, 0)),
        pl.BlockSpec(lead + (rows, 8, length_x), lambda i: zero + (i, 0, 0)),
        pl.BlockSpec(lead + (rows, 8, length_x), lambda i: zero + (i, tiles - 1, 0)),
    ]


def edge_outputs(comps, length_y, length_z, length_x, rows):
    plane = jax.ShapeDtypeStruct((comps, length_z, length_x), jnp.float32)
    row = jax.ShapeDtypeStruct((comps, length_y, 1, length_x), jnp.float32)
    plane_spec = pl.BlockSpec((comps, length_z, length_x), lambda i: (0, 0, 0))
    row_spec = pl.BlockSpec((comps, rows, 1, length_x), lambda i: (0, i, 0, 0))
    return [plane, plane, row, row], [plane_spec, plane_spec, row_spec, row_spec]


def first_kernel(*refs, rows):
    (mm_ref, mm_prev, mm_next, ms_ref, ms_prev, ms_next, w_ref, w_prev, w_next,
     factor_ref, y_low_ref, y_high_ref, z_low_ref, z_high_ref, pg_ref, w2_ref) = refs[:16]
    step = pl.program_id(0)
    last = pl.num_programs(0) - 1
    fields = ((mm_ref, mm_prev, mm_next), (ms_ref, ms_prev, ms_next), (w_ref, w_prev, w_next))

    def body(r):
        new = []
        for f, (cur, prev, nxt) in enumerate(fields):
            pair = []
            for comp in range(2):
                below, above = neighbour_planes(cur, prev, nxt, y_low_ref, y_high_ref, rows, 2 * f + comp, comp, r,
                                                step, last)
                pair.append(plane_update(cur[comp, r], below, above,
                                         z_low_ref[2 * f + comp, r], z_high_ref[2 * f + comp, r]))
            new.append(pair)
        (u1_real, u1_imag), (u2_real, u2_imag), (lam_real, lam_imag) = new
        w_real = w_ref[0, r]
        w_imag = w_ref[1, r]
        f_real = factor_ref[0, r]
        f_imag = factor_ref[1, r]
        w2_real = f_real * lam_real - f_imag * lam_imag
        w2_imag = f_real * lam_imag + f_imag * lam_real
        grad = w_real * u1_imag - w_imag * u1_real
        pg_ref[r] = grad + (w2_real * u2_imag - w2_imag * u2_real)
        w2_ref[0, r] = w2_real
        w2_ref[1, r] = w2_imag
        write_edges(step, last, rows, r, [w2_real, w2_imag], *refs[16:])

    for_rows(rows, body)


def second_kernel(w_ref, w_prev, w_next, y_low_ref, y_high_ref, z_low_ref, z_high_ref, out_ref, *, rows):
    step = pl.program_id(0)
    last = pl.num_programs(0) - 1

    def body(r):
        for comp in range(2):
            below, above = neighbour_planes(w_ref, w_prev, w_next, y_low_ref, y_high_ref, rows, comp, comp, r,
                                            step, last)
            out_ref[comp, r] = plane_update(w_ref[comp, r], below, above,
                                            z_low_ref[comp, r], z_high_ref[comp, r])

    for_rows(rows, body)


def block_rows(length_y):
    rows = 8
    while length_y % rows:
        rows //= 2
    return rows


def field_specs(shape, rows):
    comps, length_y, length_z, length_x = shape
    cur = pl.BlockSpec((comps, rows, length_z, length_x), lambda i: (0, i, 0, 0))
    prev = pl.BlockSpec((comps, 1, length_z, length_x),
                        lambda i: (0, jnp.maximum(i * rows - 1, 0), 0, 0))
    nxt = pl.BlockSpec((comps, 1, length_z, length_x),
                       lambda i: (0, jnp.minimum(i * rows + rows, length_y - 1), 0, 0))
    return [cur, prev, nxt]


def send_edges(y_first, y_last, z_first, z_last):
    results = []
    for axis, first, last in (("gy", y_first, y_last), ("gz", z_first, z_last)):
        count = lax.axis_size(axis)
        up = [(i, (i + 1) % count) for i in range(count)]
        down = [(j, i) for i, j in up]
        if count == 2:
            both = lax.ppermute(jnp.stack([last, first]), axis, up)
            results.extend([both[0], both[1]])
        else:
            results.extend([lax.ppermute(last, axis, up), lax.ppermute(first, axis, down)])
    return results


def backward_sections(mag_start, mag_middle, adjoint_end, phase, labels):
    _, length_y, length_z, length_x = mag_start.shape
    rows = block_rows(length_y)
    grid = (length_y // rows,)
    plane = jax.ShapeDtypeStruct((length_y, length_z, length_x), jnp.float32)
    pair = jax.ShapeDtypeStruct((2, length_y, length_z, length_x), jnp.float32)
    cur = pl.BlockSpec((2, rows, length_z, length_x), lambda i: (0, i, 0, 0))
    cur_plane = pl.BlockSpec((rows, length_z, length_x), lambda i: (i, 0, 0))
    whole = lambda shape: pl.BlockSpec(shape, lambda i: (0,) * len(shape))
    zspec = lambda comps: pl.BlockSpec((comps, rows, 1, length_x), lambda i: (0, i, 0, 0))
    edge_shapes, edge_specs = edge_outputs(2, length_y, length_z, length_x, rows)
    six_shapes, six_specs = edge_outputs(6, length_y, length_z, length_x, rows)
    inputs = (mag_middle, mag_start, adjoint_end, phase, labels)
    edge_rows = length_y
    six_shapes, six_specs = edge_outputs(6, length_y, length_z, length_x, edge_rows)
    edges = pl.pallas_call(
        functools.partial(edges_kernel, rows=edge_rows),
        grid=(1,),
        in_specs=[s for a in inputs for s in edge_specs_of(a.ndim, length_y, length_z, length_x, edge_rows)],
        out_specs=six_specs,
        out_shape=six_shapes,
    )(*[a for a in inputs for _ in range(4)])
    halos = send_edges(*edges)
    factor, w_first = pl.pallas_call(
        functools.partial(factor_kernel, rows=rows),
        grid=grid,
        in_specs=[cur, cur_plane, cur_plane],
        out_specs=[cur, cur],
        out_shape=[pair, pair],
    )(adjoint_end, phase, labels)
    phase_grad, w_second, *w2_edges = pl.pallas_call(
        functools.partial(first_kernel, rows=rows),
        grid=grid,
        in_specs=field_specs(mag_middle.shape, rows) + field_specs(mag_start.shape, rows)
        + field_specs(w_first.shape, rows)
        + [cur, whole((6, length_z, length_x)), whole((6, length_z, length_x)), zspec(6), zspec(6)],
        out_specs=[cur_plane, cur] + edge_specs,
        out_shape=[plane, pair] + edge_shapes,
    )(mag_middle, mag_middle, mag_middle, mag_start, mag_start, mag_start,
      w_first, w_first, w_first, factor, *halos)
    halos = send_edges(*w2_edges)
    return phase_grad, functools.partial(finish_lambda, w_second, rows, grid, cur, whole, zspec, length_z, length_x), halos


def finish_lambda(w_second, rows, grid, cur, whole, zspec, length_z, length_x, halos):
    pair = jax.ShapeDtypeStruct(w_second.shape, jnp.float32)
    lam = pl.pallas_call(
        functools.partial(second_kernel, rows=rows),
        grid=grid,
        in_specs=field_specs(w_second.shape, rows)
        + [whole((2, length_z, length_x)), whole((2, length_z, length_x)), zspec(2), zspec(2)],
        out_specs=cur,
        out_shape=pair,
    )(w_second, w_second, w_second, *halos)
    return lam


def dipole_adjoint(phase_grad, finish, halos):
    count_y = lax.axis_size("gy")
    count_z = lax.axis_size("gz")
    parts = count_y * count_z
    block_y, block_z, length_x = phase_grad.shape
    length_y = block_y * count_y
    length_z = block_z * count_z
    block_x = length_x // parts
    pieces = 2 if block_x % 2 == 0 else 1
    piece_x = block_x // pieces
    table_x = cas_table(length_x).reshape(parts, pieces, piece_x, length_x)
    table_y = cas_table(length_y)
    table_z = cas_table(length_z)
    scale = 1.0 / (float(length_y) * float(length_z) * float(length_x))
    freq_y = signed_freq(jnp.arange(length_y, dtype=jnp.int32), length_y)
    freq_z = signed_freq(jnp.arange(length_z, dtype=jnp.int32), length_z)
    index = lax.axis_index("gy") * count_z + lax.axis_index("gz")
    sent = []
    for p in range(pieces):
        spec = along("sxn,yzn->sxyz", table_x[:, p], phase_grad)
        if p == 0:
            halos, spec = lax.optimization_barrier((halos, spec))
        sent.append(lax.all_to_all(spec, ("gy", "gz"), 0, 0, tiled=True))
        if p == 0:
            lam = finish(halos)
    result = None
    for p in range(pieces):
        spec = sent[p].reshape(count_y, count_z, piece_x, block_y, block_z)
        spec = spec.transpose(2, 0, 3, 1, 4).reshape(piece_x, length_y, length_z)
        spec = along("kz,xyz->xyk", table_z, spec)
        spec = along("ky,xyz->xkz", table_y, spec)
        first_x = index * block_x + p * piece_x
        freq_x = signed_freq(first_x + jnp.arange(piece_x, dtype=jnp.int32), length_x)
        kernel = dipole_block(freq_y[None, :, None], freq_z[None, None, :], freq_x[:, None, None])
        spec = spec * kernel
        spec = along("ky,xyz->xkz", table_y, spec)
        spec = along("kz,xyz->xyk", table_z, spec)
        spec = spec.reshape(piece_x, count_y, block_y, count_z, block_z)
        spec = spec.transpose(1, 3, 0, 2, 4).reshape(parts, piece_x, block_y, block_z)
        spec = lax.all_to_all(spec, ("gy", "gz"), 0, 0, tiled=True)
        part = along("sxn,sxyz->yzn", table_x[:, p], spec)
        result = part if result is None else result + part
    return result * scale, lam


def per_device(mag_start, mag_middle, adjoint_end, phase, labels):
    phase_grad, finish, halos = backward_sections(mag_start, mag_middle, adjoint_end, phase, labels)
    chi_grad, lam = dipole_adjoint(phase_grad, finish, halos)
    return (lam, chi_grad)


def solution(mesh):
    return jax.shard_map(
        per_device,
        mesh=mesh,
        in_specs=(
            P(None, "gy", "gz", None),
            P(None, "gy", "gz", None),
            P(None, "gy", "gz", None),
            P("gy", "gz", None),
            P("gy", "gz", None),
        ),
        out_specs=(P(None, "gy", "gz", None), P("gy", "gz", None)),
        check_vma=False,
    )
```

```python
import functools
import math

import jax
import numpy as np
import jax.numpy as jnp
from jax import lax
from jax.experimental import pallas as pl
from jax.experimental.pallas import tpu as pltpu
from jax.sharding import PartitionSpec as P


def signed_freq(index, length):
    return jnp.where(index < length // 2, index, index - length)


def dipole_block(freq_y, freq_z, freq_x):
    square_z = freq_z * freq_z
    total = freq_y * freq_y + square_z + freq_x * freq_x
    ratio = square_z.astype(jnp.float32) / jnp.maximum(total, 1).astype(jnp.float32)
    return jnp.where(total == 0, jnp.float32(0.0), jnp.float32(1.0 / 3.0) - ratio)


def cas_table(length):
    index = jnp.arange(length, dtype=jnp.int32)
    product = index[:, None] * index[None, :] % length
    angle = product.astype(jnp.float32) * (2.0 * math.pi / length)
    return jnp.cos(angle) + jnp.sin(angle)


def along(spec, table, values):
    return jnp.einsum(spec, table, values, precision=lax.Precision.HIGH)


def plane_update(centre, below, above, z_low, z_high):
    length_z, length_x = centre.shape
    up = pltpu.roll(centre, 1, 0)
    down = pltpu.roll(centre, length_z - 1, 0)
    if length_z > 8:
        row = lax.broadcasted_iota(jnp.int32, (8, length_x), 0)
        up = jnp.concatenate([jnp.where(row == 0, z_low, up[:8]), up[8:]], axis=0)
        down = jnp.concatenate([down[:length_z - 8], jnp.where(row == 7, z_high, down[length_z - 8:])], axis=0)
    else:
        row = lax.broadcasted_iota(jnp.int32, centre.shape, 0)
        up = jnp.where(row == 0, z_low, up)
        down = jnp.where(row == length_z - 1, z_high, down)
    total = below + above + up + down
    total = total + pltpu.roll(centre, 1, 1) + pltpu.roll(centre, length_x - 1, 1)
    return centre + 0.15 * (total - 6.0 * centre)


def neighbour_planes(cur_ref, prev_ref, next_ref, y_low_ref, y_high_ref, rows, field, comp, r, step, last):
    if isinstance(r, int) and r == 0:
        below = jnp.where(step == 0, y_low_ref[field], prev_ref[comp, 0])
    else:
        below = cur_ref[comp, r - 1]
    if isinstance(r, int) and r == rows - 1:
        above = jnp.where(step == last, y_high_ref[field], next_ref[comp, 0])
    else:
        above = cur_ref[comp, r + 1]
    return below, above


def write_edges(step, last, rows, r, values, y_first_ref, y_last_ref, z_first_ref, z_last_ref):
    for c, value in enumerate(values):
        z_first_ref[c, r] = value[0:1]
        z_last_ref[c, r] = value[value.shape[0] - 1:]
    if isinstance(r, int) and r == 0:
        @pl.when(step == 0)
        def _():
            for c, value in enumerate(values):
                y_first_ref[c] = value
    if isinstance(r, int) and r == rows - 1:
        @pl.when(step == last)
        def _():
            for c, value in enumerate(values):
                y_last_ref[c] = value


def for_rows(rows, body):
    body(0)
    if rows > 2:
        def loop_body(r, carry):
            body(r)
            return carry
        lax.fori_loop(1, rows - 1, loop_body, 0)
    if rows > 1:
        body(rows - 1)


def sin_cos(x):
    k = jnp.floor(x * (2.0 / math.pi) + 0.5)
    r = (x - k * 1.5707963705062866) - k * (-4.371139000186243e-08)
    r2 = r * r
    s = r + r * r2 * (-1.0 / 6.0 + r2 * (1.0 / 120.0 + r2 * (-1.0 / 5040.0 + r2 * (1.0 / 362880.0))))
    c = 1.0 + r2 * (-0.5 + r2 * (1.0 / 24.0 + r2 * (-1.0 / 720.0 + r2 * (1.0 / 40320.0
                                                                        + r2 * (-1.0 / 3628800.0)))))
    quadrant = k.astype(jnp.int32) & 3
    swap = (quadrant & 1) == 1
    sin_x = jnp.where(swap, c, s)
    cos_x = jnp.where(swap, s, c)
    sin_x = jnp.where(quadrant >= 2, -sin_x, sin_x)
    cos_x = jnp.where((quadrant == 1) | (quadrant == 2), -cos_x, cos_x)
    return sin_x, cos_x


def step_factor(labels, phase):
    decays = [float(np.exp(-np.float32(rate))) for rate in (0.02, 0.3, 0.6, 1.2)]
    decay = jnp.where(labels == 1, decays[1], decays[0])
    decay = jnp.where(labels == 2, decays[2], decay)
    decay = jnp.where(labels == 3, decays[3], decay).astype(jnp.float32)
    sin_p, cos_p = sin_cos(phase)
    return decay * cos_p, decay * sin_p


def first_w(lam_real, lam_imag, labels, phase):
    f_real, f_imag = step_factor(labels, phase)
    return (f_real * lam_real - f_imag * lam_imag, f_real * lam_imag + f_imag * lam_real), (f_real, f_imag)


def factor_kernel(lam_ref, phase_ref, labels_ref, factor_ref, w_ref, *, rows):
    def body(r, carry):
        (w_real, w_imag), (f_real, f_imag) = first_w(lam_ref[0, r], lam_ref[1, r], labels_ref[r], phase_ref[r])
        factor_ref[0, r] = f_real
        factor_ref[1, r] = f_imag
        w_ref[0, r] = w_real
        w_ref[1, r] = w_imag
        return carry
    lax.fori_loop(0, rows, body, 0)


def edges_kernel(*refs, rows):
    (mm_y0, mm_y1, mm_z0, mm_z1, ms_y0, ms_y1, ms_z0, ms_z1, lam_y0, lam_y1, lam_z0, lam_z1,
     ph_y0, ph_y1, ph_z0, ph_z1, lb_y0, lb_y1, lb_z0, lb_z1,
     y_first_ref, y_last_ref, z_first_ref, z_last_ref) = refs

    @pl.when(pl.program_id(0) == 0)
    def _():
        for out_ref, m1, m2, lam, ph, lb in ((y_first_ref, mm_y0, ms_y0, lam_y0, ph_y0, lb_y0),
                                           (y_last_ref, mm_y1, ms_y1, lam_y1, ph_y1, lb_y1)):
            (w_real, w_imag), _ = first_w(lam[0, 0], lam[1, 0], lb[0], ph[0])
            planes = [m1[0, 0], m1[1, 0], m2[0, 0], m2[1, 0], w_real, w_imag]
            for c, value in enumerate(planes):
                out_ref[c] = value

    def body(r, carry):
        for out_ref, m1, m2, lam, ph, lb, at in ((z_first_ref, mm_z0, ms_z0, lam_z0, ph_z0, lb_z0, 0),
                                               (z_last_ref, mm_z1, ms_z1, lam_z1, ph_z1, lb_z1, 7)):
            (w_real, w_imag), _ = first_w(lam[0, r], lam[1, r], lb[r], ph[r])
            tiles = [m1[0, r], m1[1, r], m2[0, r], m2[1, r], w_real, w_imag]
            for c, value in enumerate(tiles):
                out_ref[c, r] = value[at:at + 1]
        return carry
    lax.fori_loop(0, rows, body, 0)


def edge_specs_of(ndim, length_y, length_z, length_x, rows):
    lead = (2,) if ndim == 4 else ()
    zero = (0,) * len(lead)
    tiles = length_z // 8
    return [
        pl.BlockSpec(lead + (1, length_z, length_x), lambda i: zero + (0, 0, 0)),
        pl.BlockSpec(lead + (1, length_z, length_x), lambda i: zero + (length_y - 1, 0, 0)),
        pl.BlockSpec(lead + (rows, 8, length_x), lambda i: zero + (i, 0, 0)),
        pl.BlockSpec(lead + (rows, 8, length_x), lambda i: zero + (i, tiles - 1, 0)),
    ]


def edge_outputs(comps, length_y, length_z, length_x, rows):
    plane = jax.ShapeDtypeStruct((comps, length_z, length_x), jnp.float32)
    row = jax.ShapeDtypeStruct((comps, length_y, 1, length_x), jnp.float32)
    plane_spec = pl.BlockSpec((comps, length_z, length_x), lambda i: (0, 0, 0))
    row_spec = pl.BlockSpec((comps, rows, 1, length_x), lambda i: (0, i, 0, 0))
    return [plane, plane, row, row], [plane_spec, plane_spec, row_spec, row_spec]


def first_kernel(*refs, rows):
    (mm_ref, mm_prev, mm_next, ms_ref, ms_prev, ms_next, w_ref, w_prev, w_next,
     factor_ref, y_low_ref, y_high_ref, z_low_ref, z_high_ref, pg_ref, w2_ref) = refs[:16]
    step = pl.program_id(0)
    last = pl.num_programs(0) - 1
    fields = ((mm_ref, mm_prev, mm_next), (ms_ref, ms_prev, ms_next), (w_ref, w_prev, w_next))

    def body(r):
        new = []
        for f, (cur, prev, nxt) in enumerate(fields):
            pair = []
            for comp in range(2):
                below, above = neighbour_planes(cur, prev, nxt, y_low_ref, y_high_ref, rows, 2 * f + comp, comp, r,
                                                step, last)
                pair.append(plane_update(cur[comp, r], below, above,
                                         z_low_ref[2 * f + comp, r], z_high_ref[2 * f + comp, r]))
            new.append(pair)
        (u1_real, u1_imag), (u2_real, u2_imag), (lam_real, lam_imag) = new
        w_real = w_ref[0, r]
        w_imag = w_ref[1, r]
        f_real = factor_ref[0, r]
        f_imag = factor_ref[1, r]
        w2_real = f_real * lam_real - f_imag * lam_imag
        w2_imag = f_real * lam_imag + f_imag * lam_real
        grad = w_real * u1_imag - w_imag * u1_real
        pg_ref[r] = grad + (w2_real * u2_imag - w2_imag * u2_real)
        w2_ref[0, r] = w2_real
        w2_ref[1, r] = w2_imag
        write_edges(step, last, rows, r, [w2_real, w2_imag], *refs[16:])

    for_rows(rows, body)


def second_kernel(w_ref, w_prev, w_next, y_low_ref, y_high_ref, z_low_ref, z_high_ref, out_ref, *, rows):
    step = pl.program_id(0)
    last = pl.num_programs(0) - 1

    def body(r):
        for comp in range(2):
            below, above = neighbour_planes(w_ref, w_prev, w_next, y_low_ref, y_high_ref, rows, comp, comp, r,
                                            step, last)
            out_ref[comp, r] = plane_update(w_ref[comp, r], below, above,
                                            z_low_ref[comp, r], z_high_ref[comp, r])

    for_rows(rows, body)


def block_rows(length_y):
    rows = 4
    while length_y % rows:
        rows //= 2
    return rows


def field_specs(shape, rows):
    comps, length_y, length_z, length_x = shape
    cur = pl.BlockSpec((comps, rows, length_z, length_x), lambda i: (0, i, 0, 0))
    prev = pl.BlockSpec((comps, 1, length_z, length_x),
                        lambda i: (0, jnp.maximum(i * rows - 1, 0), 0, 0))
    nxt = pl.BlockSpec((comps, 1, length_z, length_x),
                       lambda i: (0, jnp.minimum(i * rows + rows, length_y - 1), 0, 0))
    return [cur, prev, nxt]


def send_edges(y_first, y_last, z_first, z_last):
    results = []
    for axis, first, last in (("gy", y_first, y_last), ("gz", z_first, z_last)):
        count = lax.axis_size(axis)
        up = [(i, (i + 1) % count) for i in range(count)]
        down = [(j, i) for i, j in up]
        if count == 2:
            both = lax.ppermute(jnp.stack([last, first]), axis, up)
            results.extend([both[0], both[1]])
        else:
            results.extend([lax.ppermute(last, axis, up), lax.ppermute(first, axis, down)])
    return results


def backward_sections(mag_start, mag_middle, adjoint_end, phase, labels):
    _, length_y, length_z, length_x = mag_start.shape
    rows = block_rows(length_y)
    grid = (length_y // rows,)
    plane = jax.ShapeDtypeStruct((length_y, length_z, length_x), jnp.float32)
    pair = jax.ShapeDtypeStruct((2, length_y, length_z, length_x), jnp.float32)
    cur = pl.BlockSpec((2, rows, length_z, length_x), lambda i: (0, i, 0, 0))
    cur_plane = pl.BlockSpec((rows, length_z, length_x), lambda i: (i, 0, 0))
    whole = lambda shape: pl.BlockSpec(shape, lambda i: (0,) * len(shape))
    zspec = lambda comps: pl.BlockSpec((comps, rows, 1, length_x), lambda i: (0, i, 0, 0))
    edge_shapes, edge_specs = edge_outputs(2, length_y, length_z, length_x, rows)
    six_shapes, six_specs = edge_outputs(6, length_y, length_z, length_x, rows)
    inputs = (mag_middle, mag_start, adjoint_end, phase, labels)
    edges = pl.pallas_call(
        functools.partial(edges_kernel, rows=rows),
        grid=grid,
        in_specs=[s for a in inputs for s in edge_specs_of(a.ndim, length_y, length_z, length_x, rows)],
        out_specs=six_specs,
        out_shape=six_shapes,
    )(*[a for a in inputs for _ in range(4)])
    halos = send_edges(*edges)
    factor, w_first = pl.pallas_call(
        functools.partial(factor_kernel, rows=rows),
        grid=grid,
        in_specs=[cur, cur_plane, cur_plane],
        out_specs=[cur, cur],
        out_shape=[pair, pair],
    )(adjoint_end, phase, labels)
    phase_grad, w_second, *w2_edges = pl.pallas_call(
        functools.partial(first_kernel, rows=rows),
        grid=grid,
        in_specs=field_specs(mag_middle.shape, rows) + field_specs(mag_start.shape, rows)
        + field_specs(w_first.shape, rows)
        + [cur, whole((6, length_z, length_x)), whole((6, length_z, length_x)), zspec(6), zspec(6)],
        out_specs=[cur_plane, cur] + edge_specs,
        out_shape=[plane, pair] + edge_shapes,
    )(mag_middle, mag_middle, mag_middle, mag_start, mag_start, mag_start,
      w_first, w_first, w_first, factor, *halos)
    halos = send_edges(*w2_edges)
    return phase_grad, functools.partial(finish_lambda, w_second, rows, grid, cur, whole, zspec, length_z, length_x), halos


def finish_lambda(w_second, rows, grid, cur, whole, zspec, length_z, length_x, halos):
    pair = jax.ShapeDtypeStruct(w_second.shape, jnp.float32)
    lam = pl.pallas_call(
        functools.partial(second_kernel, rows=rows),
        grid=grid,
        in_specs=field_specs(w_second.shape, rows)
        + [whole((2, length_z, length_x)), whole((2, length_z, length_x)), zspec(2), zspec(2)],
        out_specs=cur,
        out_shape=pair,
    )(w_second, w_second, w_second, *halos)
    return lam


def dipole_adjoint(phase_grad, finish, halos):
    count_y = lax.axis_size("gy")
    count_z = lax.axis_size("gz")
    parts = count_y * count_z
    block_y, block_z, length_x = phase_grad.shape
    length_y = block_y * count_y
    length_z = block_z * count_z
    block_x = length_x // parts
    pieces = 2 if block_x % 2 == 0 else 1
    piece_x = block_x // pieces
    table_x = cas_table(length_x).reshape(parts, pieces, piece_x, length_x)
    table_y = cas_table(length_y)
    table_z = cas_table(length_z)
    scale = 1.0 / (float(length_y) * float(length_z) * float(length_x))
    freq_y = signed_freq(jnp.arange(length_y, dtype=jnp.int32), length_y)
    freq_z = signed_freq(jnp.arange(length_z, dtype=jnp.int32), length_z)
    index = lax.axis_index("gy") * count_z + lax.axis_index("gz")
    sent = []
    for p in range(pieces):
        spec = along("sxn,yzn->sxyz", table_x[:, p], phase_grad)
        if p == 0:
            halos, spec = lax.optimization_barrier((halos, spec))
        sent.append(lax.all_to_all(spec, ("gy", "gz"), 0, 0, tiled=True))
        if p == 0:
            lam = finish(halos)
    result = None
    for p in range(pieces):
        spec = sent[p].reshape(count_y, count_z, piece_x, block_y, block_z)
        spec = spec.transpose(2, 0, 3, 1, 4).reshape(piece_x, length_y, length_z)
        spec = along("kz,xyz->xyk", table_z, spec)
        spec = along("ky,xyz->xkz", table_y, spec)
        first_x = index * block_x + p * piece_x
        freq_x = signed_freq(first_x + jnp.arange(piece_x, dtype=jnp.int32), length_x)
        kernel = dipole_block(freq_y[None, :, None], freq_z[None, None, :], freq_x[:, None, None])
        spec = spec * kernel
        spec = along("ky,xyz->xkz", table_y, spec)
        spec = along("kz,xyz->xyk", table_z, spec)
        spec = spec.reshape(piece_x, count_y, block_y, count_z, block_z)
        spec = spec.transpose(1, 3, 0, 2, 4).reshape(parts, piece_x, block_y, block_z)
        spec = lax.all_to_all(spec, ("gy", "gz"), 0, 0, tiled=True)
        part = along("sxn,sxyz->yzn", table_x[:, p], spec)
        result = part if result is None else result + part
    return result * scale, lam


def per_device(mag_start, mag_middle, adjoint_end, phase, labels):
    phase_grad, finish, halos = backward_sections(mag_start, mag_middle, adjoint_end, phase, labels)
    chi_grad, lam = dipole_adjoint(phase_grad, finish, halos)
    return (lam, chi_grad)


def solution(mesh):
    return jax.shard_map(
        per_device,
        mesh=mesh,
        in_specs=(
            P(None, "gy", "gz", None),
            P(None, "gy", "gz", None),
            P(None, "gy", "gz", None),
            P("gy", "gz", None),
            P("gy", "gz", None),
        ),
        out_specs=(P(None, "gy", "gz", None), P("gy", "gz", None)),
        check_vma=False,
    )
```

```python
import functools
import math

import jax
import numpy as np
import jax.numpy as jnp
from jax import lax
from jax.experimental import pallas as pl
from jax.experimental.pallas import tpu as pltpu
from jax.sharding import PartitionSpec as P


def signed_freq(index, length):
    return jnp.where(index < length // 2, index, index - length)


def dipole_block(freq_y, freq_z, freq_x):
    square_z = freq_z * freq_z
    total = freq_y * freq_y + square_z + freq_x * freq_x
    ratio = square_z.astype(jnp.float32) / jnp.maximum(total, 1).astype(jnp.float32)
    return jnp.where(total == 0, jnp.float32(0.0), jnp.float32(1.0 / 3.0) - ratio)


def cas_table(length):
    index = jnp.arange(length, dtype=jnp.int32)
    product = index[:, None] * index[None, :] % length
    angle = product.astype(jnp.float32) * (2.0 * math.pi / length)
    return jnp.cos(angle) + jnp.sin(angle)


def along(spec, table, values):
    return jnp.einsum(spec, table, values, precision=lax.Precision.HIGH)


def plane_update(centre, below, above, z_low, z_high):
    length_z, length_x = centre.shape
    up = pltpu.roll(centre, 1, 0)
    down = pltpu.roll(centre, length_z - 1, 0)
    if length_z > 8:
        row = lax.broadcasted_iota(jnp.int32, (8, length_x), 0)
        up = jnp.concatenate([jnp.where(row == 0, z_low, up[:8]), up[8:]], axis=0)
        down = jnp.concatenate([down[:length_z - 8], jnp.where(row == 7, z_high, down[length_z - 8:])], axis=0)
    else:
        row = lax.broadcasted_iota(jnp.int32, centre.shape, 0)
        up = jnp.where(row == 0, z_low, up)
        down = jnp.where(row == length_z - 1, z_high, down)
    total = below + above + up + down
    total = total + pltpu.roll(centre, 1, 1) + pltpu.roll(centre, length_x - 1, 1)
    return centre + 0.15 * (total - 6.0 * centre)


def neighbour_planes(cur_ref, prev_ref, next_ref, y_low_ref, y_high_ref, rows, field, comp, r, step, last):
    if isinstance(r, int) and r == 0:
        below = jnp.where(step == 0, y_low_ref[field], prev_ref[comp, 0])
    else:
        below = cur_ref[comp, r - 1]
    if isinstance(r, int) and r == rows - 1:
        above = jnp.where(step == last, y_high_ref[field], next_ref[comp, 0])
    else:
        above = cur_ref[comp, r + 1]
    return below, above


def write_edges(step, last, rows, r, values, y_first_ref, y_last_ref, z_first_ref, z_last_ref):
    for c, value in enumerate(values):
        z_first_ref[c, r] = value[0:1]
        z_last_ref[c, r] = value[value.shape[0] - 1:]
    if isinstance(r, int) and r == 0:
        @pl.when(step == 0)
        def _():
            for c, value in enumerate(values):
                y_first_ref[c] = value
    if isinstance(r, int) and r == rows - 1:
        @pl.when(step == last)
        def _():
            for c, value in enumerate(values):
                y_last_ref[c] = value


def for_rows(rows, body):
    body(0)
    if rows > 2:
        def loop_body(r, carry):
            body(r)
            return carry
        lax.fori_loop(1, rows - 1, loop_body, 0)
    if rows > 1:
        body(rows - 1)


def sin_cos(x):
    k = jnp.floor(x * (2.0 / math.pi) + 0.5)
    r = (x - k * 1.5707963705062866) - k * (-4.371139000186243e-08)
    r2 = r * r
    s = r + r * r2 * (-1.0 / 6.0 + r2 * (1.0 / 120.0 + r2 * (-1.0 / 5040.0 + r2 * (1.0 / 362880.0))))
    c = 1.0 + r2 * (-0.5 + r2 * (1.0 / 24.0 + r2 * (-1.0 / 720.0 + r2 * (1.0 / 40320.0
                                                                        + r2 * (-1.0 / 3628800.0)))))
    quadrant = k.astype(jnp.int32) & 3
    swap = (quadrant & 1) == 1
    sin_x = jnp.where(swap, c, s)
    cos_x = jnp.where(swap, s, c)
    sin_x = jnp.where(quadrant >= 2, -sin_x, sin_x)
    cos_x = jnp.where((quadrant == 1) | (quadrant == 2), -cos_x, cos_x)
    return sin_x, cos_x


def step_factor(labels, phase):
    decays = [float(np.exp(-np.float32(rate))) for rate in (0.02, 0.3, 0.6, 1.2)]
    decay = jnp.where(labels == 1, decays[1], decays[0])
    decay = jnp.where(labels == 2, decays[2], decay)
    decay = jnp.where(labels == 3, decays[3], decay).astype(jnp.float32)
    sin_p, cos_p = sin_cos(phase)
    return decay * cos_p, decay * sin_p


def first_w(lam_real, lam_imag, labels, phase):
    f_real, f_imag = step_factor(labels, phase)
    return (f_real * lam_real - f_imag * lam_imag, f_real * lam_imag + f_imag * lam_real), (f_real, f_imag)


def factor_kernel(lam_ref, phase_ref, labels_ref, factor_ref, w_ref, *, rows):
    def body(r, carry):
        (w_real, w_imag), (f_real, f_imag) = first_w(lam_ref[0, r], lam_ref[1, r], labels_ref[r], phase_ref[r])
        factor_ref[0, r] = f_real
        factor_ref[1, r] = f_imag
        w_ref[0, r] = w_real
        w_ref[1, r] = w_imag
        return carry
    lax.fori_loop(0, rows, body, 0)


def edges_kernel(*refs, rows):
    (mm_y0, mm_y1, mm_z0, mm_z1, ms_y0, ms_y1, ms_z0, ms_z1, lam_y0, lam_y1, lam_z0, lam_z1,
     ph_y0, ph_y1, ph_z0, ph_z1, lb_y0, lb_y1, lb_z0, lb_z1,
     y_first_ref, y_last_ref, z_first_ref, z_last_ref) = refs

    @pl.when(pl.program_id(0) == 0)
    def _():
        for out_ref, m1, m2, lam, ph, lb in ((y_first_ref, mm_y0, ms_y0, lam_y0, ph_y0, lb_y0),
                                           (y_last_ref, mm_y1, ms_y1, lam_y1, ph_y1, lb_y1)):
            (w_real, w_imag), _ = first_w(lam[0, 0], lam[1, 0], lb[0], ph[0])
            planes = [m1[0, 0], m1[1, 0], m2[0, 0], m2[1, 0], w_real, w_imag]
            for c, value in enumerate(planes):
                out_ref[c] = value

    def body(r, carry):
        for out_ref, m1, m2, lam, ph, lb, at in ((z_first_ref, mm_z0, ms_z0, lam_z0, ph_z0, lb_z0, 0),
                                               (z_last_ref, mm_z1, ms_z1, lam_z1, ph_z1, lb_z1, 7)):
            (w_real, w_imag), _ = first_w(lam[0, r], lam[1, r], lb[r], ph[r])
            tiles = [m1[0, r], m1[1, r], m2[0, r], m2[1, r], w_real, w_imag]
            for c, value in enumerate(tiles):
                out_ref[c, r] = value[at:at + 1]
        return carry
    lax.fori_loop(0, rows, body, 0)


def edge_specs_of(ndim, length_y, length_z, length_x, rows):
    lead = (2,) if ndim == 4 else ()
    zero = (0,) * len(lead)
    tiles = length_z // 8
    return [
        pl.BlockSpec(lead + (1, length_z, length_x), lambda i: zero + (0, 0, 0)),
        pl.BlockSpec(lead + (1, length_z, length_x), lambda i: zero + (length_y - 1, 0, 0)),
        pl.BlockSpec(lead + (rows, 8, length_x), lambda i: zero + (i, 0, 0)),
        pl.BlockSpec(lead + (rows, 8, length_x), lambda i: zero + (i, tiles - 1, 0)),
    ]


def edge_outputs(comps, length_y, length_z, length_x, rows):
    plane = jax.ShapeDtypeStruct((comps, length_z, length_x), jnp.float32)
    row = jax.ShapeDtypeStruct((comps, length_y, 1, length_x), jnp.float32)
    plane_spec = pl.BlockSpec((comps, length_z, length_x), lambda i: (0, 0, 0))
    row_spec = pl.BlockSpec((comps, rows, 1, length_x), lambda i: (0, i, 0, 0))
    return [plane, plane, row, row], [plane_spec, plane_spec, row_spec, row_spec]


def first_kernel(*refs, rows):
    (mm_ref, mm_prev, mm_next, ms_ref, ms_prev, ms_next, w_ref, w_prev, w_next,
     factor_ref, y_low_ref, y_high_ref, z_low_ref, z_high_ref, pg_ref, w2_ref) = refs[:16]
    step = pl.program_id(0)
    last = pl.num_programs(0) - 1
    fields = ((mm_ref, mm_prev, mm_next), (ms_ref, ms_prev, ms_next), (w_ref, w_prev, w_next))

    def body(r):
        new = []
        for f, (cur, prev, nxt) in enumerate(fields):
            pair = []
            for comp in range(2):
                below, above = neighbour_planes(cur, prev, nxt, y_low_ref, y_high_ref, rows, 2 * f + comp, comp, r,
                                                step, last)
                pair.append(plane_update(cur[comp, r], below, above,
                                         z_low_ref[2 * f + comp, r], z_high_ref[2 * f + comp, r]))
            new.append(pair)
        (u1_real, u1_imag), (u2_real, u2_imag), (lam_real, lam_imag) = new
        w_real = w_ref[0, r]
        w_imag = w_ref[1, r]
        f_real = factor_ref[0, r]
        f_imag = factor_ref[1, r]
        w2_real = f_real * lam_real - f_imag * lam_imag
        w2_imag = f_real * lam_imag + f_imag * lam_real
        grad = w_real * u1_imag - w_imag * u1_real
        pg_ref[r] = grad + (w2_real * u2_imag - w2_imag * u2_real)
        w2_ref[0, r] = w2_real
        w2_ref[1, r] = w2_imag
        write_edges(step, last, rows, r, [w2_real, w2_imag], *refs[16:])

    for_rows(rows, body)


def second_kernel(w_ref, w_prev, w_next, y_low_ref, y_high_ref, z_low_ref, z_high_ref, out_ref, *, rows):
    step = pl.program_id(0)
    last = pl.num_programs(0) - 1

    def body(r):
        for comp in range(2):
            below, above = neighbour_planes(w_ref, w_prev, w_next, y_low_ref, y_high_ref, rows, comp, comp, r,
                                            step, last)
            out_ref[comp, r] = plane_update(w_ref[comp, r], below, above,
                                            z_low_ref[comp, r], z_high_ref[comp, r])

    for_rows(rows, body)


def block_rows(length_y):
    rows = 8
    while length_y % rows:
        rows //= 2
    return rows


def field_specs(shape, rows):
    comps, length_y, length_z, length_x = shape
    cur = pl.BlockSpec((comps, rows, length_z, length_x), lambda i: (0, i, 0, 0))
    prev = pl.BlockSpec((comps, 1, length_z, length_x),
                        lambda i: (0, jnp.maximum(i * rows - 1, 0), 0, 0))
    nxt = pl.BlockSpec((comps, 1, length_z, length_x),
                       lambda i: (0, jnp.minimum(i * rows + rows, length_y - 1), 0, 0))
    return [cur, prev, nxt]


def send_edges(y_first, y_last, z_first, z_last):
    results = []
    for axis, first, last in (("gy", y_first, y_last), ("gz", z_first, z_last)):
        count = lax.axis_size(axis)
        up = [(i, (i + 1) % count) for i in range(count)]
        down = [(j, i) for i, j in up]
        if count == 2:
            both = lax.ppermute(jnp.stack([last, first]), axis, up)
            results.extend([both[0], both[1]])
        else:
            results.extend([lax.ppermute(last, axis, up), lax.ppermute(first, axis, down)])
    return results


def backward_sections(mag_start, mag_middle, adjoint_end, phase, labels):
    _, length_y, length_z, length_x = mag_start.shape
    rows = block_rows(length_y)
    grid = (length_y // rows,)
    plane = jax.ShapeDtypeStruct((length_y, length_z, length_x), jnp.float32)
    pair = jax.ShapeDtypeStruct((2, length_y, length_z, length_x), jnp.float32)
    cur = pl.BlockSpec((2, rows, length_z, length_x), lambda i: (0, i, 0, 0))
    cur_plane = pl.BlockSpec((rows, length_z, length_x), lambda i: (i, 0, 0))
    whole = lambda shape: pl.BlockSpec(shape, lambda i: (0,) * len(shape))
    zspec = lambda comps: pl.BlockSpec((comps, rows, 1, length_x), lambda i: (0, i, 0, 0))
    edge_shapes, edge_specs = edge_outputs(2, length_y, length_z, length_x, rows)
    six_shapes, six_specs = edge_outputs(6, length_y, length_z, length_x, rows)
    inputs = (mag_middle, mag_start, adjoint_end, phase, labels)
    edges = pl.pallas_call(
        functools.partial(edges_kernel, rows=rows),
        grid=grid,
        in_specs=[s for a in inputs for s in edge_specs_of(a.ndim, length_y, length_z, length_x, rows)],
        out_specs=six_specs,
        out_shape=six_shapes,
    )(*[a for a in inputs for _ in range(4)])
    halos = send_edges(*edges)
    factor, w_first = pl.pallas_call(
        functools.partial(factor_kernel, rows=rows),
        grid=grid,
        in_specs=[cur, cur_plane, cur_plane],
        out_specs=[cur, cur],
        out_shape=[pair, pair],
    )(adjoint_end, phase, labels)
    phase_grad, w_second, *w2_edges = pl.pallas_call(
        functools.partial(first_kernel, rows=rows),
        grid=grid,
        in_specs=field_specs(mag_middle.shape, rows) + field_specs(mag_start.shape, rows)
        + field_specs(w_first.shape, rows)
        + [cur, whole((6, length_z, length_x)), whole((6, length_z, length_x)), zspec(6), zspec(6)],
        out_specs=[cur_plane, cur] + edge_specs,
        out_shape=[plane, pair] + edge_shapes,
    )(mag_middle, mag_middle, mag_middle, mag_start, mag_start, mag_start,
      w_first, w_first, w_first, factor, *halos)
    halos = send_edges(*w2_edges)
    return phase_grad, functools.partial(finish_lambda, w_second, rows, grid, cur, whole, zspec, length_z, length_x), halos


def finish_lambda(w_second, rows, grid, cur, whole, zspec, length_z, length_x, halos):
    pair = jax.ShapeDtypeStruct(w_second.shape, jnp.float32)
    lam = pl.pallas_call(
        functools.partial(second_kernel, rows=rows),
        grid=grid,
        in_specs=field_specs(w_second.shape, rows)
        + [whole((2, length_z, length_x)), whole((2, length_z, length_x)), zspec(2), zspec(2)],
        out_specs=cur,
        out_shape=pair,
    )(w_second, w_second, w_second, *halos)
    return lam


def dipole_adjoint(phase_grad, finish, halos):
    count_y = lax.axis_size("gy")
    count_z = lax.axis_size("gz")
    parts = count_y * count_z
    block_y, block_z, length_x = phase_grad.shape
    length_y = block_y * count_y
    length_z = block_z * count_z
    block_x = length_x // parts
    pieces = 2 if block_x % 2 == 0 else 1
    piece_x = block_x // pieces
    table_x = cas_table(length_x).reshape(parts, pieces, piece_x, length_x)
    table_y = cas_table(length_y)
    table_z = cas_table(length_z)
    scale = 1.0 / (float(length_y) * float(length_z) * float(length_x))
    freq_y = signed_freq(jnp.arange(length_y, dtype=jnp.int32), length_y)
    freq_z = signed_freq(jnp.arange(length_z, dtype=jnp.int32), length_z)
    index = lax.axis_index("gy") * count_z + lax.axis_index("gz")
    sent = []
    for p in range(pieces):
        spec = along("sxn,yzn->sxyz", table_x[:, p], phase_grad)
        if p == 0:
            halos, spec = lax.optimization_barrier((halos, spec))
        sent.append(lax.all_to_all(spec, ("gy", "gz"), 0, 0, tiled=True))
        if p == 0:
            lam = finish(halos)
    result = None
    for p in range(pieces):
        spec = sent[p].reshape(count_y, count_z, piece_x, block_y, block_z)
        spec = spec.transpose(2, 0, 3, 1, 4).reshape(piece_x, length_y, length_z)
        spec = along("kz,xyz->xyk", table_z, spec)
        spec = along("ky,xyz->xkz", table_y, spec)
        first_x = index * block_x + p * piece_x
        freq_x = signed_freq(first_x + jnp.arange(piece_x, dtype=jnp.int32), length_x)
        kernel = dipole_block(freq_y[None, :, None], freq_z[None, None, :], freq_x[:, None, None])
        spec = spec * kernel
        spec = along("ky,xyz->xkz", table_y, spec)
        spec = along("kz,xyz->xyk", table_z, spec)
        spec = spec.reshape(piece_x, count_y, block_y, count_z, block_z)
        spec = spec.transpose(1, 3, 0, 2, 4).reshape(parts, piece_x, block_y, block_z)
        spec = lax.all_to_all(spec, ("gy", "gz"), 0, 0, tiled=True)
        rows_in = spec.reshape(parts * piece_x, block_y * block_z)
        part = along("kn,km->mn", table_x[:, p].reshape(parts * piece_x, length_x), rows_in)
        part = part.reshape(block_y, block_z, length_x)
        result = part if result is None else result + part
    return result * scale, lam


def per_device(mag_start, mag_middle, adjoint_end, phase, labels):
    phase_grad, finish, halos = backward_sections(mag_start, mag_middle, adjoint_end, phase, labels)
    chi_grad, lam = dipole_adjoint(phase_grad, finish, halos)
    return (lam, chi_grad)


def solution(mesh):
    return jax.shard_map(
        per_device,
        mesh=mesh,
        in_specs=(
            P(None, "gy", "gz", None),
            P(None, "gy", "gz", None),
            P(None, "gy", "gz", None),
            P("gy", "gz", None),
            P("gy", "gz", None),
        ),
        out_specs=(P(None, "gy", "gz", None), P("gy", "gz", None)),
        check_vma=False,
    )
```

```python
import functools
import math

import jax
import numpy as np
import jax.numpy as jnp
from jax import lax
from jax.experimental import pallas as pl
from jax.experimental.pallas import tpu as pltpu
from jax.sharding import PartitionSpec as P


def signed_freq(index, length):
    return jnp.where(index < length // 2, index, index - length)


def dipole_block(freq_y, freq_z, freq_x):
    square_z = freq_z * freq_z
    total = freq_y * freq_y + square_z + freq_x * freq_x
    ratio = square_z.astype(jnp.float32) / jnp.maximum(total, 1).astype(jnp.float32)
    return jnp.where(total == 0, jnp.float32(0.0), jnp.float32(1.0 / 3.0) - ratio)


def cas_table(length):
    index = jnp.arange(length, dtype=jnp.int32)
    product = index[:, None] * index[None, :] % length
    angle = product.astype(jnp.float32) * (2.0 * math.pi / length)
    return jnp.cos(angle) + jnp.sin(angle)


def along(spec, table, values):
    return jnp.einsum(spec, table, values, precision=lax.Precision.HIGH)


def plane_update(centre, below, above, z_low, z_high):
    length_z, length_x = centre.shape
    up = pltpu.roll(centre, 1, 0)
    down = pltpu.roll(centre, length_z - 1, 0)
    if length_z > 8:
        row = lax.broadcasted_iota(jnp.int32, (8, length_x), 0)
        up = jnp.concatenate([jnp.where(row == 0, z_low, up[:8]), up[8:]], axis=0)
        down = jnp.concatenate([down[:length_z - 8], jnp.where(row == 7, z_high, down[length_z - 8:])], axis=0)
    else:
        row = lax.broadcasted_iota(jnp.int32, centre.shape, 0)
        up = jnp.where(row == 0, z_low, up)
        down = jnp.where(row == length_z - 1, z_high, down)
    total = below + above + up + down
    total = total + pltpu.roll(centre, 1, 1) + pltpu.roll(centre, length_x - 1, 1)
    return centre + 0.15 * (total - 6.0 * centre)


def neighbour_planes(cur_ref, prev_ref, next_ref, y_low_ref, y_high_ref, rows, field, comp, r, step, last):
    if isinstance(r, int) and r == 0:
        below = jnp.where(step == 0, y_low_ref[field], prev_ref[comp, 0])
    else:
        below = cur_ref[comp, r - 1]
    if isinstance(r, int) and r == rows - 1:
        above = jnp.where(step == last, y_high_ref[field], next_ref[comp, 0])
    else:
        above = cur_ref[comp, r + 1]
    return below, above


def write_edges(step, last, rows, r, values, y_first_ref, y_last_ref, z_first_ref, z_last_ref):
    for c, value in enumerate(values):
        z_first_ref[c, r] = value[0:1]
        z_last_ref[c, r] = value[value.shape[0] - 1:]
    if isinstance(r, int) and r == 0:
        @pl.when(step == 0)
        def _():
            for c, value in enumerate(values):
                y_first_ref[c] = value
    if isinstance(r, int) and r == rows - 1:
        @pl.when(step == last)
        def _():
            for c, value in enumerate(values):
                y_last_ref[c] = value


def for_rows(rows, body):
    body(0)
    if rows > 2:
        def loop_body(r, carry):
            body(r)
            return carry
        lax.fori_loop(1, rows - 1, loop_body, 0)
    if rows > 1:
        body(rows - 1)


def sin_cos(x):
    k = jnp.floor(x * (2.0 / math.pi) + 0.5)
    r = (x - k * 1.5707963705062866) - k * (-4.371139000186243e-08)
    r2 = r * r
    s = r + r * r2 * (-1.0 / 6.0 + r2 * (1.0 / 120.0 + r2 * (-1.0 / 5040.0 + r2 * (1.0 / 362880.0))))
    c = 1.0 + r2 * (-0.5 + r2 * (1.0 / 24.0 + r2 * (-1.0 / 720.0 + r2 * (1.0 / 40320.0
                                                                        + r2 * (-1.0 / 3628800.0)))))
    quadrant = k.astype(jnp.int32) & 3
    swap = (quadrant & 1) == 1
    sin_x = jnp.where(swap, c, s)
    cos_x = jnp.where(swap, s, c)
    sin_x = jnp.where(quadrant >= 2, -sin_x, sin_x)
    cos_x = jnp.where((quadrant == 1) | (quadrant == 2), -cos_x, cos_x)
    return sin_x, cos_x


def step_factor(labels, phase):
    decays = [float(np.exp(-np.float32(rate))) for rate in (0.02, 0.3, 0.6, 1.2)]
    decay = jnp.where(labels == 1, decays[1], decays[0])
    decay = jnp.where(labels == 2, decays[2], decay)
    decay = jnp.where(labels == 3, decays[3], decay).astype(jnp.float32)
    sin_p, cos_p = sin_cos(phase)
    return decay * cos_p, decay * sin_p


def first_w(lam_real, lam_imag, labels, phase):
    f_real, f_imag = step_factor(labels, phase)
    return (f_real * lam_real - f_imag * lam_imag, f_real * lam_imag + f_imag * lam_real), (f_real, f_imag)


def factor_kernel(lam_ref, phase_ref, labels_ref, factor_ref, w_ref, *, rows):
    def body(r, carry):
        (w_real, w_imag), (f_real, f_imag) = first_w(lam_ref[0, r], lam_ref[1, r], labels_ref[r], phase_ref[r])
        factor_ref[0, r] = f_real
        factor_ref[1, r] = f_imag
        w_ref[0, r] = w_real
        w_ref[1, r] = w_imag
        return carry
    lax.fori_loop(0, rows, body, 0)


def edges_kernel(*refs, rows):
    (mm_y0, mm_y1, mm_z0, mm_z1, ms_y0, ms_y1, ms_z0, ms_z1, lam_y0, lam_y1, lam_z0, lam_z1,
     ph_y0, ph_y1, ph_z0, ph_z1, lb_y0, lb_y1, lb_z0, lb_z1,
     y_first_ref, y_last_ref, z_first_ref, z_last_ref) = refs

    @pl.when(pl.program_id(0) == 0)
    def _():
        for out_ref, m1, m2, lam, ph, lb in ((y_first_ref, mm_y0, ms_y0, lam_y0, ph_y0, lb_y0),
                                           (y_last_ref, mm_y1, ms_y1, lam_y1, ph_y1, lb_y1)):
            (w_real, w_imag), _ = first_w(lam[0, 0], lam[1, 0], lb[0], ph[0])
            planes = [m1[0, 0], m1[1, 0], m2[0, 0], m2[1, 0], w_real, w_imag]
            for c, value in enumerate(planes):
                out_ref[c] = value

    def body(r, carry):
        for out_ref, m1, m2, lam, ph, lb, at in ((z_first_ref, mm_z0, ms_z0, lam_z0, ph_z0, lb_z0, 0),
                                               (z_last_ref, mm_z1, ms_z1, lam_z1, ph_z1, lb_z1, 7)):
            (w_real, w_imag), _ = first_w(lam[0, r], lam[1, r], lb[r], ph[r])
            tiles = [m1[0, r], m1[1, r], m2[0, r], m2[1, r], w_real, w_imag]
            for c, value in enumerate(tiles):
                out_ref[c, r] = value[at:at + 1]
        return carry
    lax.fori_loop(0, rows, body, 0)


def edge_specs_of(ndim, length_y, length_z, length_x, rows):
    lead = (2,) if ndim == 4 else ()
    zero = (0,) * len(lead)
    tiles = length_z // 8
    return [
        pl.BlockSpec(lead + (1, length_z, length_x), lambda i: zero + (0, 0, 0)),
        pl.BlockSpec(lead + (1, length_z, length_x), lambda i: zero + (length_y - 1, 0, 0)),
        pl.BlockSpec(lead + (rows, 8, length_x), lambda i: zero + (i, 0, 0)),
        pl.BlockSpec(lead + (rows, 8, length_x), lambda i: zero + (i, tiles - 1, 0)),
    ]


def edge_outputs(comps, length_y, length_z, length_x, rows):
    plane = jax.ShapeDtypeStruct((comps, length_z, length_x), jnp.float32)
    row = jax.ShapeDtypeStruct((comps, length_y, 1, length_x), jnp.float32)
    plane_spec = pl.BlockSpec((comps, length_z, length_x), lambda i: (0, 0, 0))
    row_spec = pl.BlockSpec((comps, rows, 1, length_x), lambda i: (0, i, 0, 0))
    return [plane, plane, row, row], [plane_spec, plane_spec, row_spec, row_spec]


def first_kernel(*refs, rows):
    (mm_ref, mm_prev, mm_next, ms_ref, ms_prev, ms_next, w_ref, w_prev, w_next,
     factor_ref, y_low_ref, y_high_ref, z_low_ref, z_high_ref, pg_ref, w2_ref) = refs[:16]
    step = pl.program_id(0)
    last = pl.num_programs(0) - 1
    fields = ((mm_ref, mm_prev, mm_next), (ms_ref, ms_prev, ms_next), (w_ref, w_prev, w_next))

    def body(r):
        new = []
        for f, (cur, prev, nxt) in enumerate(fields):
            pair = []
            for comp in range(2):
                below, above = neighbour_planes(cur, prev, nxt, y_low_ref, y_high_ref, rows, 2 * f + comp, comp, r,
                                                step, last)
                pair.append(plane_update(cur[comp, r], below, above,
                                         z_low_ref[2 * f + comp, r], z_high_ref[2 * f + comp, r]))
            new.append(pair)
        (u1_real, u1_imag), (u2_real, u2_imag), (lam_real, lam_imag) = new
        w_real = w_ref[0, r]
        w_imag = w_ref[1, r]
        f_real = factor_ref[0, r]
        f_imag = factor_ref[1, r]
        w2_real = f_real * lam_real - f_imag * lam_imag
        w2_imag = f_real * lam_imag + f_imag * lam_real
        grad = w_real * u1_imag - w_imag * u1_real
        pg_ref[r] = grad + (w2_real * u2_imag - w2_imag * u2_real)
        w2_ref[0, r] = w2_real
        w2_ref[1, r] = w2_imag
        write_edges(step, last, rows, r, [w2_real, w2_imag], *refs[16:])

    for_rows(rows, body)


def second_kernel(w_ref, w_prev, w_next, y_low_ref, y_high_ref, z_low_ref, z_high_ref, out_ref, *, rows):
    step = pl.program_id(0)
    last = pl.num_programs(0) - 1

    def body(r):
        for comp in range(2):
            below, above = neighbour_planes(w_ref, w_prev, w_next, y_low_ref, y_high_ref, rows, comp, comp, r,
                                            step, last)
            out_ref[comp, r] = plane_update(w_ref[comp, r], below, above,
                                            z_low_ref[comp, r], z_high_ref[comp, r])

    for_rows(rows, body)


def block_rows(length_y):
    rows = 8
    while length_y % rows:
        rows //= 2
    return rows


def field_specs(shape, rows):
    comps, length_y, length_z, length_x = shape
    cur = pl.BlockSpec((comps, rows, length_z, length_x), lambda i: (0, i, 0, 0))
    prev = pl.BlockSpec((comps, 1, length_z, length_x),
                        lambda i: (0, jnp.maximum(i * rows - 1, 0), 0, 0))
    nxt = pl.BlockSpec((comps, 1, length_z, length_x),
                       lambda i: (0, jnp.minimum(i * rows + rows, length_y - 1), 0, 0))
    return [cur, prev, nxt]


def send_edges(y_first, y_last, z_first, z_last):
    results = []
    for axis, first, last in (("gy", y_first, y_last), ("gz", z_first, z_last)):
        count = lax.axis_size(axis)
        up = [(i, (i + 1) % count) for i in range(count)]
        down = [(j, i) for i, j in up]
        if count == 2:
            both = lax.ppermute(jnp.stack([last, first]), axis, up)
            results.extend([both[0], both[1]])
        else:
            results.extend([lax.ppermute(last, axis, up), lax.ppermute(first, axis, down)])
    return results


def backward_sections(mag_start, mag_middle, adjoint_end, phase, labels):
    _, length_y, length_z, length_x = mag_start.shape
    rows = block_rows(length_y)
    grid = (length_y // rows,)
    plane = jax.ShapeDtypeStruct((length_y, length_z, length_x), jnp.float32)
    pair = jax.ShapeDtypeStruct((2, length_y, length_z, length_x), jnp.float32)
    cur = pl.BlockSpec((2, rows, length_z, length_x), lambda i: (0, i, 0, 0))
    cur_plane = pl.BlockSpec((rows, length_z, length_x), lambda i: (i, 0, 0))
    whole = lambda shape: pl.BlockSpec(shape, lambda i: (0,) * len(shape))
    zspec = lambda comps: pl.BlockSpec((comps, rows, 1, length_x), lambda i: (0, i, 0, 0))
    edge_shapes, edge_specs = edge_outputs(2, length_y, length_z, length_x, rows)
    six_shapes, six_specs = edge_outputs(6, length_y, length_z, length_x, rows)
    inputs = (mag_middle, mag_start, adjoint_end, phase, labels)
    edges = pl.pallas_call(
        functools.partial(edges_kernel, rows=rows),
        grid=grid,
        in_specs=[s for a in inputs for s in edge_specs_of(a.ndim, length_y, length_z, length_x, rows)],
        out_specs=six_specs,
        out_shape=six_shapes,
    )(*[a for a in inputs for _ in range(4)])
    halos = send_edges(*edges)
    factor, w_first = pl.pallas_call(
        functools.partial(factor_kernel, rows=rows),
        grid=grid,
        in_specs=[cur, cur_plane, cur_plane],
        out_specs=[cur, cur],
        out_shape=[pair, pair],
    )(adjoint_end, phase, labels)
    phase_grad, w_second, *w2_edges = pl.pallas_call(
        functools.partial(first_kernel, rows=rows),
        grid=grid,
        in_specs=field_specs(mag_middle.shape, rows) + field_specs(mag_start.shape, rows)
        + field_specs(w_first.shape, rows)
        + [cur, whole((6, length_z, length_x)), whole((6, length_z, length_x)), zspec(6), zspec(6)],
        out_specs=[cur_plane, cur] + edge_specs,
        out_shape=[plane, pair] + edge_shapes,
    )(mag_middle, mag_middle, mag_middle, mag_start, mag_start, mag_start,
      w_first, w_first, w_first, factor, *halos)
    halos = send_edges(*w2_edges)
    return phase_grad, functools.partial(finish_lambda, w_second, rows, grid, cur, whole, zspec, length_z, length_x), halos


def finish_lambda(w_second, rows, grid, cur, whole, zspec, length_z, length_x, halos):
    pair = jax.ShapeDtypeStruct(w_second.shape, jnp.float32)
    lam = pl.pallas_call(
        functools.partial(second_kernel, rows=rows),
        grid=grid,
        in_specs=field_specs(w_second.shape, rows)
        + [whole((2, length_z, length_x)), whole((2, length_z, length_x)), zspec(2), zspec(2)],
        out_specs=cur,
        out_shape=pair,
    )(w_second, w_second, w_second, *halos)
    return lam


def dipole_adjoint(phase_grad, finish, halos):
    count_y = lax.axis_size("gy")
    count_z = lax.axis_size("gz")
    parts = count_y * count_z
    block_y, block_z, length_x = phase_grad.shape
    length_y = block_y * count_y
    length_z = block_z * count_z
    block_x = length_x // parts
    pieces = 2 if block_x % 2 == 0 else 1
    piece_x = block_x // pieces
    table_x = cas_table(length_x).reshape(parts, pieces, piece_x, length_x)
    table_y = cas_table(length_y)
    table_z = cas_table(length_z)
    scale = 1.0 / (float(length_y) * float(length_z) * float(length_x))
    freq_y = signed_freq(jnp.arange(length_y, dtype=jnp.int32), length_y)
    freq_z = signed_freq(jnp.arange(length_z, dtype=jnp.int32), length_z)
    index = lax.axis_index("gy") * count_z + lax.axis_index("gz")
    sent = []
    for p in range(pieces):
        spec = along("sxn,yzn->sxyz", table_x[:, p], phase_grad)
        if p == 0:
            halos, spec = lax.optimization_barrier((halos, spec))
        sent.append(lax.all_to_all(spec, ("gy", "gz"), 0, 0, tiled=True))
        if p == 0:
            lam = finish(halos)
    result = None
    for p in range(pieces):
        spec = sent[p].reshape(count_y, count_z, piece_x, block_y, block_z)
        spec = spec.transpose(2, 0, 3, 1, 4).reshape(piece_x, length_y, length_z)
        spec = along("kz,xyz->xyk", table_z, spec)
        spec = along("ky,xyz->xkz", table_y, spec)
        first_x = index * block_x + p * piece_x
        freq_x = signed_freq(first_x + jnp.arange(piece_x, dtype=jnp.int32), length_x)
        kernel = dipole_block(freq_y[None, :, None], freq_z[None, None, :], freq_x[:, None, None])
        spec = spec * kernel
        spec = along("ky,xyz->xkz", table_y, spec)
        spec = along("kz,xyz->xyk", table_z, spec)
        spec = spec.reshape(piece_x, count_y, block_y, count_z, block_z)
        spec = spec.transpose(1, 3, 0, 2, 4).reshape(parts, piece_x, block_y, block_z)
        spec = lax.all_to_all(spec, ("gy", "gz"), 0, 0, tiled=True)
        rows_in = spec.reshape(parts * piece_x, block_y * block_z)
        part = along("kn,km->mn", (table_x[:, p] * scale).reshape(parts * piece_x, length_x), rows_in)
        part = part.reshape(block_y, block_z, length_x)
        result = part if result is None else result + part
    return result, lam


def per_device(mag_start, mag_middle, adjoint_end, phase, labels):
    phase_grad, finish, halos = backward_sections(mag_start, mag_middle, adjoint_end, phase, labels)
    chi_grad, lam = dipole_adjoint(phase_grad, finish, halos)
    return (lam, chi_grad)


def solution(mesh):
    return jax.shard_map(
        per_device,
        mesh=mesh,
        in_specs=(
            P(None, "gy", "gz", None),
            P(None, "gy", "gz", None),
            P(None, "gy", "gz", None),
            P("gy", "gz", None),
            P("gy", "gz", None),
        ),
        out_specs=(P(None, "gy", "gz", None), P("gy", "gz", None)),
        check_vma=False,
    )
```

```python
import functools
import math

import jax
import numpy as np
import jax.numpy as jnp
from jax import lax
from jax.experimental import pallas as pl
from jax.experimental.pallas import tpu as pltpu
from jax.sharding import PartitionSpec as P


def signed_freq(index, length):
    return jnp.where(index < length // 2, index, index - length)


def dipole_block(freq_y, freq_z, freq_x):
    square_z = freq_z * freq_z
    total = freq_y * freq_y + square_z + freq_x * freq_x
    ratio = square_z.astype(jnp.float32) / jnp.maximum(total, 1).astype(jnp.float32)
    return jnp.where(total == 0, jnp.float32(0.0), jnp.float32(1.0 / 3.0) - ratio)


def cas_table(length):
    index = jnp.arange(length, dtype=jnp.int32)
    product = index[:, None] * index[None, :] % length
    angle = product.astype(jnp.float32) * (2.0 * math.pi / length)
    return jnp.cos(angle) + jnp.sin(angle)


def along(spec, table, values):
    return jnp.einsum(spec, table, values, precision=lax.Precision.HIGH)


def plane_update(centre, below, above, z_low, z_high):
    length_z, length_x = centre.shape
    up = pltpu.roll(centre, 1, 0)
    down = pltpu.roll(centre, length_z - 1, 0)
    if length_z > 8:
        row = lax.broadcasted_iota(jnp.int32, (8, length_x), 0)
        up = jnp.concatenate([jnp.where(row == 0, z_low, up[:8]), up[8:]], axis=0)
        down = jnp.concatenate([down[:length_z - 8], jnp.where(row == 7, z_high, down[length_z - 8:])], axis=0)
    else:
        row = lax.broadcasted_iota(jnp.int32, centre.shape, 0)
        up = jnp.where(row == 0, z_low, up)
        down = jnp.where(row == length_z - 1, z_high, down)
    total = below + above + up + down
    total = total + pltpu.roll(centre, 1, 1) + pltpu.roll(centre, length_x - 1, 1)
    return centre + 0.15 * (total - 6.0 * centre)


def neighbour_planes(cur_ref, prev_ref, next_ref, y_low_ref, y_high_ref, rows, field, comp, r, step, last):
    if isinstance(r, int) and r == 0:
        below = jnp.where(step == 0, y_low_ref[field], prev_ref[comp, 0])
    else:
        below = cur_ref[comp, r - 1]
    if isinstance(r, int) and r == rows - 1:
        above = jnp.where(step == last, y_high_ref[field], next_ref[comp, 0])
    else:
        above = cur_ref[comp, r + 1]
    return below, above


def write_edges(step, last, rows, r, values, y_first_ref, y_last_ref, z_first_ref, z_last_ref):
    for c, value in enumerate(values):
        z_first_ref[c, r] = value[0:1]
        z_last_ref[c, r] = value[value.shape[0] - 1:]
    if isinstance(r, int) and r == 0:
        @pl.when(step == 0)
        def _():
            for c, value in enumerate(values):
                y_first_ref[c] = value
    if isinstance(r, int) and r == rows - 1:
        @pl.when(step == last)
        def _():
            for c, value in enumerate(values):
                y_last_ref[c] = value


def for_rows(rows, body):
    body(0)
    if rows > 2:
        def loop_body(r, carry):
            body(r)
            return carry
        lax.fori_loop(1, rows - 1, loop_body, 0)
    if rows > 1:
        body(rows - 1)


def sin_cos(x):
    k = jnp.floor(x * (2.0 / math.pi) + 0.5)
    r = (x - k * 1.5707963705062866) - k * (-4.371139000186243e-08)
    r2 = r * r
    s = r + r * r2 * (-1.0 / 6.0 + r2 * (1.0 / 120.0 + r2 * (-1.0 / 5040.0 + r2 * (1.0 / 362880.0))))
    c = 1.0 + r2 * (-0.5 + r2 * (1.0 / 24.0 + r2 * (-1.0 / 720.0 + r2 * (1.0 / 40320.0
                                                                        + r2 * (-1.0 / 3628800.0)))))
    quadrant = k.astype(jnp.int32) & 3
    swap = (quadrant & 1) == 1
    sin_x = jnp.where(swap, c, s)
    cos_x = jnp.where(swap, s, c)
    sin_x = jnp.where(quadrant >= 2, -sin_x, sin_x)
    cos_x = jnp.where((quadrant == 1) | (quadrant == 2), -cos_x, cos_x)
    return sin_x, cos_x


def step_factor(labels, phase):
    decays = [float(np.exp(-np.float32(rate))) for rate in (0.02, 0.3, 0.6, 1.2)]
    decay = jnp.where(labels == 1, decays[1], decays[0])
    decay = jnp.where(labels == 2, decays[2], decay)
    decay = jnp.where(labels == 3, decays[3], decay).astype(jnp.float32)
    sin_p, cos_p = sin_cos(phase)
    return decay * cos_p, decay * sin_p


def first_w(lam_real, lam_imag, labels, phase):
    f_real, f_imag = step_factor(labels, phase)
    return (f_real * lam_real - f_imag * lam_imag, f_real * lam_imag + f_imag * lam_real), (f_real, f_imag)


def factor_kernel(lam_ref, phase_ref, labels_ref, factor_ref, w_ref, *, rows):
    def body(r, carry):
        (w_real, w_imag), (f_real, f_imag) = first_w(lam_ref[0, r], lam_ref[1, r], labels_ref[r], phase_ref[r])
        factor_ref[0, r] = f_real
        factor_ref[1, r] = f_imag
        w_ref[0, r] = w_real
        w_ref[1, r] = w_imag
        return carry
    lax.fori_loop(0, rows, body, 0)


def edges_kernel(*refs, rows):
    (mm_y0, mm_y1, mm_z0, mm_z1, ms_y0, ms_y1, ms_z0, ms_z1, lam_y0, lam_y1, lam_z0, lam_z1,
     ph_y0, ph_y1, ph_z0, ph_z1, lb_y0, lb_y1, lb_z0, lb_z1,
     y_first_ref, y_last_ref, z_first_ref, z_last_ref) = refs

    @pl.when(pl.program_id(0) == 0)
    def _():
        for out_ref, m1, m2, lam, ph, lb in ((y_first_ref, mm_y0, ms_y0, lam_y0, ph_y0, lb_y0),
                                           (y_last_ref, mm_y1, ms_y1, lam_y1, ph_y1, lb_y1)):
            (w_real, w_imag), _ = first_w(lam[0, 0], lam[1, 0], lb[0], ph[0])
            planes = [m1[0, 0], m1[1, 0], m2[0, 0], m2[1, 0], w_real, w_imag]
            for c, value in enumerate(planes):
                out_ref[c] = value

    def body(r, carry):
        for out_ref, m1, m2, lam, ph, lb, at in ((z_first_ref, mm_z0, ms_z0, lam_z0, ph_z0, lb_z0, 0),
                                               (z_last_ref, mm_z1, ms_z1, lam_z1, ph_z1, lb_z1, 7)):
            (w_real, w_imag), _ = first_w(lam[0, r], lam[1, r], lb[r], ph[r])
            tiles = [m1[0, r], m1[1, r], m2[0, r], m2[1, r], w_real, w_imag]
            for c, value in enumerate(tiles):
                out_ref[c, r] = value[at:at + 1]
        return carry
    lax.fori_loop(0, rows, body, 0)


def edge_specs_of(ndim, length_y, length_z, length_x, rows):
    lead = (2,) if ndim == 4 else ()
    zero = (0,) * len(lead)
    tiles = length_z // 8
    return [
        pl.BlockSpec(lead + (1, length_z, length_x), lambda i: zero + (0, 0, 0)),
        pl.BlockSpec(lead + (1, length_z, length_x), lambda i: zero + (length_y - 1, 0, 0)),
        pl.BlockSpec(lead + (rows, 8, length_x), lambda i: zero + (i, 0, 0)),
        pl.BlockSpec(lead + (rows, 8, length_x), lambda i: zero + (i, tiles - 1, 0)),
    ]


def edge_outputs(comps, length_y, length_z, length_x, rows):
    plane = jax.ShapeDtypeStruct((comps, length_z, length_x), jnp.float32)
    row = jax.ShapeDtypeStruct((comps, length_y, 1, length_x), jnp.float32)
    plane_spec = pl.BlockSpec((comps, length_z, length_x), lambda i: (0, 0, 0))
    row_spec = pl.BlockSpec((comps, rows, 1, length_x), lambda i: (0, i, 0, 0))
    return [plane, plane, row, row], [plane_spec, plane_spec, row_spec, row_spec]


def first_kernel(*refs, rows):
    (mm_ref, mm_prev, mm_next, ms_ref, ms_prev, ms_next, w_ref, w_prev, w_next,
     factor_ref, y_low_ref, y_high_ref, z_low_ref, z_high_ref, pg_ref, w2_ref) = refs[:16]
    step = pl.program_id(0)
    last = pl.num_programs(0) - 1
    fields = ((mm_ref, mm_prev, mm_next), (ms_ref, ms_prev, ms_next), (w_ref, w_prev, w_next))

    def body(r):
        new = []
        for f, (cur, prev, nxt) in enumerate(fields):
            pair = []
            for comp in range(2):
                below, above = neighbour_planes(cur, prev, nxt, y_low_ref, y_high_ref, rows, 2 * f + comp, comp, r,
                                                step, last)
                pair.append(plane_update(cur[comp, r], below, above,
                                         z_low_ref[2 * f + comp, r], z_high_ref[2 * f + comp, r]))
            new.append(pair)
        (u1_real, u1_imag), (u2_real, u2_imag), (lam_real, lam_imag) = new
        w_real = w_ref[0, r]
        w_imag = w_ref[1, r]
        f_real = factor_ref[0, r]
        f_imag = factor_ref[1, r]
        w2_real = f_real * lam_real - f_imag * lam_imag
        w2_imag = f_real * lam_imag + f_imag * lam_real
        grad = w_real * u1_imag - w_imag * u1_real
        pg_ref[r] = grad + (w2_real * u2_imag - w2_imag * u2_real)
        w2_ref[0, r] = w2_real
        w2_ref[1, r] = w2_imag
        write_edges(step, last, rows, r, [w2_real, w2_imag], *refs[16:])

    for_rows(rows, body)


def second_kernel(w_ref, w_prev, w_next, y_low_ref, y_high_ref, z_low_ref, z_high_ref, out_ref, *, rows):
    step = pl.program_id(0)
    last = pl.num_programs(0) - 1

    def body(r):
        for comp in range(2):
            below, above = neighbour_planes(w_ref, w_prev, w_next, y_low_ref, y_high_ref, rows, comp, comp, r,
                                            step, last)
            out_ref[comp, r] = plane_update(w_ref[comp, r], below, above,
                                            z_low_ref[comp, r], z_high_ref[comp, r])

    for_rows(rows, body)


def block_rows(length_y):
    rows = 8
    while length_y % rows:
        rows //= 2
    return rows


def field_specs(shape, rows):
    comps, length_y, length_z, length_x = shape
    cur = pl.BlockSpec((comps, rows, length_z, length_x), lambda i: (0, i, 0, 0))
    prev = pl.BlockSpec((comps, 1, length_z, length_x),
                        lambda i: (0, jnp.maximum(i * rows - 1, 0), 0, 0))
    nxt = pl.BlockSpec((comps, 1, length_z, length_x),
                       lambda i: (0, jnp.minimum(i * rows + rows, length_y - 1), 0, 0))
    return [cur, prev, nxt]


def send_edges(y_first, y_last, z_first, z_last):
    results = []
    for axis, first, last in (("gy", y_first, y_last), ("gz", z_first, z_last)):
        count = lax.axis_size(axis)
        up = [(i, (i + 1) % count) for i in range(count)]
        down = [(j, i) for i, j in up]
        if count == 2:
            both = lax.ppermute(jnp.stack([last, first]), axis, up)
            results.extend([both[0], both[1]])
        else:
            results.extend([lax.ppermute(last, axis, up), lax.ppermute(first, axis, down)])
    return results


def backward_sections(mag_start, mag_middle, adjoint_end, phase, labels):
    _, length_y, length_z, length_x = mag_start.shape
    rows = block_rows(length_y)
    grid = (length_y // rows,)
    plane = jax.ShapeDtypeStruct((length_y, length_z, length_x), jnp.float32)
    pair = jax.ShapeDtypeStruct((2, length_y, length_z, length_x), jnp.float32)
    cur = pl.BlockSpec((2, rows, length_z, length_x), lambda i: (0, i, 0, 0))
    cur_plane = pl.BlockSpec((rows, length_z, length_x), lambda i: (i, 0, 0))
    whole = lambda shape: pl.BlockSpec(shape, lambda i: (0,) * len(shape))
    zspec = lambda comps: pl.BlockSpec((comps, rows, 1, length_x), lambda i: (0, i, 0, 0))
    edge_shapes, edge_specs = edge_outputs(2, length_y, length_z, length_x, rows)
    six_shapes, six_specs = edge_outputs(6, length_y, length_z, length_x, rows)
    inputs = (mag_middle, mag_start, adjoint_end, phase, labels)
    edges = pl.pallas_call(
        functools.partial(edges_kernel, rows=rows),
        grid=grid,
        in_specs=[s for a in inputs for s in edge_specs_of(a.ndim, length_y, length_z, length_x, rows)],
        out_specs=six_specs,
        out_shape=six_shapes,
    )(*[a for a in inputs for _ in range(4)])
    halos = send_edges(*edges)
    factor, w_first = pl.pallas_call(
        functools.partial(factor_kernel, rows=rows),
        grid=grid,
        in_specs=[cur, cur_plane, cur_plane],
        out_specs=[cur, cur],
        out_shape=[pair, pair],
    )(adjoint_end, phase, labels)
    phase_grad, w_second, *w2_edges = pl.pallas_call(
        functools.partial(first_kernel, rows=rows),
        grid=grid,
        in_specs=field_specs(mag_middle.shape, rows) + field_specs(mag_start.shape, rows)
        + field_specs(w_first.shape, rows)
        + [cur, whole((6, length_z, length_x)), whole((6, length_z, length_x)), zspec(6), zspec(6)],
        out_specs=[cur_plane, cur] + edge_specs,
        out_shape=[plane, pair] + edge_shapes,
    )(mag_middle, mag_middle, mag_middle, mag_start, mag_start, mag_start,
      w_first, w_first, w_first, factor, *halos)
    halos = send_edges(*w2_edges)
    return phase_grad, functools.partial(finish_lambda, w_second, rows, grid, cur, whole, zspec, length_z, length_x), halos


def finish_lambda(w_second, rows, grid, cur, whole, zspec, length_z, length_x, halos):
    pair = jax.ShapeDtypeStruct(w_second.shape, jnp.float32)
    lam = pl.pallas_call(
        functools.partial(second_kernel, rows=rows),
        grid=grid,
        in_specs=field_specs(w_second.shape, rows)
        + [whole((2, length_z, length_x)), whole((2, length_z, length_x)), zspec(2), zspec(2)],
        out_specs=cur,
        out_shape=pair,
    )(w_second, w_second, w_second, *halos)
    return lam


def dipole_adjoint(phase_grad, finish, halos):
    count_y = lax.axis_size("gy")
    count_z = lax.axis_size("gz")
    parts = count_y * count_z
    block_y, block_z, length_x = phase_grad.shape
    length_y = block_y * count_y
    length_z = block_z * count_z
    block_x = length_x // parts
    pieces = 2 if block_x % 2 == 0 else 1
    piece_x = block_x // pieces
    table_x = cas_table(length_x).reshape(parts, pieces, piece_x, length_x)
    table_y = cas_table(length_y)
    table_z = cas_table(length_z)
    scale = 1.0 / (float(length_y) * float(length_z) * float(length_x))
    freq_y = signed_freq(jnp.arange(length_y, dtype=jnp.int32), length_y)
    freq_z = signed_freq(jnp.arange(length_z, dtype=jnp.int32), length_z)
    index = lax.axis_index("gy") * count_z + lax.axis_index("gz")
    sent = []
    for p in range(pieces):
        flat = along("kn,mn->km", table_x[:, p].reshape(parts * piece_x, length_x),
                     phase_grad.reshape(block_y * block_z, length_x))
        if p == 0:
            halos, flat = lax.optimization_barrier((halos, flat))
        spec = lax.all_to_all(flat, ("gy", "gz"), 0, 0, tiled=True)
        sent.append(spec.reshape(parts, piece_x, block_y, block_z))
        if p == 0:
            lam = finish(halos)
    result = None
    for p in range(pieces):
        spec = sent[p].reshape(count_y, count_z, piece_x, block_y, block_z)
        spec = spec.transpose(2, 0, 3, 1, 4).reshape(piece_x, length_y, length_z)
        spec = along("kz,xyz->xyk", table_z, spec)
        spec = along("ky,xyz->xkz", table_y, spec)
        first_x = index * block_x + p * piece_x
        freq_x = signed_freq(first_x + jnp.arange(piece_x, dtype=jnp.int32), length_x)
        kernel = dipole_block(freq_y[None, :, None], freq_z[None, None, :], freq_x[:, None, None])
        spec = spec * kernel
        spec = along("ky,xyz->xkz", table_y, spec)
        spec = along("kz,xyz->xyk", table_z, spec)
        spec = spec.reshape(piece_x, count_y, block_y, count_z, block_z)
        spec = spec.transpose(1, 3, 0, 2, 4).reshape(parts, piece_x, block_y, block_z)
        spec = lax.all_to_all(spec, ("gy", "gz"), 0, 0, tiled=True)
        rows_in = spec.reshape(parts * piece_x, block_y * block_z)
        part = along("kn,km->mn", table_x[:, p].reshape(parts * piece_x, length_x), rows_in)
        part = part.reshape(block_y, block_z, length_x)
        result = part if result is None else result + part
    return result * scale, lam


def per_device(mag_start, mag_middle, adjoint_end, phase, labels):
    phase_grad, finish, halos = backward_sections(mag_start, mag_middle, adjoint_end, phase, labels)
    chi_grad, lam = dipole_adjoint(phase_grad, finish, halos)
    return (lam, chi_grad)


def solution(mesh):
    return jax.shard_map(
        per_device,
        mesh=mesh,
        in_specs=(
            P(None, "gy", "gz", None),
            P(None, "gy", "gz", None),
            P(None, "gy", "gz", None),
            P("gy", "gz", None),
            P("gy", "gz", None),
        ),
        out_specs=(P(None, "gy", "gz", None), P("gy", "gz", None)),
        check_vma=False,
    )
```
